128 devices in a mesh: req: 4 (over z), ep: 32 (over x, y, core).
Axes of the slice: x: 4, y: 4, z: 4, core: 2. Of those that a mesh axis runs over, the one named last changes fastest.
Arguments:
- queries: bfloat16 [4096, 16, 192], P('ep'), may hold values from -260 to 260
- draft_latent: bfloat16 [4096, 576], P('ep'), may hold values from -5 to 5
- hidden_in: bfloat16 [4096, 2048], P('ep', 'req'), may hold values from -36 to 36
- cache_pool: bfloat16 [2048, 128, 576], P(('req', 'ep')), may hold values from -5 to 5
- page_table: int32 [64, 32], P('ep'), may hold values from 0 to 15, as said below
- cache_len: int32 [64], P('ep'), may hold values from 1 to 3584
- parents: int32 [64, 64], P('ep'), may hold values from -1 to 62, as said below
- accept_leaf: int32 [64], P('ep'), may hold values from 0 to 63
- absorb_key: bfloat16 [16, 128, 512], replicated, may hold values from -0.5 to 0.5
- absorb_value: bfloat16 [16, 512, 128], replicated, may hold values from -0.25 to 0.25
- out_proj: bfloat16 [2048, 2048], P(None, 'req'), may hold values from -0.125 to 0.125
- norm_gain: float32 [2048], replicated, may hold values from 0.1 to 1.9
- router: bfloat16 [2048, 64], replicated, may hold values from -0.125 to 0.125
- expert_ids: int32 [4096, 6], P('ep'), may hold values from 0 to 63, all different within a row; in each aligned block of 128 rows (0 to 127, 128 to 255, ...) at most 24 rows name the same one
- expert_gate_up: bfloat16 [64, 2, 2048, 1408], P('ep', None, None, 'req'), may hold values from -0.125 to 0.125
- expert_down: bfloat16 [64, 1408, 2048], P('ep', 'req'), may hold values from -0.15625 to 0.15625
- shared_gate_up: bfloat16 [2, 2048, 1408], P(None, None, 'req'), may hold values from -0.125 to 0.125
- shared_down: bfloat16 [1408, 2048], P('req'), may hold values from -0.15625 to 0.15625
Outputs:
- layer_out: bfloat16 [4096, 2048], P('ep', 'req')
- new_pages: bfloat16 [64, 4, 128, 576], P('ep', 'req')
The draws below stay inside these ranges and needn't reach their ends.
Inputs may be any that keep to these rules, and one draw needn't show every extreme that they name: `page_table`: for the 2 requests of one ep index, the pages j with one value of j mod 4 name distinct slots. parents[r, i] < i, and it is -1 exactly at i = 0. `expert_ids`: in each aligned block of 128 rows no expert is named by more than 24 rows.
All inputs are finite; a program needn't handle non-finite values.
Results may differ from the reference program's by a relative error of at most 0.011.
Values may be sent and summed in bfloat16 or wider, within the bound.
No kernel may reach another device: no remote copies, remote signals or barrier semaphores. Data moves between devices by JAX's collectives and lax.ppermute only.
A program may use at most 128 MiB of HBM per device.

```python
import math
import jax
import jax.numpy as jnp
import numpy as np
from jax import lax

D = 2048
H = 16
QK_NOPE = 128
ROPE = 64
V_HEAD = 128
LAT = 512
FF = 1408
TOPK = 6
SFF = 1408
PAGE = 128
DRAFT = 64
REQ_DEV = 2
MAX_LEN = 4096
KV = 576
EXPERTS = 64
TOK_EP = 128
REQUESTS = 64
TOKENS = 4096
MAXP = 32
POOL_DEV = 16
POOL = 2048
LMAX = 3584
CAP = 24
N_REQ = 4
N_EP = 32


def draw_queries(key, part):
    first = jax.random.fold_in(jax.random.fold_in(key, 1), 0)
    return jnp.clip(jax.random.normal(first, (TOKENS, H, QK_NOPE + ROPE), jnp.float32), -6.0, 6.0).astype(jnp.bfloat16)


def draw_cache_pool(key, part):
    first = jax.random.fold_in(jax.random.fold_in(key, 2), 0)
    return jnp.clip(jax.random.normal(first, (POOL, PAGE, LAT + ROPE), jnp.float32), -5.0, 5.0).astype(jnp.bfloat16)


def draw_hidden_in(key, part):
    first, second, third = jax.random.split(jax.random.fold_in(key, 3), 3)
    row_scale = jnp.exp(jax.random.uniform(first, (TOKENS, 1), jnp.float32, math.log(0.3), math.log(3.0)))
    col_scale = jnp.exp(jax.random.uniform(second, (1, D), jnp.float32, math.log(0.3), math.log(3.0)))
    base = jnp.clip(jax.random.normal(third, (TOKENS, D), jnp.float32), -4.0, 4.0)
    return (base * row_scale * col_scale).astype(jnp.bfloat16)


def draw_page_table(key, part):
    streams = jax.random.split(jax.random.fold_in(key, 7), N_EP * N_REQ)
    shuffled = jax.vmap(lambda stream: jax.random.permutation(stream, POOL_DEV))(streams)
    shuffled = shuffled.reshape(N_EP, N_REQ, REQ_DEV, MAXP // N_REQ)
    table = jnp.transpose(shuffled, (0, 2, 3, 1)).reshape(REQUESTS, MAXP)
    return table.astype(jnp.int32)


def draw_cache_len(key, part):
    first, second, third = jax.random.split(jax.random.fold_in(key, 9), 3)
    longer = jax.random.randint(first, (REQUESTS,), 1, LMAX + 1)
    shorter = jax.random.randint(second, (REQUESTS,), 1, LMAX // 8 + 1)
    picked = jax.random.randint(third, (REQUESTS,), 0, 2)
    lengths = jnp.where(picked == 1, longer, shorter)
    return lengths.at[0].set(LMAX).astype(jnp.int32)


def draw_parents(key, part):
    draft_index = jnp.arange(DRAFT, dtype=jnp.int32)
    upper = jnp.maximum(jnp.minimum(draft_index, 4), 1) + 1
    backward = jax.random.randint(jax.random.fold_in(key, 11), (REQUESTS, DRAFT), 1, upper[None, :])
    return (draft_index[None, :] - backward).astype(jnp.int32)


def place_ends(values, stream_key, low, largest):
    longest = values.shape.index(max(values.shape))
    spots = []
    for shift in (0, 1):
        where = [jax.random.randint(jax.random.fold_in(stream_key, axis), (), 0, length) for axis, length in enumerate(values.shape)]
        where[longest] = (where[longest] + shift) % values.shape[longest]
        spots.append(tuple(where))
    return values.at[spots[0]].set(low).at[spots[1]].set(largest)


def levels(stream_key, shape, cuts, least, largest):
    def one(axis_at, shards_of):
        draws = jax.random.uniform(jax.random.fold_in(jax.random.fold_in(stream_key, 6), axis_at), (shards_of,), jnp.float32, least / len(cuts), largest / len(cuts))
        return jnp.repeat(jnp.exp(draws), shape[axis_at] // shards_of).reshape((-1,) + (1,) * (len(shape) - axis_at - 1))

    gain = one(*cuts[0])
    for cut in cuts[1:]:
        gain = gain * one(*cut)
    return gain


def deal_out(key, own, number, rows, count, top, limit, lean):
    order = jax.random.permutation(key, count)
    heavy_load, usual = shares(count, rows * top, limit, lean, True), shares(count, rows * top, limit, lean, False)
    places = jnp.arange(count)

    def named(sizes, rotation):
        used = int((sizes > 0).sum())
        fixed = max(1, used // 4)
        passed = fixed + (places - fixed + rotation * (used - fixed)) % max(1, count - fixed)
        return jnp.zeros((count,), jnp.int32).at[order[jnp.where(places < fixed, places, passed)]].set(jnp.asarray(sizes, jnp.int32))

    sizes = jnp.where(number % 4 == 0, named(heavy_load, number // 4), named(usual, number - number // 4 - 1))
    mixed = jax.random.permutation(jax.random.fold_in(own, 3), count)
    giver, taker = mixed[0:count // 2 * 2:2], mixed[1:count // 2 * 2:2]
    slack = jnp.minimum(sizes[giver] - 1, limit - sizes[taker]) // 2
    slack = jnp.where((giver == order[0]) | (taker == order[0]) | (sizes[taker] == 0), 0, jnp.maximum(slack, 0))
    passed = jax.random.randint(jax.random.fold_in(own, 4), (count // 2,), 0, 1 << 20) % (slack + 1)
    sizes = sizes.at[giver].add(-passed).at[taker].add(passed)
    members = jnp.searchsorted(jnp.cumsum(sizes), jnp.arange(rows * top), side="right").astype(jnp.int32)
    listing = members.reshape(top, rows).T
    listing = listing[jax.random.permutation(jax.random.fold_in(own, 1), rows)]
    rotation = jax.random.randint(jax.random.fold_in(own, 2), (rows, 1), 0, top)
    return jnp.take_along_axis(listing, (jnp.arange(top)[None, :] + rotation) % top, axis=1)


def shares(count, total, bound, skew, full):
    portions = [(1 << 20) // math.isqrt(grade ** skew) + 1 for grade in range(1, count + 1)]
    largest = bound if full else min(bound, max(-(-total // count), total * portions[0] // sum(portions)))
    least = 1 if total - largest >= count - 1 else 0
    counts, spare = [largest] + [least] * (count - 1), total - largest - least * (count - 1)
    while spare > 0:
        free = [i for i in range(1, count) if counts[i] < largest] or [i for i in range(1, count) if counts[i] < bound]
        pool, budget = sum([portions[i] for i in free]), spare
        for i in free:
            extra = min(bound - counts[i], max(1, budget * portions[i] // pool), spare)
            counts[i] = counts[i] + extra
            spare = spare - extra
    return np.array(counts)


def normal_values(rng, extent, scale, bound, cuts=(), kind=jnp.bfloat16):
    gain = levels(rng, extent, cuts, -0.22, 0.18) if cuts else 1.0
    values = jax.random.normal(rng, extent, jnp.float32) * scale * gain
    return jnp.minimum(jnp.maximum(values, -bound), bound).astype(kind)


def setup_inputs(seed: int = 0) -> dict:
    key_list = jax.random.split(jax.random.key(seed), 19)
    queries = draw_queries(jax.random.fold_in(key_list[18], 71), 0)
    draft_latent = normal_values(key_list[1], (TOKENS, KV), 1.0, 5.0, ((0, 32),))
    hidden_in = draw_hidden_in(jax.random.fold_in(key_list[18], 71), 0)
    cache_pool = draw_cache_pool(jax.random.fold_in(key_list[18], 71), 0)
    page_table = draw_page_table(jax.random.fold_in(key_list[18], 71), 0)
    cache_len = draw_cache_len(jax.random.fold_in(key_list[18], 71), 0)
    parents = draw_parents(jax.random.fold_in(key_list[18], 71), 0)
    accept_leaf = place_ends(jax.random.randint(key_list[7], (REQUESTS,), 0, DRAFT), jax.random.fold_in(key_list[7], 1), 0, DRAFT - 1).astype(jnp.int32)
    absorb_key = normal_values(key_list[8], (H, QK_NOPE, LAT), QK_NOPE ** -0.5, 0.5)
    absorb_value = normal_values(key_list[9], (H, LAT, V_HEAD), LAT ** -0.5, 0.25)
    out_proj = normal_values(key_list[10], (H * V_HEAD, D), (H * V_HEAD) ** -0.5, 0.125, ((1, 4),))
    norm_gain = jnp.clip(1.0 + 0.18 * jax.random.normal(key_list[11], (D,), jnp.float32), 0.1, 1.9)
    router = normal_values(key_list[12], (D, EXPERTS), D ** -0.5, 0.125)
    expert_ids_keys = jax.random.split(jax.random.fold_in(key_list[13], 1), TOKENS // TOK_EP)
    expert_ids_turns = jax.random.permutation(jax.random.fold_in(key_list[13], 3), TOKENS // TOK_EP)
    expert_ids = jax.vmap(lambda own, number: deal_out(jax.random.fold_in(key_list[13], 2), own, number, TOK_EP, EXPERTS, TOPK, CAP, 2))(expert_ids_keys, expert_ids_turns).reshape((TOKENS, TOPK))
    expert_gate_up = normal_values(key_list[14], (EXPERTS, 2, D, FF), D ** -0.5, 0.125, ((0, 32), (3, 4)))
    expert_down = normal_values(key_list[15], (EXPERTS, FF, D), FF ** -0.5, 0.15625, ((0, 32), (1, 4)))
    shared_gate_up = normal_values(key_list[16], (2, D, SFF), D ** -0.5, 0.125, ((2, 4),))
    shared_down = normal_values(key_list[17], (SFF, D), SFF ** -0.5, 0.15625, ((0, 4),))
    return dict(queries=queries, draft_latent=draft_latent, hidden_in=hidden_in, cache_pool=cache_pool, page_table=page_table, cache_len=cache_len, parents=parents, accept_leaf=accept_leaf, absorb_key=absorb_key, absorb_value=absorb_value, out_proj=out_proj, norm_gain=norm_gain, router=router, expert_ids=expert_ids, expert_gate_up=expert_gate_up, expert_down=expert_down, shared_gate_up=shared_gate_up, shared_down=shared_down)


def ancestors(parents):
    draft_count = parents.shape[-1]
    draft_index = jnp.arange(draft_count, dtype=jnp.int32)
    ancestry = (parents[:, :, None] == draft_index[None, None, :]).astype(jnp.float32)
    ancestry = ancestry + jnp.eye(draft_count, dtype=jnp.float32)[None]
    for doubling in range(max(1, (draft_count - 1).bit_length())):
        ancestry = jnp.minimum(jnp.einsum('rij,rjk->rik', ancestry, ancestry, precision=lax.Precision.HIGHEST), 1.0)
    return ancestry

def reference(queries, draft_latent, hidden_in, cache_pool, page_table, cache_len, parents, accept_leaf, absorb_key, absorb_value, out_proj, norm_gain, router, expert_ids, expert_gate_up, expert_down, shared_gate_up, shared_down):
    highest = lax.Precision.HIGHEST
    ancestry = ancestors(parents)
    depths = lax.optimization_barrier(jnp.sum(ancestry, axis=2)) - 1.0
    score_scale = 1.0 / math.sqrt(QK_NOPE + ROPE)
    page_index = jnp.arange(MAXP, dtype=jnp.int32)
    groups = jnp.arange(REQUESTS, dtype=jnp.int32) // REQ_DEV
    owners = page_index[None, :] % N_REQ * N_EP + groups[:, None]
    global_pages = (owners * POOL_DEV + page_table).astype(jnp.int32)
    positions = jnp.arange(MAX_LEN, dtype=jnp.int32)
    key_weight = absorb_key.astype(jnp.float32)
    value_weight = absorb_value.astype(jnp.float32)

    def one_request(request_items):
        page_rows, length, tree_mask, query_rows, drafts = request_items
        cached = cache_pool[page_rows].reshape(MAX_LEN, KV).astype(jnp.float32)
        absorbed = jnp.einsum('thd,hdl->thl', query_rows[:, :, :QK_NOPE].astype(jnp.float32), key_weight)
        absorbed = lax.optimization_barrier(absorbed.astype(jnp.bfloat16))
        query_full = jnp.concatenate([absorbed, query_rows[:, :, QK_NOPE:]], axis=2).astype(jnp.float32)
        draft_keys = drafts.astype(jnp.float32)
        cache_ok = positions < length
        tree_ok = tree_mask > 0.5
        score_cache = jnp.einsum('thk,sk->ths', query_full, cached) * score_scale
        score_cache = jnp.where(cache_ok[None, None, :], score_cache, -jnp.inf)
        score_draft = jnp.einsum('thk,sk->ths', query_full, draft_keys) * score_scale
        score_draft = jnp.where(tree_ok[:, None, :], score_draft, -jnp.inf)
        highest_score = jnp.maximum(lax.optimization_barrier(jnp.max(score_cache, axis=2)), lax.optimization_barrier(jnp.max(score_draft, axis=2)))
        weight_cache = jnp.exp(score_cache - highest_score[..., None])
        weight_draft = jnp.exp(score_draft - highest_score[..., None])
        totals = lax.optimization_barrier(jnp.sum(weight_cache, axis=2)) + lax.optimization_barrier(jnp.sum(weight_draft, axis=2))
        weight_cache = lax.optimization_barrier(weight_cache.astype(jnp.bfloat16)).astype(jnp.float32)
        weight_draft = lax.optimization_barrier(weight_draft.astype(jnp.bfloat16)).astype(jnp.float32)
        mixed_latent = jnp.einsum('ths,sl->thl', weight_cache, cached[:, :LAT])
        mixed_latent = mixed_latent + jnp.einsum('ths,sl->thl', weight_draft, draft_keys[:, :LAT])
        head_out = jnp.einsum('thl,hlv->thv', mixed_latent / totals[..., None], value_weight, precision=highest)
        return head_out.astype(jnp.bfloat16).reshape(DRAFT, H * V_HEAD)
    head_rows = lax.map(one_request, (global_pages, cache_len, ancestry, queries.reshape(REQUESTS, DRAFT, H, QK_NOPE + ROPE), draft_latent.reshape(REQUESTS, DRAFT, KV)))
    head_rows = head_rows.reshape(TOKENS, H * V_HEAD)
    attention = jnp.dot(head_rows, out_proj, preferred_element_type=jnp.float32)
    resid = (hidden_in.astype(jnp.float32) + attention).astype(jnp.bfloat16)
    resid_wide = resid.astype(jnp.float32)
    normed = resid_wide * lax.rsqrt(lax.optimization_barrier(jnp.mean(resid_wide * resid_wide, axis=1, keepdims=True)) + 1e-06)
    normed = (normed * norm_gain.astype(jnp.float32)[None, :]).astype(jnp.bfloat16)
    logits = jnp.dot(normed, router, preferred_element_type=jnp.float32)
    lifted = jax.nn.sigmoid(jnp.take_along_axis(logits, expert_ids, axis=1))
    gates = lifted / lax.optimization_barrier(jnp.sum(lifted, axis=1, keepdims=True))
    shared_gate = jnp.dot(normed, shared_gate_up[0], preferred_element_type=jnp.float32)
    shared_lift = jnp.dot(normed, shared_gate_up[1], preferred_element_type=jnp.float32)
    shared_hidden = (jax.nn.silu(shared_gate) * shared_lift).astype(jnp.bfloat16)
    shared_part = jnp.dot(shared_hidden, shared_down, preferred_element_type=jnp.float32)
    pair_experts = expert_ids.reshape(N_EP, TOK_EP * TOPK)
    marks = (pair_experts[:, :, None] == jnp.arange(EXPERTS, dtype=jnp.int32)[None, None, :]).astype(jnp.int32)
    slot_of = lax.optimization_barrier(jnp.sum(jnp.cumsum(marks, axis=1) * marks, axis=2)) - 1
    group_ids = jnp.arange(N_EP, dtype=jnp.int32)
    placement = (pair_experts * N_EP + group_ids[:, None]) * CAP + slot_of
    pair_token = group_ids[:, None] * TOK_EP + jnp.arange(TOK_EP * TOPK, dtype=jnp.int32)[None, :] // TOPK
    source = jnp.full((EXPERTS * N_EP * CAP,), TOKENS, dtype=jnp.int32).at[placement.reshape(-1)].set(pair_token.reshape(-1))
    padded = jnp.concatenate([normed, jnp.zeros((1, D), jnp.bfloat16)], axis=0)

    def one_expert(expert_items):
        row_index, gate_up, down_weight = expert_items
        rows_in = padded[row_index]
        gate_value = jnp.dot(rows_in, gate_up[0], preferred_element_type=jnp.float32)
        lift_value = jnp.dot(rows_in, gate_up[1], preferred_element_type=jnp.float32)
        hidden_rows = (jax.nn.silu(gate_value) * lift_value).astype(jnp.bfloat16)
        return jnp.dot(hidden_rows, down_weight, preferred_element_type=jnp.float32)
    expert_rows = lax.map(one_expert, (source.reshape(EXPERTS, N_EP * CAP), expert_gate_up, expert_down))
    expert_rows = expert_rows.reshape(EXPERTS * N_EP * CAP, D)
    token_place = placement.reshape(TOKENS, TOPK)
    routed = jnp.zeros((TOKENS, D), jnp.float32)
    for rank in range(TOPK):
        routed = routed + gates[:, rank:rank + 1] * expert_rows[token_place[:, rank]]
    layer_out = (resid_wide + shared_part + routed).astype(jnp.bfloat16)
    starts = cache_len // PAGE
    accepted = ancestry[jnp.arange(REQUESTS, dtype=jnp.int32), accept_leaf]
    own_latent = draft_latent.reshape(REQUESTS, DRAFT, KV).astype(jnp.float32)
    pieces = []
    for req_pos in range(N_REQ):
        page_now = starts + (req_pos - starts) % N_REQ
        slot_now = jnp.take_along_axis(global_pages, page_now[:, None], axis=1)[:, 0]
        old_page = cache_pool[slot_now].astype(jnp.float32)
        offsets = (page_now[:, None] * PAGE + jnp.arange(PAGE, dtype=jnp.int32)[None, :] - cache_len[:, None]).astype(jnp.float32)
        select = accepted[:, None, :] * (depths[:, None, :] == offsets[:, :, None]).astype(jnp.float32)
        written = jnp.einsum('rod,rdk->rok', select, own_latent, precision=highest)
        touched = lax.optimization_barrier(jnp.sum(select, axis=2)) > 0.5
        pieces.append(jnp.where(touched[..., None], written, old_page).astype(jnp.bfloat16))
    new_pages = jnp.stack(pieces, axis=1)
    return (layer_out, new_pages)
```

```python
import math

import jax
import jax.numpy as jnp
from jax import lax
from jax.sharding import PartitionSpec as P

NEGATIVE = -1e30


def ancestors(parents):
    draft_count = parents.shape[-1]
    draft_index = jnp.arange(draft_count, dtype=jnp.int32)
    ancestry = (parents[:, :, None] == draft_index[None, None, :]).astype(jnp.float32)
    ancestry = ancestry + jnp.eye(draft_count, dtype=jnp.float32)[None]
    for doubling in range(max(1, (draft_count - 1).bit_length())):
        ancestry = jnp.minimum(
            jnp.einsum("rij,rjk->rik", ancestry, ancestry, precision=lax.Precision.HIGHEST), 1.0
        )
    return ancestry


def per_device(
    queries,
    draft_latent,
    hidden_in,
    cache_pool,
    page_table,
    cache_len,
    parents,
    accept_leaf,
    absorb_key,
    absorb_value,
    out_proj,
    norm_gain,
    router,
    expert_ids,
    expert_gate_up,
    expert_down,
    shared_gate_up,
    shared_down,
):
    highest = lax.Precision.HIGHEST
    req_count = lax.axis_size("req")
    req_index = lax.axis_index("req")
    ep_count = lax.axis_size("ep")
    request_count, draft_count = parents.shape
    token_count = request_count * draft_count
    head_count = queries.shape[1]
    nope_width = absorb_key.shape[1]
    latent_width = absorb_key.shape[2]
    page_size = cache_pool.shape[1]
    key_width = cache_pool.shape[2]
    page_count = page_table.shape[1]
    score_scale = 1.0 / math.sqrt(queries.shape[2])
    ancestry = ancestors(parents)
    depths = jnp.sum(ancestry, axis=2) - 1.0
    local_pages = page_count // req_count
    page_cols = req_index + req_count * jnp.arange(local_pages, dtype=jnp.int32)
    slot_rows = jnp.take(page_table, page_cols, axis=1)
    cached = cache_pool[slot_rows].reshape(request_count, local_pages * page_size, key_width)
    positions = (
        page_cols[:, None] * page_size + jnp.arange(page_size, dtype=jnp.int32)[None, :]
    ).reshape(-1)
    cache_ok = positions[None, :] < cache_len[:, None]
    draft_share = draft_count // req_count
    draft_cols = req_index * draft_share + jnp.arange(draft_share, dtype=jnp.int32)
    own_latent = draft_latent.reshape(request_count, draft_count, key_width)
    draft_keys = jnp.take(own_latent, draft_cols, axis=1)
    tree_ok = jnp.take(ancestry, draft_cols, axis=2) > 0.5
    absorbed = jnp.einsum(
        "thd,hdl->thl", queries[:, :, :nope_width], absorb_key, preferred_element_type=jnp.float32
    ).astype(jnp.bfloat16)
    query_full = jnp.concatenate([absorbed, queries[:, :, nope_width:]], axis=2)
    query_full = query_full.reshape(request_count, draft_count, head_count, key_width)
    score_cache = (
        jnp.einsum("rthk,rsk->rths", query_full, cached, preferred_element_type=jnp.float32)
        * score_scale
    )
    score_cache = jnp.where(cache_ok[:, None, None, :], score_cache, NEGATIVE)
    score_draft = (
        jnp.einsum("rthk,rsk->rths", query_full, draft_keys, preferred_element_type=jnp.float32)
        * score_scale
    )
    score_draft = jnp.where(tree_ok[:, :, None, :], score_draft, NEGATIVE)
    highest_score = jnp.maximum(jnp.max(score_cache, axis=3), jnp.max(score_draft, axis=3))
    weight_cache = jnp.where(
        cache_ok[:, None, None, :], jnp.exp(score_cache - highest_score[..., None]), 0.0
    )
    weight_draft = jnp.where(
        tree_ok[:, :, None, :], jnp.exp(score_draft - highest_score[..., None]), 0.0
    )
    totals = jnp.sum(weight_cache, axis=3) + jnp.sum(weight_draft, axis=3)
    mixed_latent = jnp.einsum(
        "rths,rsl->rthl",
        weight_cache.astype(jnp.bfloat16),
        cached[:, :, :latent_width],
        preferred_element_type=jnp.float32,
    )
    mixed_latent = mixed_latent + jnp.einsum(
        "rths,rsl->rthl",
        weight_draft.astype(jnp.bfloat16),
        draft_keys[:, :, :latent_width],
        preferred_element_type=jnp.float32,
    )
    value_weight = absorb_value.astype(jnp.float32)
    partial_head = jnp.einsum("rthl,hlv->rthv", mixed_latent, value_weight, precision=highest)
    head_width = head_count * partial_head.shape[-1]
    packed = jnp.concatenate(
        [
            partial_head.reshape(token_count, head_width),
            highest_score.reshape(token_count, head_count),
            totals.reshape(token_count, head_count),
        ],
        axis=1,
    )
    gathered = lax.all_gather(packed, "req")
    part_heads = gathered[:, :, :head_width].reshape(req_count, token_count, head_count, -1)
    part_max = gathered[:, :, head_width : head_width + head_count]
    part_sum = gathered[:, :, head_width + head_count :]
    top = jnp.max(part_max, axis=0)
    factor = jnp.exp(part_max - top[None])
    merged_sum = jnp.sum(factor * part_sum, axis=0)
    head_out = jnp.sum(factor[..., None] * part_heads, axis=0) / merged_sum[..., None]
    head_rows = head_out.astype(jnp.bfloat16).reshape(token_count, -1)
    attention = jnp.dot(head_rows, out_proj, preferred_element_type=jnp.float32)
    resid_cols = (hidden_in.astype(jnp.float32) + attention).astype(jnp.bfloat16)
    resid = lax.all_gather(resid_cols, "req", axis=1, tiled=True)
    resid_wide = resid.astype(jnp.float32)
    normed = resid_wide * lax.rsqrt(
        jnp.mean(resid_wide * resid_wide, axis=1, keepdims=True) + 1e-06
    )
    normed = (normed * norm_gain[None, :]).astype(jnp.bfloat16)
    logits = jnp.dot(normed, router, preferred_element_type=jnp.float32)
    lifted = jax.nn.sigmoid(jnp.take_along_axis(logits, expert_ids, axis=1))
    gates = lifted / jnp.sum(lifted, axis=1, keepdims=True)
    shared_gate = jnp.dot(normed, shared_gate_up[0], preferred_element_type=jnp.float32)
    shared_lift = jnp.dot(normed, shared_gate_up[1], preferred_element_type=jnp.float32)
    shared_hidden = (jax.nn.silu(shared_gate) * shared_lift).astype(jnp.bfloat16)
    shared_part = jnp.dot(shared_hidden, shared_down, preferred_element_type=jnp.float32)
    route_width = expert_ids.shape[1]
    local_experts = expert_gate_up.shape[0]
    expert_total = local_experts * ep_count
    capacity = (2 * token_count * route_width + expert_total - 1) // expert_total
    pair_experts = expert_ids.reshape(-1)
    marks = (pair_experts[:, None] == jnp.arange(expert_total, dtype=jnp.int32)[None, :]).astype(
        jnp.int32
    )
    slot_of = jnp.sum(jnp.cumsum(marks, axis=0) * marks, axis=1) - 1
    placement = (pair_experts * capacity + slot_of).reshape(token_count, route_width)
    slot_count = expert_total * capacity
    slot_index = jnp.arange(slot_count, dtype=jnp.int32)
    hits = placement[None, :, :] == slot_index[:, None, None]
    dispatch = jnp.any(hits, axis=2).astype(jnp.bfloat16)
    outgoing = jnp.dot(dispatch, normed, preferred_element_type=jnp.float32).astype(jnp.bfloat16)
    outgoing = outgoing.reshape(ep_count, local_experts, capacity, -1)
    gate_weight = expert_gate_up[:, 0]
    lift_weight = expert_gate_up[:, 1]
    incoming = lax.all_to_all(outgoing, "ep", split_axis=0, concat_axis=0, tiled=True)
    gate_value = jnp.einsum(
        "pecd,edf->pecf", incoming, gate_weight, preferred_element_type=jnp.float32
    )
    lift_value = jnp.einsum(
        "pecd,edf->pecf", incoming, lift_weight, preferred_element_type=jnp.float32
    )
    hidden_rows = (jax.nn.silu(gate_value) * lift_value).astype(jnp.bfloat16)
    result = jnp.einsum(
        "pecf,efd->pecd", hidden_rows, expert_down, preferred_element_type=jnp.float32
    )
    returned = lax.all_to_all(
        result.astype(jnp.bfloat16), "ep", split_axis=0, concat_axis=0, tiled=True
    ).reshape(slot_count, -1)
    combine = jnp.sum(
        jnp.where(
            placement[:, :, None] == slot_index[None, None, :], gates[:, :, None], 0.0
        ),
        axis=1,
    )
    combine_high = combine.astype(jnp.bfloat16)
    combine_low = (combine - combine_high.astype(jnp.float32)).astype(jnp.bfloat16)
    routed = jnp.dot(combine_high, returned, preferred_element_type=jnp.float32) + jnp.dot(
        combine_low, returned, preferred_element_type=jnp.float32
    )
    term = shared_part + routed
    summed = lax.psum_scatter(
        term.astype(jnp.bfloat16), "req", scatter_dimension=1, tiled=True
    ).astype(jnp.float32)
    layer_out = (resid_cols.astype(jnp.float32) + summed).astype(jnp.bfloat16)
    starts = cache_len // page_size
    page_now = starts + jnp.mod(req_index - starts, req_count)
    slot_now = jnp.take_along_axis(page_table, page_now[:, None], axis=1)[:, 0]
    old_page = cache_pool[slot_now]
    offsets = (
        page_now[:, None] * page_size
        + jnp.arange(page_size, dtype=jnp.int32)[None, :]
        - cache_len[:, None]
    ).astype(jnp.float32)
    accepted = jnp.take_along_axis(ancestry, accept_leaf[:, None, None], axis=1)[:, 0, :]
    select = accepted[:, None, :] * (depths[:, None, :] == offsets[:, :, None]).astype(jnp.float32)
    written = jnp.einsum(
        "rod,rdk->rok", select.astype(jnp.bfloat16), own_latent, preferred_element_type=jnp.float32
    )
    touched = jnp.sum(select, axis=2) > 0.5
    fresh = jnp.where(touched[..., None], written, old_page.astype(jnp.float32)).astype(
        jnp.bfloat16
    )
    return (layer_out, fresh[:, None])


def solution(mesh):
    in_specs = (
        P("ep", None, None),
        P("ep", None),
        P("ep", "req"),
        P(("req", "ep"), None, None),
        P("ep", None),
        P("ep"),
        P("ep", None),
        P("ep"),
        P(),
        P(),
        P(None, "req"),
        P(),
        P(),
        P("ep", None),
        P("ep", None, None, "req"),
        P("ep", "req", None),
        P(None, None, "req"),
        P("req", None),
    )
    out_specs = (P("ep", "req"), P("ep", "req", None, None))
    return jax.shard_map(
        per_device, mesh=mesh, in_specs=in_specs, out_specs=out_specs, check_vma=False
    )
```

```python
import math

import jax
import jax.numpy as jnp
from jax import lax
from jax.sharding import PartitionSpec as P

NEGATIVE = -1e30


def ancestors(parents):
    draft_count = parents.shape[-1]
    draft_index = jnp.arange(draft_count, dtype=jnp.int32)
    ancestry = (parents[:, :, None] == draft_index[None, None, :]).astype(jnp.float32)
    ancestry = ancestry + jnp.eye(draft_count, dtype=jnp.float32)[None]
    for doubling in range(max(1, (draft_count - 1).bit_length())):
        ancestry = jnp.minimum(
            jnp.einsum("rij,rjk->rik", ancestry, ancestry, precision=lax.Precision.HIGHEST), 1.0
        )
    return ancestry


def split_exact(values):
    pieces = []
    rest = values
    for _ in range(3):
        piece = lax.reduce_precision(rest, exponent_bits=8, mantissa_bits=7)
        pieces.append(piece.astype(jnp.bfloat16))
        rest = rest - piece
    return pieces


def per_device(
    queries,
    draft_latent,
    hidden_in,
    cache_pool,
    page_table,
    cache_len,
    parents,
    accept_leaf,
    absorb_key,
    absorb_value,
    out_proj,
    norm_gain,
    router,
    expert_ids,
    expert_gate_up,
    expert_down,
    shared_gate_up,
    shared_down,
):
    highest = lax.Precision.HIGHEST
    req_count = lax.axis_size("req")
    req_index = lax.axis_index("req")
    ep_count = lax.axis_size("ep")
    request_count, draft_count = parents.shape
    token_count = request_count * draft_count
    head_count = queries.shape[1]
    nope_width = absorb_key.shape[1]
    latent_width = absorb_key.shape[2]
    page_size = cache_pool.shape[1]
    key_width = cache_pool.shape[2]
    page_count = page_table.shape[1]
    score_scale = 1.0 / math.sqrt(queries.shape[2])
    ancestry = ancestors(parents)
    depths = jnp.sum(ancestry, axis=2) - 1.0
    local_pages = page_count // req_count
    page_cols = req_index + req_count * jnp.arange(local_pages, dtype=jnp.int32)
    slot_rows = jnp.take(page_table, page_cols, axis=1)
    cached = cache_pool[slot_rows].reshape(request_count, local_pages * page_size, key_width)
    positions = (
        page_cols[:, None] * page_size + jnp.arange(page_size, dtype=jnp.int32)[None, :]
    ).reshape(-1)
    cache_ok = positions[None, :] < cache_len[:, None]
    draft_share = draft_count // req_count
    draft_cols = req_index * draft_share + jnp.arange(draft_share, dtype=jnp.int32)
    own_latent = draft_latent.reshape(request_count, draft_count, key_width)
    draft_keys = jnp.take(own_latent, draft_cols, axis=1)
    tree_ok = jnp.take(ancestry, draft_cols, axis=2) > 0.5
    absorbed = jnp.einsum(
        "thd,hdl->thl", queries[:, :, :nope_width], absorb_key, preferred_element_type=jnp.float32
    ).astype(jnp.bfloat16)
    query_full = jnp.concatenate([absorbed, queries[:, :, nope_width:]], axis=2)
    query_full = query_full.reshape(request_count, draft_count, head_count, key_width)
    score_cache = (
        jnp.einsum("rthk,rsk->rths", query_full, cached, preferred_element_type=jnp.float32)
        * score_scale
    )
    score_cache = jnp.where(cache_ok[:, None, None, :], score_cache, NEGATIVE)
    score_draft = (
        jnp.einsum("rthk,rsk->rths", query_full, draft_keys, preferred_element_type=jnp.float32)
        * score_scale
    )
    score_draft = jnp.where(tree_ok[:, :, None, :], score_draft, NEGATIVE)
    highest_score = jnp.maximum(jnp.max(score_cache, axis=3), jnp.max(score_draft, axis=3))
    weight_cache = jnp.where(
        cache_ok[:, None, None, :], jnp.exp(score_cache - highest_score[..., None]), 0.0
    )
    weight_draft = jnp.where(
        tree_ok[:, :, None, :], jnp.exp(score_draft - highest_score[..., None]), 0.0
    )
    totals = jnp.sum(weight_cache, axis=3) + jnp.sum(weight_draft, axis=3)
    mixed_latent = jnp.einsum(
        "rths,rsl->rthl",
        weight_cache.astype(jnp.bfloat16),
        cached[:, :, :latent_width],
        preferred_element_type=jnp.float32,
    )
    mixed_latent = mixed_latent + jnp.einsum(
        "rths,rsl->rthl",
        weight_draft.astype(jnp.bfloat16),
        draft_keys[:, :, :latent_width],
        preferred_element_type=jnp.float32,
    )
    value_weight = absorb_value.astype(jnp.float32)
    partial_head = jnp.einsum("rthl,hlv->rthv", mixed_latent, value_weight, precision=highest)
    head_width = head_count * partial_head.shape[-1]
    low_parts = split_exact(jnp.concatenate([highest_score, totals], axis=-1))
    packed = jnp.concatenate(
        [partial_head.reshape(token_count, head_width).astype(jnp.bfloat16)]
        + [part.reshape(token_count, 2 * head_count) for part in low_parts],
        axis=1,
    )
    gathered = lax.all_gather(packed, "req").astype(jnp.float32)
    part_heads = gathered[:, :, :head_width].reshape(req_count, token_count, head_count, -1)
    rejoined = sum(
        gathered[:, :, head_width + 2 * head_count * k : head_width + 2 * head_count * (k + 1)]
        for k in range(3)
    )
    part_max = rejoined[:, :, :head_count]
    part_sum = rejoined[:, :, head_count:]
    top = jnp.max(part_max, axis=0)
    factor = jnp.exp(part_max - top[None])
    merged_sum = jnp.sum(factor * part_sum, axis=0)
    head_out = jnp.sum(factor[..., None] * part_heads, axis=0) / merged_sum[..., None]
    head_rows = head_out.astype(jnp.bfloat16).reshape(token_count, -1)
    attention = jnp.dot(head_rows, out_proj, preferred_element_type=jnp.float32)
    resid_cols = (hidden_in.astype(jnp.float32) + attention).astype(jnp.bfloat16)
    resid = lax.all_gather(resid_cols, "req", axis=1, tiled=True)
    resid_wide = resid.astype(jnp.float32)
    normed = resid_wide * lax.rsqrt(
        jnp.mean(resid_wide * resid_wide, axis=1, keepdims=True) + 1e-06
    )
    normed = (normed * norm_gain[None, :]).astype(jnp.bfloat16)
    logits = jnp.dot(normed, router, preferred_element_type=jnp.float32)
    lifted = jax.nn.sigmoid(jnp.take_along_axis(logits, expert_ids, axis=1))
    gates = lifted / jnp.sum(lifted, axis=1, keepdims=True)
    shared_gate = jnp.dot(normed, shared_gate_up[0], preferred_element_type=jnp.float32)
    shared_lift = jnp.dot(normed, shared_gate_up[1], preferred_element_type=jnp.float32)
    shared_hidden = (jax.nn.silu(shared_gate) * shared_lift).astype(jnp.bfloat16)
    shared_part = jnp.dot(shared_hidden, shared_down, preferred_element_type=jnp.float32)
    route_width = expert_ids.shape[1]
    local_experts = expert_gate_up.shape[0]
    expert_total = local_experts * ep_count
    capacity = (2 * token_count * route_width + expert_total - 1) // expert_total
    pair_experts = expert_ids.reshape(-1)
    marks = (pair_experts[:, None] == jnp.arange(expert_total, dtype=jnp.int32)[None, :]).astype(
        jnp.int32
    )
    slot_of = jnp.sum(jnp.cumsum(marks, axis=0) * marks, axis=1) - 1
    placement = (pair_experts * capacity + slot_of).reshape(token_count, route_width)
    slot_count = expert_total * capacity
    slot_index = jnp.arange(slot_count, dtype=jnp.int32)
    hits = placement[None, :, :] == slot_index[:, None, None]
    dispatch = jnp.any(hits, axis=2).astype(jnp.bfloat16)
    outgoing = jnp.dot(dispatch, normed, preferred_element_type=jnp.float32).astype(jnp.bfloat16)
    outgoing = outgoing.reshape(ep_count, local_experts, capacity, -1)
    gate_weight = expert_gate_up[:, 0]
    lift_weight = expert_gate_up[:, 1]
    incoming = lax.all_to_all(outgoing, "ep", split_axis=0, concat_axis=0, tiled=True)
    gate_value = jnp.einsum(
        "pecd,edf->pecf", incoming, gate_weight, preferred_element_type=jnp.float32
    )
    lift_value = jnp.einsum(
        "pecd,edf->pecf", incoming, lift_weight, preferred_element_type=jnp.float32
    )
    hidden_rows = (jax.nn.silu(gate_value) * lift_value).astype(jnp.bfloat16)
    result = jnp.einsum(
        "pecf,efd->pecd", hidden_rows, expert_down, preferred_element_type=jnp.float32
    )
    feature_share = result.shape[-1] // req_count
    sending = result.astype(jnp.bfloat16).reshape(
        ep_count, local_experts, capacity, req_count, feature_share
    )
    sending = jnp.transpose(sending, (3, 0, 1, 2, 4)).reshape(
        req_count * ep_count, local_experts, capacity, feature_share
    )
    returned = lax.all_to_all(sending, ("req", "ep"), 0, 0, tiled=True).reshape(
        req_count * slot_count, feature_share
    )
    combine = jnp.sum(
        jnp.where(
            placement[:, :, None] == slot_index[None, None, :], gates[:, :, None], 0.0
        ),
        axis=1,
    )
    combine = jnp.tile(combine, (1, req_count))
    combine_high = combine.astype(jnp.bfloat16)
    combine_low = (combine - combine_high.astype(jnp.float32)).astype(jnp.bfloat16)
    routed = jnp.dot(combine_high, returned, preferred_element_type=jnp.float32) + jnp.dot(
        combine_low, returned, preferred_element_type=jnp.float32
    )
    shared_cols = lax.psum_scatter(
        shared_part.astype(jnp.bfloat16), "req", scatter_dimension=1, tiled=True
    )
    layer_out = (
        resid_cols.astype(jnp.float32) + shared_cols.astype(jnp.float32) + routed
    ).astype(jnp.bfloat16)
    starts = cache_len // page_size
    page_now = starts + jnp.mod(req_index - starts, req_count)
    slot_now = jnp.take_along_axis(page_table, page_now[:, None], axis=1)[:, 0]
    old_page = cache_pool[slot_now]
    offsets = (
        page_now[:, None] * page_size
        + jnp.arange(page_size, dtype=jnp.int32)[None, :]
        - cache_len[:, None]
    ).astype(jnp.float32)
    accepted = jnp.take_along_axis(ancestry, accept_leaf[:, None, None], axis=1)[:, 0, :]
    select = accepted[:, None, :] * (depths[:, None, :] == offsets[:, :, None]).astype(jnp.float32)
    written = jnp.einsum(
        "rod,rdk->rok", select.astype(jnp.bfloat16), own_latent, preferred_element_type=jnp.float32
    )
    touched = jnp.sum(select, axis=2) > 0.5
    fresh = jnp.where(touched[..., None], written, old_page.astype(jnp.float32)).astype(
        jnp.bfloat16
    )
    return (layer_out, fresh[:, None])


def solution(mesh):
    in_specs = (
        P("ep", None, None),
        P("ep", None),
        P("ep", "req"),
        P(("req", "ep"), None, None),
        P("ep", None),
        P("ep"),
        P("ep", None),
        P("ep"),
        P(),
        P(),
        P(None, "req"),
        P(),
        P(),
        P("ep", None),
        P("ep", None, None, "req"),
        P("ep", "req", None),
        P(None, None, "req"),
        P("req", None),
    )
    out_specs = (P("ep", "req"), P("ep", "req", None, None))
    return jax.shard_map(
        per_device, mesh=mesh, in_specs=in_specs, out_specs=out_specs, check_vma=False
    )
```

```python
import functools
import math

import jax
import jax.numpy as jnp
from jax import lax
from jax.experimental import pallas as pl
from jax.experimental.pallas import tpu as pltpu
from jax.sharding import PartitionSpec as P

NEGATIVE = -1e30


def ancestors(parents):
    draft_count = parents.shape[-1]
    draft_index = jnp.arange(draft_count, dtype=jnp.int32)
    ancestry = (parents[:, :, None] == draft_index[None, None, :]).astype(jnp.float32)
    ancestry = ancestry + jnp.eye(draft_count, dtype=jnp.float32)[None]
    for doubling in range(max(1, (draft_count - 1).bit_length())):
        ancestry = jnp.minimum(
            jnp.einsum("rij,rjk->rik", ancestry, ancestry, precision=lax.Precision.HIGHEST), 1.0
        )
    return ancestry


def split_exact(values):
    pieces = []
    rest = values
    for _ in range(3):
        piece = lax.reduce_precision(rest, exponent_bits=8, mantissa_bits=7)
        pieces.append(piece.astype(jnp.bfloat16))
        rest = rest - piece
    return pieces


def attention_kernel(
    slots_ref, limits_ref, q_ref, page_ref, draft_ref, tree_ref, mixed_ref, stats_ref, keys,
    *, page_size, latent_width, score_scale, row_block
):
    request = pl.program_id(0)
    page = pl.program_id(1)
    page_total = pl.num_programs(1)
    keys[pl.ds(pl.multiple_of(page * page_size, page_size), page_size), :] = page_ref[0]

    @pl.when(page == page_total - 1)
    def _():
        key_rows = keys.shape[0]
        column = lax.broadcasted_iota(jnp.int32, (1, key_rows), 1)
        limit = jnp.zeros((1, key_rows), jnp.int32)
        for index in range(key_rows // page_size):
            limit = jnp.where(column // page_size == index, limits_ref[request, index], limit)
        cache_ok = (column % page_size) < limit
        lane = lax.broadcasted_iota(jnp.int32, (row_block, stats_ref.shape[2]), 1)

        def body(block, carry):
            rows = pl.ds(pl.multiple_of(block * row_block, row_block), row_block)
            query = q_ref[0, rows, :]
            contract = (((1,), (1,)), ((), ()))
            score = lax.dot_general(
                query, keys[...], contract, preferred_element_type=jnp.float32
            ) * score_scale
            score = jnp.where(cache_ok, score, NEGATIVE)
            draft_score = lax.dot_general(
                query, draft_ref[0], contract, preferred_element_type=jnp.float32
            ) * score_scale
            tree_ok = tree_ref[0, rows, :] > 0.5
            draft_score = jnp.where(tree_ok, draft_score, NEGATIVE)
            top = jnp.maximum(
                jnp.max(score, axis=1, keepdims=True), jnp.max(draft_score, axis=1, keepdims=True)
            )
            weight = jnp.where(cache_ok, jnp.exp(score - top), 0.0)
            draft_weight = jnp.where(tree_ok, jnp.exp(draft_score - top), 0.0)
            total = jnp.sum(weight, axis=1, keepdims=True) + jnp.sum(
                draft_weight, axis=1, keepdims=True
            )
            mixed = jnp.dot(
                weight.astype(jnp.bfloat16),
                keys[:, :latent_width],
                preferred_element_type=jnp.float32,
            ) + jnp.dot(
                draft_weight.astype(jnp.bfloat16),
                draft_ref[0, :, :latent_width],
                preferred_element_type=jnp.float32,
            )
            mixed_ref[0, rows, :] = mixed
            stats_ref[0, rows, :] = jnp.where(lane == 0, top, jnp.where(lane == 1, total, 0.0))
            return carry

        lax.fori_loop(0, q_ref.shape[1] // row_block, body, 0)


def paged_attention(slots, limits, query_rows, cache_pool, draft_rows, tree_rows, latent_width, score_scale):
    request_count, row_count, key_width = query_rows.shape
    local_pages = slots.shape[1]
    page_size = cache_pool.shape[1]
    draft_pad = draft_rows.shape[1]
    row_block = 128
    kernel = functools.partial(
        attention_kernel,
        page_size=page_size,
        latent_width=latent_width,
        score_scale=score_scale,
        row_block=row_block,
    )
    key_rows = local_pages * page_size
    flops = 2 * request_count * row_count * (key_rows + draft_pad) * (key_width + latent_width)
    cost = pl.CostEstimate(
        flops=flops,
        transcendentals=request_count * row_count * (key_rows + draft_pad),
        bytes_accessed=2 * request_count * (row_count + key_rows) * key_width
        + 4 * request_count * row_count * (latent_width + 128 + draft_pad),
    )
    grid_spec = pltpu.PrefetchScalarGridSpec(
        num_scalar_prefetch=2,
        grid=(request_count, local_pages),
        in_specs=[
            pl.BlockSpec((1, row_count, key_width), lambda r, j, s, n: (r, 0, 0)),
            pl.BlockSpec((1, page_size, key_width), lambda r, j, s, n: (s[r, j], 0, 0)),
            pl.BlockSpec((1, draft_pad, key_width), lambda r, j, s, n: (r, 0, 0)),
            pl.BlockSpec((1, row_count, draft_pad), lambda r, j, s, n: (r, 0, 0)),
        ],
        out_specs=[
            pl.BlockSpec((1, row_count, latent_width), lambda r, j, s, n: (r, 0, 0)),
            pl.BlockSpec((1, row_count, 128), lambda r, j, s, n: (r, 0, 0)),
        ],
        scratch_shapes=[pltpu.VMEM((key_rows, key_width), jnp.bfloat16)],
    )
    return pl.pallas_call(
        kernel,
        grid_spec=grid_spec,
        out_shape=[
            jax.ShapeDtypeStruct((request_count, row_count, latent_width), jnp.float32),
            jax.ShapeDtypeStruct((request_count, row_count, 128), jnp.float32),
        ],
        compiler_params=pltpu.CompilerParams(
            dimension_semantics=("arbitrary", "arbitrary"), vmem_limit_bytes=48 * 1024 * 1024
        ),
        cost_estimate=cost,
    )(slots, limits, query_rows, cache_pool, draft_rows, tree_rows)


def per_device(
    queries,
    draft_latent,
    hidden_in,
    cache_pool,
    page_table,
    cache_len,
    parents,
    accept_leaf,
    absorb_key,
    absorb_value,
    out_proj,
    norm_gain,
    router,
    expert_ids,
    expert_gate_up,
    expert_down,
    shared_gate_up,
    shared_down,
):
    highest = lax.Precision.HIGHEST
    req_count = lax.axis_size("req")
    req_index = lax.axis_index("req")
    ep_count = lax.axis_size("ep")
    request_count, draft_count = parents.shape
    token_count = request_count * draft_count
    head_count = queries.shape[1]
    nope_width = absorb_key.shape[1]
    latent_width = absorb_key.shape[2]
    page_size = cache_pool.shape[1]
    key_width = cache_pool.shape[2]
    page_count = page_table.shape[1]
    score_scale = 1.0 / math.sqrt(queries.shape[2])
    ancestry = ancestors(parents)
    depths = jnp.sum(ancestry, axis=2) - 1.0
    local_pages = page_count // req_count
    page_cols = req_index + req_count * jnp.arange(local_pages, dtype=jnp.int32)
    slot_rows = jnp.take(page_table, page_cols, axis=1)
    pool_slots = cache_pool.shape[0]
    slot_rows = jnp.clip(slot_rows, 0, pool_slots - 1).astype(jnp.int32)
    limits = jnp.clip(
        cache_len[:, None] - page_cols[None, :] * page_size, 0, page_size
    ).astype(jnp.int32)
    draft_share = draft_count // req_count
    draft_cols = req_index * draft_share + jnp.arange(draft_share, dtype=jnp.int32)
    own_latent = draft_latent.reshape(request_count, draft_count, key_width)
    draft_keys = jnp.take(own_latent, draft_cols, axis=1)
    draft_pad = 128
    draft_rows = jnp.pad(draft_keys, ((0, 0), (0, draft_pad - draft_share), (0, 0)))
    tree_ok = (jnp.take(ancestry, draft_cols, axis=2) > 0.5).astype(jnp.float32)
    tree_rows = jnp.broadcast_to(
        tree_ok[:, :, None, :], (request_count, draft_count, head_count, draft_share)
    ).reshape(request_count, draft_count * head_count, draft_share)
    tree_rows = jnp.pad(tree_rows, ((0, 0), (0, 0), (0, draft_pad - draft_share)))
    absorbed = jnp.einsum(
        "thd,hdl->thl", queries[:, :, :nope_width], absorb_key, preferred_element_type=jnp.float32
    ).astype(jnp.bfloat16)
    query_full = jnp.concatenate([absorbed, queries[:, :, nope_width:]], axis=2)
    query_rows = query_full.reshape(request_count, draft_count * head_count, key_width)
    mixed_rows, stats = paged_attention(
        slot_rows, limits, query_rows, cache_pool, draft_rows, tree_rows, latent_width, score_scale
    )
    mixed_latent = mixed_rows.reshape(request_count, draft_count, head_count, latent_width)
    highest_score = stats[:, :, 0].reshape(request_count, draft_count, head_count)
    totals = stats[:, :, 1].reshape(request_count, draft_count, head_count)
    value_weight = absorb_value.astype(jnp.float32)
    partial_head = jnp.einsum("rthl,hlv->rthv", mixed_latent, value_weight, precision=highest)
    head_width = head_count * partial_head.shape[-1]
    low_parts = split_exact(jnp.concatenate([highest_score, totals], axis=-1))
    packed = jnp.concatenate(
        [partial_head.reshape(token_count, head_width).astype(jnp.bfloat16)]
        + [part.reshape(token_count, 2 * head_count) for part in low_parts],
        axis=1,
    )
    gathered = lax.all_gather(packed, "req").astype(jnp.float32)
    part_heads = gathered[:, :, :head_width].reshape(req_count, token_count, head_count, -1)
    rejoined = sum(
        gathered[:, :, head_width + 2 * head_count * k : head_width + 2 * head_count * (k + 1)]
        for k in range(3)
    )
    part_max = rejoined[:, :, :head_count]
    part_sum = rejoined[:, :, head_count:]
    top = jnp.max(part_max, axis=0)
    factor = jnp.exp(part_max - top[None])
    merged_sum = jnp.sum(factor * part_sum, axis=0)
    head_out = jnp.sum(factor[..., None] * part_heads, axis=0) / merged_sum[..., None]
    head_rows = head_out.astype(jnp.bfloat16).reshape(token_count, -1)
    attention = jnp.dot(head_rows, out_proj, preferred_element_type=jnp.float32)
    resid_cols = (hidden_in.astype(jnp.float32) + attention).astype(jnp.bfloat16)
    resid = lax.all_gather(resid_cols, "req", axis=1, tiled=True)
    resid_wide = resid.astype(jnp.float32)
    normed = resid_wide * lax.rsqrt(
        jnp.mean(resid_wide * resid_wide, axis=1, keepdims=True) + 1e-06
    )
    normed = (normed * norm_gain[None, :]).astype(jnp.bfloat16)
    logits = jnp.dot(normed, router, preferred_element_type=jnp.float32)
    lifted = jax.nn.sigmoid(jnp.take_along_axis(logits, expert_ids, axis=1))
    gates = lifted / jnp.sum(lifted, axis=1, keepdims=True)
    shared_gate = jnp.dot(normed, shared_gate_up[0], preferred_element_type=jnp.float32)
    shared_lift = jnp.dot(normed, shared_gate_up[1], preferred_element_type=jnp.float32)
    shared_hidden = (jax.nn.silu(shared_gate) * shared_lift).astype(jnp.bfloat16)
    shared_part = jnp.dot(shared_hidden, shared_down, preferred_element_type=jnp.float32)
    route_width = expert_ids.shape[1]
    local_experts = expert_gate_up.shape[0]
    expert_total = local_experts * ep_count
    capacity = (2 * token_count * route_width + expert_total - 1) // expert_total
    pair_experts = expert_ids.reshape(-1)
    marks = (pair_experts[:, None] == jnp.arange(expert_total, dtype=jnp.int32)[None, :]).astype(
        jnp.int32
    )
    slot_of = jnp.sum(jnp.cumsum(marks, axis=0) * marks, axis=1) - 1
    placement = (pair_experts * capacity + slot_of).reshape(token_count, route_width)
    slot_count = expert_total * capacity
    slot_index = jnp.arange(slot_count, dtype=jnp.int32)
    hits = placement[None, :, :] == slot_index[:, None, None]
    dispatch = jnp.any(hits, axis=2).astype(jnp.bfloat16)
    outgoing = jnp.dot(dispatch, normed, preferred_element_type=jnp.float32).astype(jnp.bfloat16)
    outgoing = outgoing.reshape(ep_count, local_experts, capacity, -1)
    gate_weight = expert_gate_up[:, 0]
    lift_weight = expert_gate_up[:, 1]
    incoming = lax.all_to_all(outgoing, "ep", split_axis=0, concat_axis=0, tiled=True)
    gate_value = jnp.einsum(
        "pecd,edf->pecf", incoming, gate_weight, preferred_element_type=jnp.float32
    )
    lift_value = jnp.einsum(
        "pecd,edf->pecf", incoming, lift_weight, preferred_element_type=jnp.float32
    )
    hidden_rows = (jax.nn.silu(gate_value) * lift_value).astype(jnp.bfloat16)
    result = jnp.einsum(
        "pecf,efd->pecd", hidden_rows, expert_down, preferred_element_type=jnp.float32
    )
    feature_share = result.shape[-1] // req_count
    sending = result.astype(jnp.bfloat16).reshape(
        ep_count, local_experts, capacity, req_count, feature_share
    )
    sending = jnp.transpose(sending, (3, 0, 1, 2, 4)).reshape(
        req_count * ep_count, local_experts, capacity, feature_share
    )
    returned = lax.all_to_all(sending, ("req", "ep"), 0, 0, tiled=True).reshape(
        req_count * slot_count, feature_share
    )
    combine = jnp.sum(
        jnp.where(
            placement[:, :, None] == slot_index[None, None, :], gates[:, :, None], 0.0
        ),
        axis=1,
    )
    combine = jnp.tile(combine, (1, req_count))
    combine_high = combine.astype(jnp.bfloat16)
    combine_low = (combine - combine_high.astype(jnp.float32)).astype(jnp.bfloat16)
    routed = jnp.dot(combine_high, returned, preferred_element_type=jnp.float32) + jnp.dot(
        combine_low, returned, preferred_element_type=jnp.float32
    )
    shared_cols = lax.psum_scatter(
        shared_part.astype(jnp.bfloat16), "req", scatter_dimension=1, tiled=True
    )
    layer_out = (
        resid_cols.astype(jnp.float32) + shared_cols.astype(jnp.float32) + routed
    ).astype(jnp.bfloat16)
    starts = cache_len // page_size
    page_now = starts + jnp.mod(req_index - starts, req_count)
    slot_now = jnp.take_along_axis(page_table, page_now[:, None], axis=1)[:, 0]
    old_page = cache_pool[slot_now]
    offsets = (
        page_now[:, None] * page_size
        + jnp.arange(page_size, dtype=jnp.int32)[None, :]
        - cache_len[:, None]
    ).astype(jnp.float32)
    accepted = jnp.take_along_axis(ancestry, accept_leaf[:, None, None], axis=1)[:, 0, :]
    select = accepted[:, None, :] * (depths[:, None, :] == offsets[:, :, None]).astype(jnp.float32)
    written = jnp.einsum(
        "rod,rdk->rok", select.astype(jnp.bfloat16), own_latent, preferred_element_type=jnp.float32
    )
    touched = jnp.sum(select, axis=2) > 0.5
    fresh = jnp.where(touched[..., None], written, old_page.astype(jnp.float32)).astype(
        jnp.bfloat16
    )
    return (layer_out, fresh[:, None])


def solution(mesh):
    in_specs = (
        P("ep", None, None),
        P("ep", None),
        P("ep", "req"),
        P(("req", "ep"), None, None),
        P("ep", None),
        P("ep"),
        P("ep", None),
        P("ep"),
        P(),
        P(),
        P(None, "req"),
        P(),
        P(),
        P("ep", None),
        P("ep", None, None, "req"),
        P("ep", "req", None),
        P(None, None, "req"),
        P("req", None),
    )
    out_specs = (P("ep", "req"), P("ep", "req", None, None))
    return jax.shard_map(
        per_device, mesh=mesh, in_specs=in_specs, out_specs=out_specs, check_vma=False
    )
```

```python
import functools
import math

import jax
import jax.numpy as jnp
from jax import lax
from jax.experimental import pallas as pl
from jax.experimental.pallas import tpu as pltpu
from jax.sharding import PartitionSpec as P

NEGATIVE = -1e30


def ancestors(parents):
    draft_count = parents.shape[-1]
    draft_index = jnp.arange(draft_count, dtype=jnp.int32)
    ancestry = (parents[:, :, None] == draft_index[None, None, :]).astype(jnp.float32)
    ancestry = ancestry + jnp.eye(draft_count, dtype=jnp.float32)[None]
    for doubling in range(max(1, (draft_count - 1).bit_length())):
        ancestry = jnp.minimum(
            jnp.einsum("rij,rjk->rik", ancestry, ancestry, precision=lax.Precision.HIGHEST), 1.0
        )
    return ancestry


def split_exact(values):
    pieces = []
    rest = values
    for _ in range(3):
        piece = lax.reduce_precision(rest, exponent_bits=8, mantissa_bits=7)
        pieces.append(piece.astype(jnp.bfloat16))
        rest = rest - piece
    return pieces


def attention_kernel(
    slots_ref, limits_ref, q_ref, rope_ref, page_ref, draft_ref, tree_ref, mixed_ref, stats_ref,
    keys,
    *, page_size, latent_width, score_scale, row_block
):
    request = pl.program_id(0)
    page = pl.program_id(1)
    page_total = pl.num_programs(1)
    keys[pl.ds(pl.multiple_of(page * page_size, page_size), page_size), :] = page_ref[0]

    @pl.when(page == page_total - 1)
    def _():
        key_rows = keys.shape[0]
        column = lax.broadcasted_iota(jnp.int32, (1, key_rows), 1)
        limit = jnp.zeros((1, key_rows), jnp.int32)
        for index in range(key_rows // page_size):
            limit = jnp.where(column // page_size == index, limits_ref[request, index], limit)
        cache_ok = (column % page_size) < limit
        lane = lax.broadcasted_iota(jnp.int32, (row_block, stats_ref.shape[2]), 1)

        def body(block, carry):
            rows = pl.ds(pl.multiple_of(block * row_block, row_block), row_block)
            query = q_ref[0, rows, :]
            rope = rope_ref[0, rows, :]
            contract = (((1,), (1,)), ((), ()))

            def scores_of(key_ref):
                return (
                    lax.dot_general(
                        query, key_ref[:, :latent_width], contract,
                        preferred_element_type=jnp.float32,
                    )
                    + lax.dot_general(
                        rope, key_ref[:, latent_width:], contract,
                        preferred_element_type=jnp.float32,
                    )
                ) * score_scale

            score = scores_of(keys)
            score = jnp.where(cache_ok, score, NEGATIVE)
            draft_score = scores_of(draft_ref.at[0])
            tree_ok = tree_ref[0, rows, :] > 0.5
            draft_score = jnp.where(tree_ok, draft_score, NEGATIVE)
            top = jnp.maximum(
                jnp.max(score, axis=1, keepdims=True), jnp.max(draft_score, axis=1, keepdims=True)
            )
            weight = jnp.where(cache_ok, jnp.exp(score - top), 0.0)
            draft_weight = jnp.where(tree_ok, jnp.exp(draft_score - top), 0.0)
            total = jnp.sum(weight, axis=1, keepdims=True) + jnp.sum(
                draft_weight, axis=1, keepdims=True
            )
            mixed = jnp.dot(
                weight.astype(jnp.bfloat16),
                keys[:, :latent_width],
                preferred_element_type=jnp.float32,
            ) + jnp.dot(
                draft_weight.astype(jnp.bfloat16),
                draft_ref[0, :, :latent_width],
                preferred_element_type=jnp.float32,
            )
            mixed_ref[0, rows, :] = mixed
            stats_ref[0, rows, :] = jnp.where(lane == 0, top, jnp.where(lane == 1, total, 0.0))
            return carry

        lax.fori_loop(0, q_ref.shape[1] // row_block, body, 0)


def paged_attention(slots, limits, query_rows, rope_rows, cache_pool, draft_rows, tree_rows, score_scale):
    request_count, row_count, latent_width = query_rows.shape
    key_width = cache_pool.shape[2]
    rope_width = rope_rows.shape[2]
    local_pages = slots.shape[1]
    page_size = cache_pool.shape[1]
    draft_pad = draft_rows.shape[1]
    row_block = 128
    kernel = functools.partial(
        attention_kernel,
        page_size=page_size,
        latent_width=latent_width,
        score_scale=score_scale,
        row_block=row_block,
    )
    key_rows = local_pages * page_size
    flops = 2 * request_count * row_count * (key_rows + draft_pad) * (key_width + latent_width)
    cost = pl.CostEstimate(
        flops=flops,
        transcendentals=request_count * row_count * (key_rows + draft_pad),
        bytes_accessed=2 * request_count * (row_count + key_rows) * key_width
        + 4 * request_count * row_count * (latent_width + 128 + draft_pad),
    )
    grid_spec = pltpu.PrefetchScalarGridSpec(
        num_scalar_prefetch=2,
        grid=(request_count, local_pages),
        in_specs=[
            pl.BlockSpec((1, row_count, latent_width), lambda r, j, s, n: (r, 0, 0)),
            pl.BlockSpec((1, row_count, rope_width), lambda r, j, s, n: (r, 0, 0)),
            pl.BlockSpec((1, page_size, key_width), lambda r, j, s, n: (s[r, j], 0, 0)),
            pl.BlockSpec((1, draft_pad, key_width), lambda r, j, s, n: (r, 0, 0)),
            pl.BlockSpec((1, row_count, draft_pad), lambda r, j, s, n: (r, 0, 0)),
        ],
        out_specs=[
            pl.BlockSpec((1, row_count, latent_width), lambda r, j, s, n: (r, 0, 0)),
            pl.BlockSpec((1, row_count, 128), lambda r, j, s, n: (r, 0, 0)),
        ],
        scratch_shapes=[pltpu.VMEM((key_rows, key_width), jnp.bfloat16)],
    )
    return pl.pallas_call(
        kernel,
        grid_spec=grid_spec,
        out_shape=[
            jax.ShapeDtypeStruct((request_count, row_count, latent_width), jnp.float32),
            jax.ShapeDtypeStruct((request_count, row_count, 128), jnp.float32),
        ],
        compiler_params=pltpu.CompilerParams(
            dimension_semantics=("arbitrary", "arbitrary"), vmem_limit_bytes=48 * 1024 * 1024
        ),
        cost_estimate=cost,
    )(slots, limits, query_rows, rope_rows, cache_pool, draft_rows, tree_rows)


def per_device(
    queries,
    draft_latent,
    hidden_in,
    cache_pool,
    page_table,
    cache_len,
    parents,
    accept_leaf,
    absorb_key,
    absorb_value,
    out_proj,
    norm_gain,
    router,
    expert_ids,
    expert_gate_up,
    expert_down,
    shared_gate_up,
    shared_down,
):
    highest = lax.Precision.HIGHEST
    req_count = lax.axis_size("req")
    req_index = lax.axis_index("req")
    ep_count = lax.axis_size("ep")
    request_count, draft_count = parents.shape
    token_count = request_count * draft_count
    head_count = queries.shape[1]
    nope_width = absorb_key.shape[1]
    latent_width = absorb_key.shape[2]
    page_size = cache_pool.shape[1]
    key_width = cache_pool.shape[2]
    page_count = page_table.shape[1]
    score_scale = 1.0 / math.sqrt(queries.shape[2])
    ancestry = ancestors(parents)
    depths = jnp.sum(ancestry, axis=2) - 1.0
    local_pages = page_count // req_count
    page_cols = req_index + req_count * jnp.arange(local_pages, dtype=jnp.int32)
    slot_rows = jnp.take(page_table, page_cols, axis=1)
    pool_slots = cache_pool.shape[0]
    slot_rows = jnp.clip(slot_rows, 0, pool_slots - 1).astype(jnp.int32)
    limits = jnp.clip(
        cache_len[:, None] - page_cols[None, :] * page_size, 0, page_size
    ).astype(jnp.int32)
    draft_share = draft_count // req_count
    draft_cols = req_index * draft_share + jnp.arange(draft_share, dtype=jnp.int32)
    own_latent = draft_latent.reshape(request_count, draft_count, key_width)
    draft_keys = jnp.take(own_latent, draft_cols, axis=1)
    draft_pad = 128
    draft_rows = jnp.pad(draft_keys, ((0, 0), (0, draft_pad - draft_share), (0, 0)))
    tree_ok = (jnp.take(ancestry, draft_cols, axis=2) > 0.5).astype(jnp.float32)
    tree_rows = jnp.broadcast_to(
        tree_ok[:, :, None, :], (request_count, draft_count, head_count, draft_share)
    ).reshape(request_count, draft_count * head_count, draft_share)
    tree_rows = jnp.pad(tree_rows, ((0, 0), (0, 0), (0, draft_pad - draft_share)))
    absorbed = jnp.einsum(
        "thd,hdl->thl", queries[:, :, :nope_width], absorb_key, preferred_element_type=jnp.float32
    ).astype(jnp.bfloat16)
    query_rows = absorbed.reshape(request_count, draft_count * head_count, latent_width)
    rope_rows = queries[:, :, nope_width:].reshape(request_count, draft_count * head_count, -1)
    mixed_rows, stats = paged_attention(
        slot_rows, limits, query_rows, rope_rows, cache_pool, draft_rows, tree_rows, score_scale
    )
    mixed_latent = mixed_rows.reshape(request_count, draft_count, head_count, latent_width)
    highest_score = stats[:, :, 0].reshape(request_count, draft_count, head_count)
    totals = stats[:, :, 1].reshape(request_count, draft_count, head_count)
    mixed_high = mixed_latent.astype(jnp.bfloat16)
    mixed_low = (mixed_latent - mixed_high.astype(jnp.float32)).astype(jnp.bfloat16)
    partial_head = jnp.einsum(
        "rthl,hlv->rthv", mixed_high, absorb_value, preferred_element_type=jnp.float32
    ) + jnp.einsum("rthl,hlv->rthv", mixed_low, absorb_value, preferred_element_type=jnp.float32)
    head_width = head_count * partial_head.shape[-1]
    low_parts = split_exact(jnp.concatenate([highest_score, totals], axis=-1))
    packed = jnp.concatenate(
        [partial_head.reshape(token_count, head_width).astype(jnp.bfloat16)]
        + [part.reshape(token_count, 2 * head_count) for part in low_parts],
        axis=1,
    )
    gathered = lax.all_gather(packed, "req").astype(jnp.float32)
    part_heads = gathered[:, :, :head_width]
    rejoined = sum(
        gathered[:, :, head_width + 2 * head_count * k : head_width + 2 * head_count * (k + 1)]
        for k in range(3)
    )
    part_max = rejoined[:, :, :head_count]
    part_sum = rejoined[:, :, head_count:]
    top = jnp.max(part_max, axis=0)
    factor = jnp.exp(part_max - top[None])
    merged_sum = jnp.sum(factor * part_sum, axis=0)
    value_width = head_width // head_count
    factor_wide = jnp.repeat(factor / merged_sum[None], value_width, axis=2)
    head_rows = jnp.sum(factor_wide * part_heads, axis=0).astype(jnp.bfloat16)
    attention = jnp.dot(head_rows, out_proj, preferred_element_type=jnp.float32)
    resid_cols = (hidden_in.astype(jnp.float32) + attention).astype(jnp.bfloat16)
    resid = lax.all_gather(resid_cols, "req", axis=1, tiled=True)
    resid_wide = resid.astype(jnp.float32)
    normed = resid_wide * lax.rsqrt(
        jnp.mean(resid_wide * resid_wide, axis=1, keepdims=True) + 1e-06
    )
    normed = (normed * norm_gain[None, :]).astype(jnp.bfloat16)
    logits = jnp.dot(normed, router, preferred_element_type=jnp.float32)
    lifted = jax.nn.sigmoid(jnp.take_along_axis(logits, expert_ids, axis=1))
    gates = lifted / jnp.sum(lifted, axis=1, keepdims=True)
    shared_gate = jnp.dot(normed, shared_gate_up[0], preferred_element_type=jnp.float32)
    shared_lift = jnp.dot(normed, shared_gate_up[1], preferred_element_type=jnp.float32)
    shared_hidden = (jax.nn.silu(shared_gate) * shared_lift).astype(jnp.bfloat16)
    shared_part = jnp.dot(shared_hidden, shared_down, preferred_element_type=jnp.float32)
    route_width = expert_ids.shape[1]
    local_experts = expert_gate_up.shape[0]
    expert_total = local_experts * ep_count
    capacity = (2 * token_count * route_width + expert_total - 1) // expert_total
    pair_experts = expert_ids.reshape(-1)
    marks = (pair_experts[:, None] == jnp.arange(expert_total, dtype=jnp.int32)[None, :]).astype(
        jnp.int32
    )
    slot_of = jnp.sum(jnp.cumsum(marks, axis=0) * marks, axis=1) - 1
    placement = (pair_experts * capacity + slot_of).reshape(token_count, route_width)
    slot_count = expert_total * capacity
    slot_index = jnp.arange(slot_count, dtype=jnp.int32)
    hits = placement[None, :, :] == slot_index[:, None, None]
    dispatch = jnp.any(hits, axis=2).astype(jnp.bfloat16)
    outgoing = jnp.dot(dispatch, normed, preferred_element_type=jnp.float32).astype(jnp.bfloat16)
    outgoing = outgoing.reshape(ep_count, local_experts, capacity, -1)
    gate_weight = expert_gate_up[:, 0]
    lift_weight = expert_gate_up[:, 1]
    incoming = lax.all_to_all(outgoing, "ep", split_axis=0, concat_axis=0, tiled=True)
    gate_value = jnp.einsum(
        "pecd,edf->pecf", incoming, gate_weight, preferred_element_type=jnp.float32
    )
    lift_value = jnp.einsum(
        "pecd,edf->pecf", incoming, lift_weight, preferred_element_type=jnp.float32
    )
    hidden_rows = (jax.nn.silu(gate_value) * lift_value).astype(jnp.bfloat16)
    feature_share = expert_down.shape[-1] // req_count
    sending = jnp.stack(
        [
            jnp.stack(
                [
                    jnp.dot(
                        hidden_rows[:, expert],
                        expert_down[expert, :, share * feature_share : (share + 1) * feature_share],
                        preferred_element_type=jnp.float32,
                    ).astype(jnp.bfloat16)
                    for expert in range(local_experts)
                ],
                axis=1,
            )
            for share in range(req_count)
        ],
        axis=0,
    ).reshape(req_count * ep_count, local_experts, capacity, feature_share)
    returned = lax.all_to_all(sending, ("req", "ep"), 0, 0, tiled=True).reshape(
        req_count * slot_count, feature_share
    )
    combine = jnp.sum(
        jnp.where(
            placement[:, :, None] == slot_index[None, None, :], gates[:, :, None], 0.0
        ),
        axis=1,
    )
    combine = jnp.tile(combine, (1, req_count))
    combine_high = combine.astype(jnp.bfloat16)
    combine_low = (combine - combine_high.astype(jnp.float32)).astype(jnp.bfloat16)
    routed = jnp.dot(combine_high, returned, preferred_element_type=jnp.float32) + jnp.dot(
        combine_low, returned, preferred_element_type=jnp.float32
    )
    shared_cols = lax.psum_scatter(
        shared_part.astype(jnp.bfloat16), "req", scatter_dimension=1, tiled=True
    )
    layer_out = (
        resid_cols.astype(jnp.float32) + shared_cols.astype(jnp.float32) + routed
    ).astype(jnp.bfloat16)
    starts = cache_len // page_size
    page_now = starts + jnp.mod(req_index - starts, req_count)
    slot_now = jnp.take_along_axis(page_table, page_now[:, None], axis=1)[:, 0]
    old_page = cache_pool[slot_now]
    offsets = (
        page_now[:, None] * page_size
        + jnp.arange(page_size, dtype=jnp.int32)[None, :]
        - cache_len[:, None]
    ).astype(jnp.float32)
    accepted = jnp.take_along_axis(ancestry, accept_leaf[:, None, None], axis=1)[:, 0, :]
    select = accepted[:, None, :] * (depths[:, None, :] == offsets[:, :, None]).astype(jnp.float32)
    written = jnp.einsum(
        "rod,rdk->rok", select.astype(jnp.bfloat16), own_latent, preferred_element_type=jnp.float32
    )
    touched = jnp.sum(select, axis=2) > 0.5
    fresh = jnp.where(touched[..., None], written, old_page.astype(jnp.float32)).astype(
        jnp.bfloat16
    )
    return (layer_out, fresh[:, None])


def solution(mesh):
    in_specs = (
        P("ep", None, None),
        P("ep", None),
        P("ep", "req"),
        P(("req", "ep"), None, None),
        P("ep", None),
        P("ep"),
        P("ep", None),
        P("ep"),
        P(),
        P(),
        P(None, "req"),
        P(),
        P(),
        P("ep", None),
        P("ep", None, None, "req"),
        P("ep", "req", None),
        P(None, None, "req"),
        P("req", None),
    )
    out_specs = (P("ep", "req"), P("ep", "req", None, None))
    return jax.shard_map(
        per_device, mesh=mesh, in_specs=in_specs, out_specs=out_specs, check_vma=False
    )
```

```python
import functools
import math

import jax
import jax.numpy as jnp
from jax import lax
from jax.experimental import pallas as pl
from jax.experimental.pallas import tpu as pltpu
from jax.sharding import PartitionSpec as P

NEGATIVE = -1e30


def ancestors(parents):
    draft_count = parents.shape[-1]
    draft_index = jnp.arange(draft_count, dtype=jnp.int32)
    ancestry = (parents[:, :, None] == draft_index[None, None, :]).astype(jnp.float32)
    ancestry = ancestry + jnp.eye(draft_count, dtype=jnp.float32)[None]
    for doubling in range(max(1, (draft_count - 1).bit_length())):
        ancestry = jnp.minimum(
            jnp.einsum("rij,rjk->rik", ancestry, ancestry, precision=lax.Precision.HIGHEST), 1.0
        )
    return ancestry


def split_exact(values):
    pieces = []
    rest = values
    for _ in range(3):
        piece = lax.reduce_precision(rest, exponent_bits=8, mantissa_bits=7)
        pieces.append(piece.astype(jnp.bfloat16))
        rest = rest - piece
    return pieces


def attention_kernel(
    slots_ref, limits_ref, q_ref, rope_ref, page_ref, draft_ref, tree_ref, mixed_ref, stats_ref,
    keys,
    *, page_size, latent_width, score_scale, row_block
):
    request = pl.program_id(0)
    page = pl.program_id(1)
    page_total = pl.num_programs(1)
    keys[pl.ds(pl.multiple_of(page * page_size, page_size), page_size), :] = page_ref[0]

    @pl.when(page == page_total - 1)
    def _():
        key_rows = keys.shape[0]
        column = lax.broadcasted_iota(jnp.int32, (1, key_rows), 1)
        limit = jnp.zeros((1, key_rows), jnp.int32)
        for index in range(key_rows // page_size):
            limit = jnp.where(column // page_size == index, limits_ref[request, index], limit)
        cache_ok = (column % page_size) < limit
        lane = lax.broadcasted_iota(jnp.int32, (row_block, stats_ref.shape[2]), 1)

        def body(block, carry):
            rows = pl.ds(pl.multiple_of(block * row_block, row_block), row_block)
            query = q_ref[0, rows, :]
            rope = rope_ref[0, rows, :]
            contract = (((1,), (1,)), ((), ()))

            def scores_of(key_ref):
                return (
                    lax.dot_general(
                        query, key_ref[:, :latent_width], contract,
                        preferred_element_type=jnp.float32,
                    )
                    + lax.dot_general(
                        rope, key_ref[:, latent_width:], contract,
                        preferred_element_type=jnp.float32,
                    )
                ) * score_scale

            score = scores_of(keys)
            score = jnp.where(cache_ok, score, NEGATIVE)
            draft_score = scores_of(draft_ref.at[0])
            tree_ok = tree_ref[0, rows, :] > 0.5
            draft_score = jnp.where(tree_ok, draft_score, NEGATIVE)
            top = jnp.maximum(
                jnp.max(score, axis=1, keepdims=True), jnp.max(draft_score, axis=1, keepdims=True)
            )
            weight = jnp.where(cache_ok, jnp.exp(score - top), 0.0)
            draft_weight = jnp.where(tree_ok, jnp.exp(draft_score - top), 0.0)
            total = jnp.sum(weight, axis=1, keepdims=True) + jnp.sum(
                draft_weight, axis=1, keepdims=True
            )
            mixed = jnp.dot(
                weight.astype(jnp.bfloat16),
                keys[:, :latent_width],
                preferred_element_type=jnp.float32,
            ) + jnp.dot(
                draft_weight.astype(jnp.bfloat16),
                draft_ref[0, :, :latent_width],
                preferred_element_type=jnp.float32,
            )
            mixed_ref[0, rows, :] = mixed
            stats_ref[0, rows, :] = jnp.where(lane == 0, top, jnp.where(lane == 1, total, 0.0))
            return carry

        lax.fori_loop(0, q_ref.shape[1] // row_block, body, 0)


def paged_attention(slots, limits, query_rows, rope_rows, cache_pool, draft_rows, tree_rows, score_scale):
    request_count, row_count, latent_width = query_rows.shape
    key_width = cache_pool.shape[2]
    rope_width = rope_rows.shape[2]
    local_pages = slots.shape[1]
    page_size = cache_pool.shape[1]
    draft_pad = draft_rows.shape[1]
    row_block = 128
    kernel = functools.partial(
        attention_kernel,
        page_size=page_size,
        latent_width=latent_width,
        score_scale=score_scale,
        row_block=row_block,
    )
    key_rows = local_pages * page_size
    flops = 2 * request_count * row_count * (key_rows + draft_pad) * (key_width + latent_width)
    cost = pl.CostEstimate(
        flops=flops,
        transcendentals=request_count * row_count * (key_rows + draft_pad),
        bytes_accessed=2 * request_count * (row_count + key_rows) * key_width
        + 4 * request_count * row_count * (latent_width + 128 + draft_pad),
    )
    grid_spec = pltpu.PrefetchScalarGridSpec(
        num_scalar_prefetch=2,
        grid=(request_count, local_pages),
        in_specs=[
            pl.BlockSpec((1, row_count, latent_width), lambda r, j, s, n: (r, 0, 0)),
            pl.BlockSpec((1, row_count, rope_width), lambda r, j, s, n: (r, 0, 0)),
            pl.BlockSpec((1, page_size, key_width), lambda r, j, s, n: (s[r, j], 0, 0)),
            pl.BlockSpec((1, draft_pad, key_width), lambda r, j, s, n: (r, 0, 0)),
            pl.BlockSpec((1, row_count, draft_pad), lambda r, j, s, n: (r, 0, 0)),
        ],
        out_specs=[
            pl.BlockSpec((1, row_count, latent_width), lambda r, j, s, n: (r, 0, 0)),
            pl.BlockSpec((1, row_count, 128), lambda r, j, s, n: (r, 0, 0)),
        ],
        scratch_shapes=[pltpu.VMEM((key_rows, key_width), jnp.bfloat16)],
    )
    return pl.pallas_call(
        kernel,
        grid_spec=grid_spec,
        out_shape=[
            jax.ShapeDtypeStruct((request_count, row_count, latent_width), jnp.float32),
            jax.ShapeDtypeStruct((request_count, row_count, 128), jnp.float32),
        ],
        compiler_params=pltpu.CompilerParams(
            dimension_semantics=("arbitrary", "arbitrary"), vmem_limit_bytes=48 * 1024 * 1024
        ),
        cost_estimate=cost,
    )(slots, limits, query_rows, rope_rows, cache_pool, draft_rows, tree_rows)


def per_device(
    queries,
    draft_latent,
    hidden_in,
    cache_pool,
    page_table,
    cache_len,
    parents,
    accept_leaf,
    absorb_key,
    absorb_value,
    out_proj,
    norm_gain,
    router,
    expert_ids,
    expert_gate_up,
    expert_down,
    shared_gate_up,
    shared_down,
):
    highest = lax.Precision.HIGHEST
    req_count = lax.axis_size("req")
    req_index = lax.axis_index("req")
    ep_count = lax.axis_size("ep")
    request_count, draft_count = parents.shape
    token_count = request_count * draft_count
    head_count = queries.shape[1]
    nope_width = absorb_key.shape[1]
    latent_width = absorb_key.shape[2]
    page_size = cache_pool.shape[1]
    key_width = cache_pool.shape[2]
    page_count = page_table.shape[1]
    score_scale = 1.0 / math.sqrt(queries.shape[2])
    ancestry = ancestors(parents)
    depths = jnp.sum(ancestry, axis=2) - 1.0
    local_pages = page_count // req_count
    page_cols = req_index + req_count * jnp.arange(local_pages, dtype=jnp.int32)
    slot_rows = jnp.take(page_table, page_cols, axis=1)
    pool_slots = cache_pool.shape[0]
    slot_rows = jnp.clip(slot_rows, 0, pool_slots - 1).astype(jnp.int32)
    limits = jnp.clip(
        cache_len[:, None] - page_cols[None, :] * page_size, 0, page_size
    ).astype(jnp.int32)
    draft_share = draft_count // req_count
    draft_cols = req_index * draft_share + jnp.arange(draft_share, dtype=jnp.int32)
    own_latent = draft_latent.reshape(request_count, draft_count, key_width)
    draft_keys = jnp.take(own_latent, draft_cols, axis=1)
    draft_pad = 128
    draft_rows = jnp.pad(draft_keys, ((0, 0), (0, draft_pad - draft_share), (0, 0)))
    tree_ok = (jnp.take(ancestry, draft_cols, axis=2) > 0.5).astype(jnp.float32)
    tree_rows = jnp.broadcast_to(
        tree_ok[:, :, None, :], (request_count, draft_count, head_count, draft_share)
    ).reshape(request_count, draft_count * head_count, draft_share)
    tree_rows = jnp.pad(tree_rows, ((0, 0), (0, 0), (0, draft_pad - draft_share)))
    absorbed = jnp.einsum(
        "thd,hdl->thl", queries[:, :, :nope_width], absorb_key, preferred_element_type=jnp.float32
    ).astype(jnp.bfloat16)
    query_rows = absorbed.reshape(request_count, draft_count * head_count, latent_width)
    rope_rows = queries[:, :, nope_width:].reshape(request_count, draft_count * head_count, -1)
    mixed_rows, stats = paged_attention(
        slot_rows, limits, query_rows, rope_rows, cache_pool, draft_rows, tree_rows, score_scale
    )
    mixed_latent = mixed_rows.reshape(request_count, draft_count, head_count, latent_width)
    highest_score = stats[:, :, 0].reshape(request_count, draft_count, head_count)
    totals = stats[:, :, 1].reshape(request_count, draft_count, head_count)
    mixed_high = mixed_latent.astype(jnp.bfloat16)
    mixed_low = (mixed_latent - mixed_high.astype(jnp.float32)).astype(jnp.bfloat16)
    partial_head = jnp.einsum(
        "rthl,hlv->rthv", mixed_high, absorb_value, preferred_element_type=jnp.float32
    ) + jnp.einsum("rthl,hlv->rthv", mixed_low, absorb_value, preferred_element_type=jnp.float32)
    head_width = head_count * partial_head.shape[-1]
    low_parts = split_exact(jnp.concatenate([highest_score, totals], axis=-1))
    packed = jnp.concatenate(
        [partial_head.reshape(token_count, head_width).astype(jnp.bfloat16)]
        + [part.reshape(token_count, 2 * head_count) for part in low_parts],
        axis=1,
    )
    gathered = lax.all_gather(packed, "req").astype(jnp.float32)
    part_heads = gathered[:, :, :head_width]
    rejoined = sum(
        gathered[:, :, head_width + 2 * head_count * k : head_width + 2 * head_count * (k + 1)]
        for k in range(3)
    )
    part_max = rejoined[:, :, :head_count]
    part_sum = rejoined[:, :, head_count:]
    top = jnp.max(part_max, axis=0)
    factor = jnp.exp(part_max - top[None])
    merged_sum = jnp.sum(factor * part_sum, axis=0)
    value_width = head_width // head_count
    spread = (
        jnp.arange(head_width, dtype=jnp.int32)[None, :] // value_width
        == jnp.arange(head_count, dtype=jnp.int32)[:, None]
    ).astype(jnp.bfloat16)
    scale_rows = (factor / merged_sum[None]).reshape(req_count * token_count, head_count)
    scale_high = scale_rows.astype(jnp.bfloat16)
    scale_low = (scale_rows - scale_high.astype(jnp.float32)).astype(jnp.bfloat16)
    factor_wide = (
        jnp.dot(scale_high, spread, preferred_element_type=jnp.float32)
        + jnp.dot(scale_low, spread, preferred_element_type=jnp.float32)
    ).reshape(req_count, token_count, head_width)
    head_rows = jnp.sum(factor_wide * part_heads, axis=0).astype(jnp.bfloat16)
    attention = jnp.dot(head_rows, out_proj, preferred_element_type=jnp.float32)
    resid_cols = (hidden_in.astype(jnp.float32) + attention).astype(jnp.bfloat16)
    resid = lax.all_gather(resid_cols, "req", axis=1, tiled=True)
    resid_wide = resid.astype(jnp.float32)
    normed = resid_wide * lax.rsqrt(
        jnp.mean(resid_wide * resid_wide, axis=1, keepdims=True) + 1e-06
    )
    normed = (normed * norm_gain[None, :]).astype(jnp.bfloat16)
    logits = jnp.dot(normed, router, preferred_element_type=jnp.float32)
    lifted = jax.nn.sigmoid(jnp.take_along_axis(logits, expert_ids, axis=1))
    gates = lifted / jnp.sum(lifted, axis=1, keepdims=True)
    shared_gate = jnp.dot(normed, shared_gate_up[0], preferred_element_type=jnp.float32)
    shared_lift = jnp.dot(normed, shared_gate_up[1], preferred_element_type=jnp.float32)
    shared_hidden = (jax.nn.silu(shared_gate) * shared_lift).astype(jnp.bfloat16)
    shared_part = jnp.dot(shared_hidden, shared_down, preferred_element_type=jnp.float32)
    route_width = expert_ids.shape[1]
    local_experts = expert_gate_up.shape[0]
    expert_total = local_experts * ep_count
    capacity = (2 * token_count * route_width + expert_total - 1) // expert_total
    pair_experts = expert_ids.reshape(-1)
    marks = (pair_experts[:, None] == jnp.arange(expert_total, dtype=jnp.int32)[None, :]).astype(
        jnp.int32
    )
    slot_of = jnp.sum(jnp.cumsum(marks, axis=0) * marks, axis=1) - 1
    placement = (pair_experts * capacity + slot_of).reshape(token_count, route_width)
    slot_count = expert_total * capacity
    slot_index = jnp.arange(slot_count, dtype=jnp.int32)
    hits = placement[None, :, :] == slot_index[:, None, None]
    dispatch = jnp.any(hits, axis=2).astype(jnp.bfloat16)
    outgoing = jnp.dot(dispatch, normed, preferred_element_type=jnp.float32).astype(jnp.bfloat16)
    outgoing = outgoing.reshape(ep_count, local_experts, capacity, -1)
    gate_weight = expert_gate_up[:, 0]
    lift_weight = expert_gate_up[:, 1]
    incoming = lax.all_to_all(outgoing, "ep", split_axis=0, concat_axis=0, tiled=True)
    gate_value = jnp.einsum(
        "pecd,edf->pecf", incoming, gate_weight, preferred_element_type=jnp.float32
    )
    lift_value = jnp.einsum(
        "pecd,edf->pecf", incoming, lift_weight, preferred_element_type=jnp.float32
    )
    hidden_rows = (jax.nn.silu(gate_value) * lift_value).astype(jnp.bfloat16)
    feature_share = expert_down.shape[-1] // req_count
    sending = jnp.stack(
        [
            jnp.stack(
                [
                    jnp.dot(
                        hidden_rows[:, expert],
                        expert_down[expert, :, share * feature_share : (share + 1) * feature_share],
                        preferred_element_type=jnp.float32,
                    ).astype(jnp.bfloat16)
                    for expert in range(local_experts)
                ],
                axis=1,
            )
            for share in range(req_count)
        ],
        axis=0,
    ).reshape(req_count * ep_count, local_experts, capacity, feature_share)
    returned = lax.all_to_all(sending, ("req", "ep"), 0, 0, tiled=True).reshape(
        req_count * slot_count, feature_share
    )
    combine = jnp.sum(
        jnp.where(
            placement[:, :, None] == slot_index[None, None, :], gates[:, :, None], 0.0
        ),
        axis=1,
    )
    combine = jnp.tile(combine, (1, req_count))
    combine_high = combine.astype(jnp.bfloat16)
    combine_low = (combine - combine_high.astype(jnp.float32)).astype(jnp.bfloat16)
    routed = jnp.dot(combine_high, returned, preferred_element_type=jnp.float32) + jnp.dot(
        combine_low, returned, preferred_element_type=jnp.float32
    )
    shared_cols = lax.psum_scatter(
        shared_part.astype(jnp.bfloat16), "req", scatter_dimension=1, tiled=True
    )
    layer_out = (
        resid_cols.astype(jnp.float32) + shared_cols.astype(jnp.float32) + routed
    ).astype(jnp.bfloat16)
    starts = cache_len // page_size
    page_now = starts + jnp.mod(req_index - starts, req_count)
    slot_now = jnp.take_along_axis(page_table, page_now[:, None], axis=1)[:, 0]
    old_page = cache_pool[slot_now]
    offsets = (
        page_now[:, None] * page_size
        + jnp.arange(page_size, dtype=jnp.int32)[None, :]
        - cache_len[:, None]
    ).astype(jnp.float32)
    accepted = jnp.take_along_axis(ancestry, accept_leaf[:, None, None], axis=1)[:, 0, :]
    select = accepted[:, None, :] * (depths[:, None, :] == offsets[:, :, None]).astype(jnp.float32)
    written = jnp.einsum(
        "rod,rdk->rok", select.astype(jnp.bfloat16), own_latent, preferred_element_type=jnp.float32
    )
    touched = jnp.sum(select, axis=2) > 0.5
    fresh = jnp.where(touched[..., None], written, old_page.astype(jnp.float32)).astype(
        jnp.bfloat16
    )
    return (layer_out, fresh[:, None])


def solution(mesh):
    in_specs = (
        P("ep", None, None),
        P("ep", None),
        P("ep", "req"),
        P(("req", "ep"), None, None),
        P("ep", None),
        P("ep"),
        P("ep", None),
        P("ep"),
        P(),
        P(),
        P(None, "req"),
        P(),
        P(),
        P("ep", None),
        P("ep", None, None, "req"),
        P("ep", "req", None),
        P(None, None, "req"),
        P("req", None),
    )
    out_specs = (P("ep", "req"), P("ep", "req", None, None))
    return jax.shard_map(
        per_device, mesh=mesh, in_specs=in_specs, out_specs=out_specs, check_vma=False
    )
```

```python
import functools
import math

import jax
import jax.numpy as jnp
from jax import lax
from jax.experimental import pallas as pl
from jax.experimental.pallas import tpu as pltpu
from jax.sharding import PartitionSpec as P

NEGATIVE = -1e30


def ancestors(parents):
    draft_count = parents.shape[-1]
    draft_index = jnp.arange(draft_count, dtype=jnp.int32)
    ancestry = (parents[:, :, None] == draft_index[None, None, :]).astype(jnp.float32)
    ancestry = ancestry + jnp.eye(draft_count, dtype=jnp.float32)[None]
    for doubling in range(max(1, (draft_count - 1).bit_length())):
        ancestry = jnp.minimum(
            jnp.einsum("rij,rjk->rik", ancestry, ancestry, precision=lax.Precision.HIGHEST), 1.0
        )
    return ancestry


def split_exact(values):
    pieces = []
    rest = values
    for _ in range(3):
        piece = lax.reduce_precision(rest, exponent_bits=8, mantissa_bits=7)
        pieces.append(piece.astype(jnp.bfloat16))
        rest = rest - piece
    return pieces


def attention_kernel(
    slots_ref, limits_ref, q_ref, rope_ref, page_ref, draft_ref, tree_ref, mixed_ref, stats_ref,
    keys,
    *, page_size, latent_width, score_scale, row_block
):
    request = pl.program_id(0)
    page = pl.program_id(1)
    page_total = pl.num_programs(1)
    keys[pl.ds(pl.multiple_of(page * page_size, page_size), page_size), :] = page_ref[0]

    @pl.when(page == page_total - 1)
    def _():
        key_rows = keys.shape[0]
        column = lax.broadcasted_iota(jnp.int32, (1, key_rows), 1)
        limit = jnp.zeros((1, key_rows), jnp.int32)
        for index in range(key_rows // page_size):
            limit = jnp.where(column // page_size == index, limits_ref[request, index], limit)
        cache_ok = (column % page_size) < limit
        lane = lax.broadcasted_iota(jnp.int32, (row_block, stats_ref.shape[2]), 1)

        def body(block, carry):
            rows = pl.ds(pl.multiple_of(block * row_block, row_block), row_block)
            query = q_ref[0, rows, :]
            rope = rope_ref[0, rows, :]
            contract = (((1,), (1,)), ((), ()))

            def scores_of(key_ref):
                return (
                    lax.dot_general(
                        query, key_ref[:, :latent_width], contract,
                        preferred_element_type=jnp.float32,
                    )
                    + lax.dot_general(
                        rope, key_ref[:, latent_width:], contract,
                        preferred_element_type=jnp.float32,
                    )
                ) * score_scale

            score = scores_of(keys)
            score = jnp.where(cache_ok, score, NEGATIVE)
            draft_score = scores_of(draft_ref.at[0])
            tree_ok = tree_ref[0, rows, :] > 0.5
            draft_score = jnp.where(tree_ok, draft_score, NEGATIVE)
            top = jnp.maximum(
                jnp.max(score, axis=1, keepdims=True), jnp.max(draft_score, axis=1, keepdims=True)
            )
            weight = jnp.where(cache_ok, jnp.exp(score - top), 0.0)
            draft_weight = jnp.where(tree_ok, jnp.exp(draft_score - top), 0.0)
            total = jnp.sum(weight, axis=1, keepdims=True) + jnp.sum(
                draft_weight, axis=1, keepdims=True
            )
            mixed = jnp.dot(
                weight.astype(jnp.bfloat16),
                keys[:, :latent_width],
                preferred_element_type=jnp.float32,
            ) + jnp.dot(
                draft_weight.astype(jnp.bfloat16),
                draft_ref[0, :, :latent_width],
                preferred_element_type=jnp.float32,
            )
            mixed_ref[0, rows, :] = mixed
            stats_ref[0, rows, :] = jnp.where(lane == 0, top, jnp.where(lane == 1, total, 0.0))
            return carry

        lax.fori_loop(0, q_ref.shape[1] // row_block, body, 0)


def paged_attention(slots, limits, query_rows, rope_rows, cache_pool, draft_rows, tree_rows, score_scale):
    request_count, row_count, latent_width = query_rows.shape
    key_width = cache_pool.shape[2]
    rope_width = rope_rows.shape[2]
    local_pages = slots.shape[1]
    page_size = cache_pool.shape[1]
    draft_pad = draft_rows.shape[1]
    row_block = 128
    kernel = functools.partial(
        attention_kernel,
        page_size=page_size,
        latent_width=latent_width,
        score_scale=score_scale,
        row_block=row_block,
    )
    key_rows = local_pages * page_size
    flops = 2 * request_count * row_count * (key_rows + draft_pad) * (key_width + latent_width)
    cost = pl.CostEstimate(
        flops=flops,
        transcendentals=request_count * row_count * (key_rows + draft_pad),
        bytes_accessed=2 * request_count * (row_count + key_rows) * key_width
        + 4 * request_count * row_count * (latent_width + 128 + draft_pad),
    )
    grid_spec = pltpu.PrefetchScalarGridSpec(
        num_scalar_prefetch=2,
        grid=(request_count, local_pages),
        in_specs=[
            pl.BlockSpec((1, row_count, latent_width), lambda r, j, s, n: (r, 0, 0)),
            pl.BlockSpec((1, row_count, rope_width), lambda r, j, s, n: (r, 0, 0)),
            pl.BlockSpec((1, page_size, key_width), lambda r, j, s, n: (s[r, j], 0, 0)),
            pl.BlockSpec((1, draft_pad, key_width), lambda r, j, s, n: (r, 0, 0)),
            pl.BlockSpec((1, row_count, draft_pad), lambda r, j, s, n: (r, 0, 0)),
        ],
        out_specs=[
            pl.BlockSpec((1, row_count, latent_width), lambda r, j, s, n: (r, 0, 0)),
            pl.BlockSpec((1, row_count, 128), lambda r, j, s, n: (r, 0, 0)),
        ],
        scratch_shapes=[pltpu.VMEM((key_rows, key_width), jnp.bfloat16)],
    )
    return pl.pallas_call(
        kernel,
        grid_spec=grid_spec,
        out_shape=[
            jax.ShapeDtypeStruct((request_count, row_count, latent_width), jnp.float32),
            jax.ShapeDtypeStruct((request_count, row_count, 128), jnp.float32),
        ],
        compiler_params=pltpu.CompilerParams(
            dimension_semantics=("arbitrary", "arbitrary"), vmem_limit_bytes=48 * 1024 * 1024
        ),
        cost_estimate=cost,
    )(slots, limits, query_rows, rope_rows, cache_pool, draft_rows, tree_rows)


def per_device(
    queries,
    draft_latent,
    hidden_in,
    cache_pool,
    page_table,
    cache_len,
    parents,
    accept_leaf,
    absorb_key,
    absorb_value,
    out_proj,
    norm_gain,
    router,
    expert_ids,
    expert_gate_up,
    expert_down,
    shared_gate_up,
    shared_down,
):
    highest = lax.Precision.HIGHEST
    req_count = lax.axis_size("req")
    req_index = lax.axis_index("req")
    ep_count = lax.axis_size("ep")
    request_count, draft_count = parents.shape
    token_count = request_count * draft_count
    head_count = queries.shape[1]
    nope_width = absorb_key.shape[1]
    latent_width = absorb_key.shape[2]
    page_size = cache_pool.shape[1]
    key_width = cache_pool.shape[2]
    page_count = page_table.shape[1]
    score_scale = 1.0 / math.sqrt(queries.shape[2])
    ancestry = ancestors(parents)
    depths = jnp.sum(ancestry, axis=2) - 1.0
    local_pages = page_count // req_count
    page_cols = req_index + req_count * jnp.arange(local_pages, dtype=jnp.int32)
    slot_rows = jnp.take(page_table, page_cols, axis=1)
    pool_slots = cache_pool.shape[0]
    slot_rows = jnp.clip(slot_rows, 0, pool_slots - 1).astype(jnp.int32)
    limits = jnp.clip(
        cache_len[:, None] - page_cols[None, :] * page_size, 0, page_size
    ).astype(jnp.int32)
    draft_share = draft_count // req_count
    draft_cols = req_index * draft_share + jnp.arange(draft_share, dtype=jnp.int32)
    own_latent = draft_latent.reshape(request_count, draft_count, key_width)
    draft_keys = jnp.take(own_latent, draft_cols, axis=1)
    draft_pad = 128
    draft_rows = jnp.pad(draft_keys, ((0, 0), (0, draft_pad - draft_share), (0, 0)))
    tree_ok = (jnp.take(ancestry, draft_cols, axis=2) > 0.5).astype(jnp.float32)
    tree_rows = jnp.broadcast_to(
        tree_ok[:, :, None, :], (request_count, draft_count, head_count, draft_share)
    ).reshape(request_count, draft_count * head_count, draft_share)
    tree_rows = jnp.pad(tree_rows, ((0, 0), (0, 0), (0, draft_pad - draft_share)))
    absorbed = jnp.einsum(
        "thd,hdl->thl", queries[:, :, :nope_width], absorb_key, preferred_element_type=jnp.float32
    ).astype(jnp.bfloat16)
    query_rows = absorbed.reshape(request_count, draft_count * head_count, latent_width)
    rope_rows = queries[:, :, nope_width:].reshape(request_count, draft_count * head_count, -1)
    value_width = absorb_value.shape[2]
    head_width = head_count * value_width
    spread = (
        jnp.arange(head_width, dtype=jnp.int32)[None, :] // value_width
        == jnp.arange(head_count, dtype=jnp.int32)[:, None]
    ).astype(jnp.bfloat16)

    def request_heads(request):
        pick = slice(request, request + 1)
        mixed_rows, stats = paged_attention(
            slot_rows[pick], limits[pick], query_rows[pick], rope_rows[pick], cache_pool,
            draft_rows[pick], tree_rows[pick], score_scale,
        )
        mixed_latent = mixed_rows.reshape(draft_count, head_count, latent_width)
        highest_score = stats[0, :, 0].reshape(draft_count, head_count)
        totals = stats[0, :, 1].reshape(draft_count, head_count)
        mixed_high = mixed_latent.astype(jnp.bfloat16)
        mixed_low = (mixed_latent - mixed_high.astype(jnp.float32)).astype(jnp.bfloat16)
        partial_head = jnp.einsum(
            "thl,hlv->thv", mixed_high, absorb_value, preferred_element_type=jnp.float32
        ) + jnp.einsum("thl,hlv->thv", mixed_low, absorb_value, preferred_element_type=jnp.float32)
        low_parts = split_exact(jnp.concatenate([highest_score, totals], axis=-1))
        packed = jnp.concatenate(
            [partial_head.reshape(draft_count, head_width).astype(jnp.bfloat16)] + low_parts,
            axis=1,
        )
        gathered = lax.all_gather(packed, "req").astype(jnp.float32)
        part_heads = gathered[:, :, :head_width]
        rejoined = sum(
            gathered[:, :, head_width + 2 * head_count * k : head_width + 2 * head_count * (k + 1)]
            for k in range(3)
        )
        part_max = rejoined[:, :, :head_count]
        part_sum = rejoined[:, :, head_count:]
        top = jnp.max(part_max, axis=0)
        factor = jnp.exp(part_max - top[None])
        merged_sum = jnp.sum(factor * part_sum, axis=0)
        scale_rows = (factor / merged_sum[None]).reshape(req_count * draft_count, head_count)
        scale_high = scale_rows.astype(jnp.bfloat16)
        scale_low = (scale_rows - scale_high.astype(jnp.float32)).astype(jnp.bfloat16)
        factor_wide = (
            jnp.dot(scale_high, spread, preferred_element_type=jnp.float32)
            + jnp.dot(scale_low, spread, preferred_element_type=jnp.float32)
        ).reshape(req_count, draft_count, head_width)
        return jnp.sum(factor_wide * part_heads, axis=0).astype(jnp.bfloat16)

    head_rows = jnp.concatenate(
        [request_heads(request) for request in range(request_count)], axis=0
    )
    attention = jnp.dot(head_rows, out_proj, preferred_element_type=jnp.float32)
    resid_cols = (hidden_in.astype(jnp.float32) + attention).astype(jnp.bfloat16)
    resid = lax.all_gather(resid_cols, "req", axis=1, tiled=True)
    resid_wide = resid.astype(jnp.float32)
    normed = resid_wide * lax.rsqrt(
        jnp.mean(resid_wide * resid_wide, axis=1, keepdims=True) + 1e-06
    )
    normed = (normed * norm_gain[None, :]).astype(jnp.bfloat16)
    logits = jnp.dot(normed, router, preferred_element_type=jnp.float32)
    lifted = jax.nn.sigmoid(jnp.take_along_axis(logits, expert_ids, axis=1))
    gates = lifted / jnp.sum(lifted, axis=1, keepdims=True)
    shared_gate = jnp.dot(normed, shared_gate_up[0], preferred_element_type=jnp.float32)
    shared_lift = jnp.dot(normed, shared_gate_up[1], preferred_element_type=jnp.float32)
    shared_hidden = (jax.nn.silu(shared_gate) * shared_lift).astype(jnp.bfloat16)
    shared_part = jnp.dot(shared_hidden, shared_down, preferred_element_type=jnp.float32)
    route_width = expert_ids.shape[1]
    local_experts = expert_gate_up.shape[0]
    expert_total = local_experts * ep_count
    capacity = (2 * token_count * route_width + expert_total - 1) // expert_total
    pair_experts = expert_ids.reshape(-1)
    marks = (pair_experts[:, None] == jnp.arange(expert_total, dtype=jnp.int32)[None, :]).astype(
        jnp.int32
    )
    slot_of = jnp.sum(jnp.cumsum(marks, axis=0) * marks, axis=1) - 1
    placement = (pair_experts * capacity + slot_of).reshape(token_count, route_width)
    slot_count = expert_total * capacity
    slot_index = jnp.arange(slot_count, dtype=jnp.int32)
    hits = placement[None, :, :] == slot_index[:, None, None]
    dispatch = jnp.any(hits, axis=2).astype(jnp.bfloat16)
    outgoing = jnp.dot(dispatch, normed, preferred_element_type=jnp.float32).astype(jnp.bfloat16)
    outgoing = outgoing.reshape(ep_count, local_experts, capacity, -1)
    gate_weight = expert_gate_up[:, 0]
    lift_weight = expert_gate_up[:, 1]
    incoming = lax.all_to_all(outgoing, "ep", split_axis=0, concat_axis=0, tiled=True)
    gate_value = jnp.einsum(
        "pecd,edf->pecf", incoming, gate_weight, preferred_element_type=jnp.float32
    )
    lift_value = jnp.einsum(
        "pecd,edf->pecf", incoming, lift_weight, preferred_element_type=jnp.float32
    )
    hidden_rows = (jax.nn.silu(gate_value) * lift_value).astype(jnp.bfloat16)
    feature_share = expert_down.shape[-1] // req_count
    sending = jnp.stack(
        [
            jnp.stack(
                [
                    jnp.dot(
                        hidden_rows[:, expert],
                        expert_down[expert, :, share * feature_share : (share + 1) * feature_share],
                        preferred_element_type=jnp.float32,
                    ).astype(jnp.bfloat16)
                    for expert in range(local_experts)
                ],
                axis=1,
            )
            for share in range(req_count)
        ],
        axis=0,
    ).reshape(req_count * ep_count, local_experts, capacity, feature_share)
    returned = lax.all_to_all(sending, ("req", "ep"), 0, 0, tiled=True).reshape(
        req_count * slot_count, feature_share
    )
    combine = jnp.sum(
        jnp.where(
            placement[:, :, None] == slot_index[None, None, :], gates[:, :, None], 0.0
        ),
        axis=1,
    )
    combine = jnp.tile(combine, (1, req_count))
    combine_high = combine.astype(jnp.bfloat16)
    combine_low = (combine - combine_high.astype(jnp.float32)).astype(jnp.bfloat16)
    routed = jnp.dot(combine_high, returned, preferred_element_type=jnp.float32) + jnp.dot(
        combine_low, returned, preferred_element_type=jnp.float32
    )
    shared_cols = lax.psum_scatter(
        shared_part.astype(jnp.bfloat16), "req", scatter_dimension=1, tiled=True
    )
    layer_out = (
        resid_cols.astype(jnp.float32) + shared_cols.astype(jnp.float32) + routed
    ).astype(jnp.bfloat16)
    starts = cache_len // page_size
    page_now = starts + jnp.mod(req_index - starts, req_count)
    slot_now = jnp.take_along_axis(page_table, page_now[:, None], axis=1)[:, 0]
    old_page = cache_pool[slot_now]
    offsets = (
        page_now[:, None] * page_size
        + jnp.arange(page_size, dtype=jnp.int32)[None, :]
        - cache_len[:, None]
    ).astype(jnp.float32)
    accepted = jnp.take_along_axis(ancestry, accept_leaf[:, None, None], axis=1)[:, 0, :]
    select = accepted[:, None, :] * (depths[:, None, :] == offsets[:, :, None]).astype(jnp.float32)
    written = jnp.einsum(
        "rod,rdk->rok", select.astype(jnp.bfloat16), own_latent, preferred_element_type=jnp.float32
    )
    touched = jnp.sum(select, axis=2) > 0.5
    fresh = jnp.where(touched[..., None], written, old_page.astype(jnp.float32)).astype(
        jnp.bfloat16
    )
    return (layer_out, fresh[:, None])


def solution(mesh):
    in_specs = (
        P("ep", None, None),
        P("ep", None),
        P("ep", "req"),
        P(("req", "ep"), None, None),
        P("ep", None),
        P("ep"),
        P("ep", None),
        P("ep"),
        P(),
        P(),
        P(None, "req"),
        P(),
        P(),
        P("ep", None),
        P("ep", None, None, "req"),
        P("ep", "req", None),
        P(None, None, "req"),
        P("req", None),
    )
    out_specs = (P("ep", "req"), P("ep", "req", None, None))
    return jax.shard_map(
        per_device, mesh=mesh, in_specs=in_specs, out_specs=out_specs, check_vma=False
    )
```

```python
import functools
import math

import jax
import jax.numpy as jnp
from jax import lax
from jax.experimental import pallas as pl
from jax.experimental.pallas import tpu as pltpu
from jax.sharding import PartitionSpec as P

NEGATIVE = -1e30


def ancestors(parents):
    draft_count = parents.shape[-1]
    draft_index = jnp.arange(draft_count, dtype=jnp.int32)
    ancestry = (parents[:, :, None] == draft_index[None, None, :]).astype(jnp.float32)
    ancestry = ancestry + jnp.eye(draft_count, dtype=jnp.float32)[None]
    for doubling in range(max(1, (draft_count - 1).bit_length())):
        ancestry = jnp.minimum(
            jnp.einsum("rij,rjk->rik", ancestry, ancestry, precision=lax.Precision.HIGHEST), 1.0
        )
    return ancestry


def split_exact(values):
    pieces = []
    rest = values
    for _ in range(3):
        piece = lax.reduce_precision(rest, exponent_bits=8, mantissa_bits=7)
        pieces.append(piece.astype(jnp.bfloat16))
        rest = rest - piece
    return pieces


def attention_kernel(
    slots_ref, limits_ref, q_ref, rope_ref, page_ref, draft_ref, tree_ref, mixed_ref, stats_ref,
    keys,
    *, page_size, latent_width, score_scale, row_block
):
    request = pl.program_id(0)
    page = pl.program_id(1)
    page_total = pl.num_programs(1)
    keys[pl.ds(pl.multiple_of(page * page_size, page_size), page_size), :] = page_ref[0]

    @pl.when(page == page_total - 1)
    def _():
        key_rows = keys.shape[0]
        column = lax.broadcasted_iota(jnp.int32, (1, key_rows), 1)
        limit = jnp.zeros((1, key_rows), jnp.int32)
        for index in range(key_rows // page_size):
            limit = jnp.where(column // page_size == index, limits_ref[request, index], limit)
        cache_ok = (column % page_size) < limit
        lane = lax.broadcasted_iota(jnp.int32, (row_block, stats_ref.shape[2]), 1)

        def body(block, carry):
            rows = pl.ds(pl.multiple_of(block * row_block, row_block), row_block)
            query = q_ref[0, rows, :]
            rope = rope_ref[0, rows, :]
            contract = (((1,), (1,)), ((), ()))

            def scores_of(key_ref):
                return (
                    lax.dot_general(
                        query, key_ref[:, :latent_width], contract,
                        preferred_element_type=jnp.float32,
                    )
                    + lax.dot_general(
                        rope, key_ref[:, latent_width:], contract,
                        preferred_element_type=jnp.float32,
                    )
                ) * score_scale

            score = scores_of(keys)
            score = jnp.where(cache_ok, score, NEGATIVE)
            draft_score = scores_of(draft_ref.at[0])
            tree_ok = tree_ref[0, rows, :] > 0.5
            draft_score = jnp.where(tree_ok, draft_score, NEGATIVE)
            top = jnp.maximum(
                jnp.max(score, axis=1, keepdims=True), jnp.max(draft_score, axis=1, keepdims=True)
            )
            weight = jnp.exp(score - top)
            draft_weight = jnp.exp(draft_score - top)
            total = jnp.sum(weight, axis=1, keepdims=True) + jnp.sum(
                draft_weight, axis=1, keepdims=True
            )
            mixed = jnp.dot(
                weight.astype(jnp.bfloat16),
                keys[:, :latent_width],
                preferred_element_type=jnp.float32,
            ) + jnp.dot(
                draft_weight.astype(jnp.bfloat16),
                draft_ref[0, :, :latent_width],
                preferred_element_type=jnp.float32,
            )
            mixed_ref[0, rows, :] = mixed
            stats_ref[0, rows, :] = jnp.where(lane == 0, top, jnp.where(lane == 1, total, 0.0))
            return carry

        lax.fori_loop(0, q_ref.shape[1] // row_block, body, 0)


def paged_attention(slots, limits, query_rows, rope_rows, cache_pool, draft_rows, tree_rows, score_scale):
    request_count, row_count, latent_width = query_rows.shape
    key_width = cache_pool.shape[2]
    rope_width = rope_rows.shape[2]
    local_pages = slots.shape[1]
    page_size = cache_pool.shape[1]
    draft_pad = draft_rows.shape[1]
    row_block = 128
    kernel = functools.partial(
        attention_kernel,
        page_size=page_size,
        latent_width=latent_width,
        score_scale=score_scale,
        row_block=row_block,
    )
    key_rows = local_pages * page_size
    flops = 2 * request_count * row_count * (key_rows + draft_pad) * (key_width + latent_width)
    cost = pl.CostEstimate(
        flops=flops,
        transcendentals=request_count * row_count * (key_rows + draft_pad),
        bytes_accessed=2 * request_count * (row_count + key_rows) * key_width
        + 4 * request_count * row_count * (latent_width + 128 + draft_pad),
    )
    grid_spec = pltpu.PrefetchScalarGridSpec(
        num_scalar_prefetch=2,
        grid=(request_count, local_pages),
        in_specs=[
            pl.BlockSpec((1, row_count, latent_width), lambda r, j, s, n: (r, 0, 0)),
            pl.BlockSpec((1, row_count, rope_width), lambda r, j, s, n: (r, 0, 0)),
            pl.BlockSpec((1, page_size, key_width), lambda r, j, s, n: (s[r, j], 0, 0)),
            pl.BlockSpec((1, draft_pad, key_width), lambda r, j, s, n: (r, 0, 0)),
            pl.BlockSpec((1, row_count, draft_pad), lambda r, j, s, n: (r, 0, 0)),
        ],
        out_specs=[
            pl.BlockSpec((1, row_count, latent_width), lambda r, j, s, n: (r, 0, 0)),
            pl.BlockSpec((1, row_count, 128), lambda r, j, s, n: (r, 0, 0)),
        ],
        scratch_shapes=[pltpu.VMEM((key_rows, key_width), jnp.bfloat16)],
    )
    return pl.pallas_call(
        kernel,
        grid_spec=grid_spec,
        out_shape=[
            jax.ShapeDtypeStruct((request_count, row_count, latent_width), jnp.float32),
            jax.ShapeDtypeStruct((request_count, row_count, 128), jnp.float32),
        ],
        compiler_params=pltpu.CompilerParams(
            dimension_semantics=("arbitrary", "arbitrary"), vmem_limit_bytes=48 * 1024 * 1024
        ),
        cost_estimate=cost,
    )(slots, limits, query_rows, rope_rows, cache_pool, draft_rows, tree_rows)


def per_device(
    queries,
    draft_latent,
    hidden_in,
    cache_pool,
    page_table,
    cache_len,
    parents,
    accept_leaf,
    absorb_key,
    absorb_value,
    out_proj,
    norm_gain,
    router,
    expert_ids,
    expert_gate_up,
    expert_down,
    shared_gate_up,
    shared_down,
):
    highest = lax.Precision.HIGHEST
    req_count = lax.axis_size("req")
    req_index = lax.axis_index("req")
    ep_count = lax.axis_size("ep")
    request_count, draft_count = parents.shape
    token_count = request_count * draft_count
    head_count = queries.shape[1]
    nope_width = absorb_key.shape[1]
    latent_width = absorb_key.shape[2]
    page_size = cache_pool.shape[1]
    key_width = cache_pool.shape[2]
    page_count = page_table.shape[1]
    score_scale = 1.0 / math.sqrt(queries.shape[2])
    ancestry = ancestors(parents)
    depths = jnp.sum(ancestry, axis=2) - 1.0
    local_pages = page_count // req_count
    page_cols = req_index + req_count * jnp.arange(local_pages, dtype=jnp.int32)
    slot_rows = jnp.take(page_table, page_cols, axis=1)
    pool_slots = cache_pool.shape[0]
    slot_rows = jnp.clip(slot_rows, 0, pool_slots - 1).astype(jnp.int32)
    limits = jnp.clip(
        cache_len[:, None] - page_cols[None, :] * page_size, 0, page_size
    ).astype(jnp.int32)
    draft_share = draft_count // req_count
    draft_cols = req_index * draft_share + jnp.arange(draft_share, dtype=jnp.int32)
    own_latent = draft_latent.reshape(request_count, draft_count, key_width)
    draft_keys = jnp.take(own_latent, draft_cols, axis=1)
    draft_pad = 128
    draft_rows = jnp.pad(draft_keys, ((0, 0), (0, draft_pad - draft_share), (0, 0)))
    tree_ok = (jnp.take(ancestry, draft_cols, axis=2) > 0.5).astype(jnp.float32)
    tree_rows = jnp.broadcast_to(
        tree_ok[:, :, None, :], (request_count, draft_count, head_count, draft_share)
    ).reshape(request_count, draft_count * head_count, draft_share)
    tree_rows = jnp.pad(tree_rows, ((0, 0), (0, 0), (0, draft_pad - draft_share)))
    absorbed = jnp.einsum(
        "thd,hdl->thl", queries[:, :, :nope_width], absorb_key, preferred_element_type=jnp.float32
    ).astype(jnp.bfloat16)
    query_rows = absorbed.reshape(request_count, draft_count * head_count, latent_width)
    rope_rows = queries[:, :, nope_width:].reshape(request_count, draft_count * head_count, -1)
    mixed_rows, stats = paged_attention(
        slot_rows, limits, query_rows, rope_rows, cache_pool, draft_rows, tree_rows, score_scale
    )
    mixed_latent = mixed_rows.reshape(request_count, draft_count, head_count, latent_width)
    highest_score = stats[:, :, 0].reshape(request_count, draft_count, head_count)
    totals = stats[:, :, 1].reshape(request_count, draft_count, head_count)
    mixed_high = mixed_latent.astype(jnp.bfloat16)
    mixed_low = (mixed_latent - mixed_high.astype(jnp.float32)).astype(jnp.bfloat16)
    partial_head = jnp.einsum(
        "rthl,hlv->rthv", mixed_high, absorb_value, preferred_element_type=jnp.float32
    ) + jnp.einsum("rthl,hlv->rthv", mixed_low, absorb_value, preferred_element_type=jnp.float32)
    head_width = head_count * partial_head.shape[-1]
    low_parts = split_exact(jnp.concatenate([highest_score, totals], axis=-1))
    packed = jnp.concatenate(
        [partial_head.reshape(token_count, head_width).astype(jnp.bfloat16)]
        + [part.reshape(token_count, 2 * head_count) for part in low_parts],
        axis=1,
    )
    copies = jnp.broadcast_to(packed[None], (req_count,) + packed.shape)
    gathered = lax.all_to_all(copies, "req", 0, 0, tiled=True).astype(jnp.float32)
    part_heads = gathered[:, :, :head_width]
    rejoined = sum(
        gathered[:, :, head_width + 2 * head_count * k : head_width + 2 * head_count * (k + 1)]
        for k in range(3)
    )
    part_max = rejoined[:, :, :head_count]
    part_sum = rejoined[:, :, head_count:]
    top = jnp.max(part_max, axis=0)
    factor = jnp.exp(part_max - top[None])
    merged_sum = jnp.sum(factor * part_sum, axis=0)
    value_width = head_width // head_count
    spread = (
        jnp.arange(head_width, dtype=jnp.int32)[None, :] // value_width
        == jnp.arange(head_count, dtype=jnp.int32)[:, None]
    ).astype(jnp.bfloat16)
    scale_rows = (factor / merged_sum[None]).reshape(req_count * token_count, head_count)
    scale_high = scale_rows.astype(jnp.bfloat16)
    scale_low = (scale_rows - scale_high.astype(jnp.float32)).astype(jnp.bfloat16)
    factor_wide = (
        jnp.dot(scale_high, spread, preferred_element_type=jnp.float32)
        + jnp.dot(scale_low, spread, preferred_element_type=jnp.float32)
    ).reshape(req_count, token_count, head_width)
    head_rows = jnp.sum(factor_wide * part_heads, axis=0).astype(jnp.bfloat16)
    attention = jnp.dot(head_rows, out_proj, preferred_element_type=jnp.float32)
    resid_cols = (hidden_in.astype(jnp.float32) + attention).astype(jnp.bfloat16)
    resid = lax.all_gather(resid_cols, "req", axis=1, tiled=True)
    resid_wide = resid.astype(jnp.float32)
    normed = resid_wide * lax.rsqrt(
        jnp.mean(resid_wide * resid_wide, axis=1, keepdims=True) + 1e-06
    )
    normed = (normed * norm_gain[None, :]).astype(jnp.bfloat16)
    logits = jnp.dot(normed, router, preferred_element_type=jnp.float32)
    lifted = jax.nn.sigmoid(jnp.take_along_axis(logits, expert_ids, axis=1))
    gates = lifted / jnp.sum(lifted, axis=1, keepdims=True)
    shared_gate = jnp.dot(normed, shared_gate_up[0], preferred_element_type=jnp.float32)
    shared_lift = jnp.dot(normed, shared_gate_up[1], preferred_element_type=jnp.float32)
    shared_hidden = (jax.nn.silu(shared_gate) * shared_lift).astype(jnp.bfloat16)
    shared_part = jnp.dot(shared_hidden, shared_down, preferred_element_type=jnp.float32)
    route_width = expert_ids.shape[1]
    local_experts = expert_gate_up.shape[0]
    expert_total = local_experts * ep_count
    capacity = (2 * token_count * route_width + expert_total - 1) // expert_total
    pair_experts = expert_ids.reshape(-1)
    marks = (pair_experts[:, None] == jnp.arange(expert_total, dtype=jnp.int32)[None, :]).astype(
        jnp.int32
    )
    slot_of = jnp.sum(jnp.cumsum(marks, axis=0) * marks, axis=1) - 1
    placement = (pair_experts * capacity + slot_of).reshape(token_count, route_width)
    slot_count = expert_total * capacity
    slot_index = jnp.arange(slot_count, dtype=jnp.int32)
    hits = placement[None, :, :] == slot_index[:, None, None]
    dispatch = jnp.any(hits, axis=2).astype(jnp.bfloat16)
    outgoing = jnp.dot(dispatch, normed, preferred_element_type=jnp.float32).astype(jnp.bfloat16)
    outgoing = outgoing.reshape(ep_count, local_experts, capacity, -1)
    gate_weight = expert_gate_up[:, 0]
    lift_weight = expert_gate_up[:, 1]
    incoming = lax.all_to_all(outgoing, "ep", split_axis=0, concat_axis=0, tiled=True)
    gate_value = jnp.einsum(
        "pecd,edf->pecf", incoming, gate_weight, preferred_element_type=jnp.float32
    )
    lift_value = jnp.einsum(
        "pecd,edf->pecf", incoming, lift_weight, preferred_element_type=jnp.float32
    )
    hidden_rows = (jax.nn.silu(gate_value) * lift_value).astype(jnp.bfloat16)
    feature_share = expert_down.shape[-1] // req_count
    sending = jnp.stack(
        [
            jnp.stack(
                [
                    jnp.dot(
                        hidden_rows[:, expert],
                        expert_down[expert, :, share * feature_share : (share + 1) * feature_share],
                        preferred_element_type=jnp.float32,
                    ).astype(jnp.bfloat16)
                    for expert in range(local_experts)
                ],
                axis=1,
            )
            for share in range(req_count)
        ],
        axis=0,
    ).reshape(req_count * ep_count, local_experts, capacity, feature_share)
    returned = lax.all_to_all(sending, ("req", "ep"), 0, 0, tiled=True).reshape(
        req_count * slot_count, feature_share
    )
    combine = jnp.sum(
        jnp.where(
            placement[:, :, None] == slot_index[None, None, :], gates[:, :, None], 0.0
        ),
        axis=1,
    )
    combine = jnp.tile(combine, (1, req_count))
    combine_high = combine.astype(jnp.bfloat16)
    combine_low = (combine - combine_high.astype(jnp.float32)).astype(jnp.bfloat16)
    routed = jnp.dot(combine_high, returned, preferred_element_type=jnp.float32) + jnp.dot(
        combine_low, returned, preferred_element_type=jnp.float32
    )
    shared_cols = lax.psum_scatter(
        shared_part.astype(jnp.bfloat16), "req", scatter_dimension=1, tiled=True
    )
    layer_out = (
        resid_cols.astype(jnp.float32) + shared_cols.astype(jnp.float32) + routed
    ).astype(jnp.bfloat16)
    starts = cache_len // page_size
    page_now = starts + jnp.mod(req_index - starts, req_count)
    slot_now = jnp.take_along_axis(page_table, page_now[:, None], axis=1)[:, 0]
    old_page = cache_pool[slot_now]
    offsets = (
        page_now[:, None] * page_size
        + jnp.arange(page_size, dtype=jnp.int32)[None, :]
        - cache_len[:, None]
    ).astype(jnp.float32)
    accepted = jnp.take_along_axis(ancestry, accept_leaf[:, None, None], axis=1)[:, 0, :]
    select = accepted[:, None, :] * (depths[:, None, :] == offsets[:, :, None]).astype(jnp.float32)
    written = jnp.einsum(
        "rod,rdk->rok", select.astype(jnp.bfloat16), own_latent, preferred_element_type=jnp.float32
    )
    touched = jnp.sum(select, axis=2) > 0.5
    fresh = jnp.where(touched[..., None], written, old_page.astype(jnp.float32)).astype(
        jnp.bfloat16
    )
    return (layer_out, fresh[:, None])


def solution(mesh):
    in_specs = (
        P("ep", None, None),
        P("ep", None),
        P("ep", "req"),
        P(("req", "ep"), None, None),
        P("ep", None),
        P("ep"),
        P("ep", None),
        P("ep"),
        P(),
        P(),
        P(None, "req"),
        P(),
        P(),
        P("ep", None),
        P("ep", None, None, "req"),
        P("ep", "req", None),
        P(None, None, "req"),
        P("req", None),
    )
    out_specs = (P("ep", "req"), P("ep", "req", None, None))
    return jax.shard_map(
        per_device, mesh=mesh, in_specs=in_specs, out_specs=out_specs, check_vma=False
    )
```

```python
import functools
import math

import jax
import jax.numpy as jnp
from jax import lax
from jax.experimental import pallas as pl
from jax.experimental.pallas import tpu as pltpu
from jax.sharding import PartitionSpec as P

NEGATIVE = -1e30


def ancestors(parents):
    draft_count = parents.shape[-1]
    draft_index = jnp.arange(draft_count, dtype=jnp.int32)
    ancestry = (parents[:, :, None] == draft_index[None, None, :]).astype(jnp.float32)
    ancestry = ancestry + jnp.eye(draft_count, dtype=jnp.float32)[None]
    for doubling in range(max(1, (draft_count - 1).bit_length())):
        ancestry = jnp.minimum(
            jnp.einsum("rij,rjk->rik", ancestry, ancestry, precision=lax.Precision.HIGHEST), 1.0
        )
    return ancestry


def split_exact(values):
    pieces = []
    rest = values
    for _ in range(3):
        piece = lax.reduce_precision(rest, exponent_bits=8, mantissa_bits=7)
        pieces.append(piece.astype(jnp.bfloat16))
        rest = rest - piece
    return pieces


def attention_kernel(
    slots_ref, limits_ref, q_ref, rope_ref, page_ref, draft_ref, tree_ref, mixed_ref, stats_ref,
    keys,
    *, page_size, latent_width, score_scale, row_block
):
    request = pl.program_id(0)
    page = pl.program_id(1)
    page_total = pl.num_programs(1)
    keys[page] = page_ref[0]

    @pl.when(page == page_total - 1)
    def _():
        local_pages = keys.shape[0]
        key_rows = local_pages * page_size
        column = lax.broadcasted_iota(jnp.int32, (1, key_rows), 1)
        limit = jnp.zeros((1, key_rows), jnp.int32)
        for index in range(local_pages):
            limit = jnp.where(column // page_size == index, limits_ref[request, index], limit)
        cache_ok = (column % page_size) < limit
        lane = lax.broadcasted_iota(jnp.int32, (row_block, stats_ref.shape[2]), 1)

        def body(block, carry):
            rows = pl.ds(pl.multiple_of(block * row_block, row_block), row_block)
            query = q_ref[0, rows, :]
            rope = rope_ref[0, rows, :]
            contract = (((1,), (1,)), ((), ()))
            score = jnp.concatenate(
                [
                    jnp.dot(query, keys[index, :latent_width, :], preferred_element_type=jnp.float32)
                    + jnp.dot(rope, keys[index, latent_width:, :], preferred_element_type=jnp.float32)
                    for index in range(local_pages)
                ],
                axis=1,
            ) * score_scale
            score = jnp.where(cache_ok, score, NEGATIVE)
            draft_score = (
                lax.dot_general(
                    query, draft_ref[0, :, :latent_width], contract,
                    preferred_element_type=jnp.float32,
                )
                + lax.dot_general(
                    rope, draft_ref[0, :, latent_width:], contract,
                    preferred_element_type=jnp.float32,
                )
            ) * score_scale
            tree_ok = tree_ref[0, rows, :] > 0.5
            draft_score = jnp.where(tree_ok, draft_score, NEGATIVE)
            top = jnp.maximum(
                jnp.max(score, axis=1, keepdims=True), jnp.max(draft_score, axis=1, keepdims=True)
            )
            weight = jnp.exp(score - top)
            draft_weight = jnp.exp(draft_score - top)
            total = jnp.sum(weight, axis=1, keepdims=True) + jnp.sum(
                draft_weight, axis=1, keepdims=True
            )
            weight_low = weight.astype(jnp.bfloat16)
            mixed = jnp.dot(
                draft_weight.astype(jnp.bfloat16),
                draft_ref[0, :, :latent_width],
                preferred_element_type=jnp.float32,
            )
            for index in range(local_pages):
                mixed = mixed + lax.dot_general(
                    weight_low[:, index * page_size : (index + 1) * page_size],
                    keys[index, :latent_width, :],
                    contract,
                    preferred_element_type=jnp.float32,
                )
            mixed_ref[0, rows, :] = mixed
            stats_ref[0, rows, :] = jnp.where(lane == 0, top, jnp.where(lane == 1, total, 0.0))
            return carry

        lax.fori_loop(0, q_ref.shape[1] // row_block, body, 0)


def paged_attention(slots, limits, query_rows, rope_rows, cache_pool, draft_rows, tree_rows, score_scale):
    request_count, row_count, latent_width = query_rows.shape
    key_width = cache_pool.shape[1]
    rope_width = rope_rows.shape[2]
    local_pages = slots.shape[1]
    page_size = cache_pool.shape[2]
    draft_pad = draft_rows.shape[1]
    row_block = 128
    kernel = functools.partial(
        attention_kernel,
        page_size=page_size,
        latent_width=latent_width,
        score_scale=score_scale,
        row_block=row_block,
    )
    key_rows = local_pages * page_size
    flops = 2 * request_count * row_count * (key_rows + draft_pad) * (key_width + latent_width)
    cost = pl.CostEstimate(
        flops=flops,
        transcendentals=request_count * row_count * (key_rows + draft_pad),
        bytes_accessed=2 * request_count * (row_count + key_rows) * key_width
        + 4 * request_count * row_count * (latent_width + 128 + draft_pad),
    )
    grid_spec = pltpu.PrefetchScalarGridSpec(
        num_scalar_prefetch=2,
        grid=(request_count, local_pages),
        in_specs=[
            pl.BlockSpec((1, row_count, latent_width), lambda r, j, s, n: (r, 0, 0)),
            pl.BlockSpec((1, row_count, rope_width), lambda r, j, s, n: (r, 0, 0)),
            pl.BlockSpec((1, key_width, page_size), lambda r, j, s, n: (s[r, j], 0, 0)),
            pl.BlockSpec((1, draft_pad, key_width), lambda r, j, s, n: (r, 0, 0)),
            pl.BlockSpec((1, row_count, draft_pad), lambda r, j, s, n: (r, 0, 0)),
        ],
        out_specs=[
            pl.BlockSpec((1, row_count, latent_width), lambda r, j, s, n: (r, 0, 0)),
            pl.BlockSpec((1, row_count, 128), lambda r, j, s, n: (r, 0, 0)),
        ],
        scratch_shapes=[pltpu.VMEM((local_pages, key_width, page_size), jnp.bfloat16)],
    )
    return pl.pallas_call(
        kernel,
        grid_spec=grid_spec,
        out_shape=[
            jax.ShapeDtypeStruct((request_count, row_count, latent_width), jnp.float32),
            jax.ShapeDtypeStruct((request_count, row_count, 128), jnp.float32),
        ],
        compiler_params=pltpu.CompilerParams(
            dimension_semantics=("arbitrary", "arbitrary"), vmem_limit_bytes=48 * 1024 * 1024
        ),
        cost_estimate=cost,
    )(slots, limits, query_rows, rope_rows, cache_pool, draft_rows, tree_rows)


def per_device(
    queries,
    draft_latent,
    hidden_in,
    cache_pool,
    page_table,
    cache_len,
    parents,
    accept_leaf,
    absorb_key,
    absorb_value,
    out_proj,
    norm_gain,
    router,
    expert_ids,
    expert_gate_up,
    expert_down,
    shared_gate_up,
    shared_down,
):
    highest = lax.Precision.HIGHEST
    req_count = lax.axis_size("req")
    req_index = lax.axis_index("req")
    ep_count = lax.axis_size("ep")
    request_count, draft_count = parents.shape
    token_count = request_count * draft_count
    head_count = queries.shape[1]
    nope_width = absorb_key.shape[1]
    latent_width = absorb_key.shape[2]
    page_size = cache_pool.shape[1]
    key_width = cache_pool.shape[2]
    page_count = page_table.shape[1]
    score_scale = 1.0 / math.sqrt(queries.shape[2])
    ancestry = ancestors(parents)
    depths = jnp.sum(ancestry, axis=2) - 1.0
    local_pages = page_count // req_count
    page_cols = req_index + req_count * jnp.arange(local_pages, dtype=jnp.int32)
    slot_rows = jnp.take(page_table, page_cols, axis=1)
    pool_slots = cache_pool.shape[0]
    slot_rows = jnp.clip(slot_rows, 0, pool_slots - 1).astype(jnp.int32)
    limits = jnp.clip(
        cache_len[:, None] - page_cols[None, :] * page_size, 0, page_size
    ).astype(jnp.int32)
    draft_share = draft_count // req_count
    draft_cols = req_index * draft_share + jnp.arange(draft_share, dtype=jnp.int32)
    own_latent = draft_latent.reshape(request_count, draft_count, key_width)
    draft_keys = jnp.take(own_latent, draft_cols, axis=1)
    draft_pad = 128
    draft_rows = jnp.pad(draft_keys, ((0, 0), (0, draft_pad - draft_share), (0, 0)))
    tree_ok = (jnp.take(ancestry, draft_cols, axis=2) > 0.5).astype(jnp.float32)
    tree_rows = jnp.broadcast_to(
        tree_ok[:, :, None, :], (request_count, draft_count, head_count, draft_share)
    ).reshape(request_count, draft_count * head_count, draft_share)
    tree_rows = jnp.pad(tree_rows, ((0, 0), (0, 0), (0, draft_pad - draft_share)))
    absorbed = jnp.einsum(
        "thd,hdl->thl", queries[:, :, :nope_width], absorb_key, preferred_element_type=jnp.float32
    ).astype(jnp.bfloat16)
    query_rows = absorbed.reshape(request_count, draft_count * head_count, latent_width)
    rope_rows = queries[:, :, nope_width:].reshape(request_count, draft_count * head_count, -1)
    mixed_rows, stats = paged_attention(
        slot_rows, limits, query_rows, rope_rows, jnp.swapaxes(cache_pool, 1, 2), draft_rows,
        tree_rows, score_scale,
    )
    mixed_latent = mixed_rows.reshape(request_count, draft_count, head_count, latent_width)
    highest_score = stats[:, :, 0].reshape(request_count, draft_count, head_count)
    totals = stats[:, :, 1].reshape(request_count, draft_count, head_count)
    mixed_high = mixed_latent.astype(jnp.bfloat16)
    mixed_low = (mixed_latent - mixed_high.astype(jnp.float32)).astype(jnp.bfloat16)
    partial_head = jnp.einsum(
        "rthl,hlv->rthv", mixed_high, absorb_value, preferred_element_type=jnp.float32
    ) + jnp.einsum("rthl,hlv->rthv", mixed_low, absorb_value, preferred_element_type=jnp.float32)
    head_width = head_count * partial_head.shape[-1]
    low_parts = split_exact(jnp.concatenate([highest_score, totals], axis=-1))
    packed = jnp.concatenate(
        [partial_head.reshape(token_count, head_width).astype(jnp.bfloat16)]
        + [part.reshape(token_count, 2 * head_count) for part in low_parts],
        axis=1,
    )
    gathered = lax.all_gather(packed, "req").astype(jnp.float32)
    part_heads = gathered[:, :, :head_width]
    rejoined = sum(
        gathered[:, :, head_width + 2 * head_count * k : head_width + 2 * head_count * (k + 1)]
        for k in range(3)
    )
    part_max = rejoined[:, :, :head_count]
    part_sum = rejoined[:, :, head_count:]
    top = jnp.max(part_max, axis=0)
    factor = jnp.exp(part_max - top[None])
    merged_sum = jnp.sum(factor * part_sum, axis=0)
    value_width = head_width // head_count
    spread = (
        jnp.arange(head_width, dtype=jnp.int32)[None, :] // value_width
        == jnp.arange(head_count, dtype=jnp.int32)[:, None]
    ).astype(jnp.bfloat16)
    scale_rows = (factor / merged_sum[None]).reshape(req_count * token_count, head_count)
    scale_high = scale_rows.astype(jnp.bfloat16)
    scale_low = (scale_rows - scale_high.astype(jnp.float32)).astype(jnp.bfloat16)
    factor_wide = (
        jnp.dot(scale_high, spread, preferred_element_type=jnp.float32)
        + jnp.dot(scale_low, spread, preferred_element_type=jnp.float32)
    ).reshape(req_count, token_count, head_width)
    head_rows = jnp.sum(factor_wide * part_heads, axis=0).astype(jnp.bfloat16)
    attention = jnp.dot(head_rows, out_proj, preferred_element_type=jnp.float32)
    resid_cols = (hidden_in.astype(jnp.float32) + attention).astype(jnp.bfloat16)
    resid = lax.all_gather(resid_cols, "req", axis=1, tiled=True)
    resid_wide = resid.astype(jnp.float32)
    normed = resid_wide * lax.rsqrt(
        jnp.mean(resid_wide * resid_wide, axis=1, keepdims=True) + 1e-06
    )
    normed = (normed * norm_gain[None, :]).astype(jnp.bfloat16)
    logits = jnp.dot(normed, router, preferred_element_type=jnp.float32)
    lifted = jax.nn.sigmoid(jnp.take_along_axis(logits, expert_ids, axis=1))
    gates = lifted / jnp.sum(lifted, axis=1, keepdims=True)
    shared_gate = jnp.dot(normed, shared_gate_up[0], preferred_element_type=jnp.float32)
    shared_lift = jnp.dot(normed, shared_gate_up[1], preferred_element_type=jnp.float32)
    shared_hidden = (jax.nn.silu(shared_gate) * shared_lift).astype(jnp.bfloat16)
    shared_part = jnp.dot(shared_hidden, shared_down, preferred_element_type=jnp.float32)
    route_width = expert_ids.shape[1]
    local_experts = expert_gate_up.shape[0]
    expert_total = local_experts * ep_count
    capacity = (2 * token_count * route_width + expert_total - 1) // expert_total
    pair_experts = expert_ids.reshape(-1)
    marks = (pair_experts[:, None] == jnp.arange(expert_total, dtype=jnp.int32)[None, :]).astype(
        jnp.int32
    )
    slot_of = jnp.sum(jnp.cumsum(marks, axis=0) * marks, axis=1) - 1
    placement = (pair_experts * capacity + slot_of).reshape(token_count, route_width)
    slot_count = expert_total * capacity
    slot_index = jnp.arange(slot_count, dtype=jnp.int32)
    hits = placement[None, :, :] == slot_index[:, None, None]
    dispatch = jnp.any(hits, axis=2).astype(jnp.bfloat16)
    outgoing = jnp.dot(dispatch, normed, preferred_element_type=jnp.float32).astype(jnp.bfloat16)
    outgoing = outgoing.reshape(ep_count, local_experts, capacity, -1)
    gate_weight = expert_gate_up[:, 0]
    lift_weight = expert_gate_up[:, 1]
    incoming = lax.all_to_all(outgoing, "ep", split_axis=0, concat_axis=0, tiled=True)
    gate_value = jnp.einsum(
        "pecd,edf->pecf", incoming, gate_weight, preferred_element_type=jnp.float32
    )
    lift_value = jnp.einsum(
        "pecd,edf->pecf", incoming, lift_weight, preferred_element_type=jnp.float32
    )
    hidden_rows = (jax.nn.silu(gate_value) * lift_value).astype(jnp.bfloat16)
    feature_share = expert_down.shape[-1] // req_count
    sending = jnp.stack(
        [
            jnp.stack(
                [
                    jnp.dot(
                        hidden_rows[:, expert],
                        expert_down[expert, :, share * feature_share : (share + 1) * feature_share],
                        preferred_element_type=jnp.float32,
                    ).astype(jnp.bfloat16)
                    for expert in range(local_experts)
                ],
                axis=1,
            )
            for share in range(req_count)
        ],
        axis=0,
    ).reshape(req_count * ep_count, local_experts, capacity, feature_share)
    returned = lax.all_to_all(sending, ("req", "ep"), 0, 0, tiled=True).reshape(
        req_count * slot_count, feature_share
    )
    combine = jnp.sum(
        jnp.where(
            placement[:, :, None] == slot_index[None, None, :], gates[:, :, None], 0.0
        ),
        axis=1,
    )
    combine = jnp.tile(combine, (1, req_count))
    combine_high = combine.astype(jnp.bfloat16)
    combine_low = (combine - combine_high.astype(jnp.float32)).astype(jnp.bfloat16)
    routed = jnp.dot(combine_high, returned, preferred_element_type=jnp.float32) + jnp.dot(
        combine_low, returned, preferred_element_type=jnp.float32
    )
    shared_cols = lax.psum_scatter(
        shared_part.astype(jnp.bfloat16), "req", scatter_dimension=1, tiled=True
    )
    layer_out = (
        resid_cols.astype(jnp.float32) + shared_cols.astype(jnp.float32) + routed
    ).astype(jnp.bfloat16)
    starts = cache_len // page_size
    page_now = starts + jnp.mod(req_index - starts, req_count)
    slot_now = jnp.take_along_axis(page_table, page_now[:, None], axis=1)[:, 0]
    old_page = cache_pool[slot_now]
    offsets = (
        page_now[:, None] * page_size
        + jnp.arange(page_size, dtype=jnp.int32)[None, :]
        - cache_len[:, None]
    ).astype(jnp.float32)
    accepted = jnp.take_along_axis(ancestry, accept_leaf[:, None, None], axis=1)[:, 0, :]
    select = accepted[:, None, :] * (depths[:, None, :] == offsets[:, :, None]).astype(jnp.float32)
    written = jnp.einsum(
        "rod,rdk->rok", select.astype(jnp.bfloat16), own_latent, preferred_element_type=jnp.float32
    )
    touched = jnp.sum(select, axis=2) > 0.5
    fresh = jnp.where(touched[..., None], written, old_page.astype(jnp.float32)).astype(
        jnp.bfloat16
    )
    return (layer_out, fresh[:, None])


def solution(mesh):
    in_specs = (
        P("ep", None, None),
        P("ep", None),
        P("ep", "req"),
        P(("req", "ep"), None, None),
        P("ep", None),
        P("ep"),
        P("ep", None),
        P("ep"),
        P(),
        P(),
        P(None, "req"),
        P(),
        P(),
        P("ep", None),
        P("ep", None, None, "req"),
        P("ep", "req", None),
        P(None, None, "req"),
        P("req", None),
    )
    out_specs = (P("ep", "req"), P("ep", "req", None, None))
    return jax.shard_map(
        per_device, mesh=mesh, in_specs=in_specs, out_specs=out_specs, check_vma=False
    )
```

```python
import functools
import math

import jax
import jax.numpy as jnp
from jax import lax
from jax.experimental import pallas as pl
from jax.experimental.pallas import tpu as pltpu
from jax.sharding import PartitionSpec as P

NEGATIVE = -1e30


def ancestors(parents):
    draft_count = parents.shape[-1]
    draft_index = jnp.arange(draft_count, dtype=jnp.int32)
    ancestry = (parents[:, :, None] == draft_index[None, None, :]).astype(jnp.float32)
    ancestry = ancestry + jnp.eye(draft_count, dtype=jnp.float32)[None]
    for doubling in range(max(1, (draft_count - 1).bit_length())):
        ancestry = jnp.minimum(
            jnp.einsum("rij,rjk->rik", ancestry, ancestry, precision=lax.Precision.HIGHEST), 1.0
        )
    return ancestry


def split_exact(values):
    pieces = []
    rest = values
    for _ in range(3):
        piece = lax.reduce_precision(rest, exponent_bits=8, mantissa_bits=7)
        pieces.append(piece.astype(jnp.bfloat16))
        rest = rest - piece
    return pieces


def attention_kernel(
    slots_ref, limits_ref, q_ref, rope_ref, page_ref, draft_ref, tree_ref, mixed_ref, stats_ref,
    keys,
    *, page_size, latent_width, score_scale, row_block
):
    request = pl.program_id(0)
    page = pl.program_id(1)
    page_total = pl.num_programs(1)
    keys[page] = page_ref[0]

    @pl.when(page == page_total - 1)
    def _():
        local_pages = keys.shape[0]
        key_rows = local_pages * page_size
        column = lax.broadcasted_iota(jnp.int32, (1, key_rows), 1)
        limit = jnp.zeros((1, key_rows), jnp.int32)
        for index in range(local_pages):
            limit = jnp.where(column // page_size == index, limits_ref[request, index], limit)
        cache_ok = (column % page_size) < limit
        lane = lax.broadcasted_iota(jnp.int32, (row_block, stats_ref.shape[2]), 1)

        def body(block, carry):
            rows = pl.ds(pl.multiple_of(block * row_block, row_block), row_block)
            query = q_ref[0, rows, :]
            rope = rope_ref[0, rows, :]
            contract = (((1,), (1,)), ((), ()))
            score = jnp.concatenate(
                [
                    jnp.dot(query, keys[index, :latent_width, :], preferred_element_type=jnp.float32)
                    + jnp.dot(rope, keys[index, latent_width:, :], preferred_element_type=jnp.float32)
                    for index in range(local_pages)
                ],
                axis=1,
            ) * score_scale
            score = jnp.where(cache_ok, score, NEGATIVE)
            draft_score = (
                lax.dot_general(
                    query, draft_ref[0, :, :latent_width], contract,
                    preferred_element_type=jnp.float32,
                )
                + lax.dot_general(
                    rope, draft_ref[0, :, latent_width:], contract,
                    preferred_element_type=jnp.float32,
                )
            ) * score_scale
            tree_ok = tree_ref[0, rows, :] > 0.5
            draft_score = jnp.where(tree_ok, draft_score, NEGATIVE)
            top = jnp.maximum(
                jnp.max(score, axis=1, keepdims=True), jnp.max(draft_score, axis=1, keepdims=True)
            )
            weight = jnp.exp(score - top)
            draft_weight = jnp.exp(draft_score - top)
            total = jnp.sum(weight, axis=1, keepdims=True) + jnp.sum(
                draft_weight, axis=1, keepdims=True
            )
            weight_low = weight.astype(jnp.bfloat16)
            mixed = jnp.dot(
                draft_weight.astype(jnp.bfloat16),
                draft_ref[0, :, :latent_width],
                preferred_element_type=jnp.float32,
            )
            for index in range(local_pages):
                mixed = mixed + lax.dot_general(
                    weight_low[:, index * page_size : (index + 1) * page_size],
                    keys[index, :latent_width, :],
                    contract,
                    preferred_element_type=jnp.float32,
                )
            mixed_ref[0, rows, :] = mixed
            stats_ref[0, rows, :] = jnp.where(lane == 0, top, jnp.where(lane == 1, total, 0.0))
            return carry

        lax.fori_loop(0, q_ref.shape[1] // row_block, body, 0)


def paged_attention(slots, limits, query_rows, rope_rows, cache_pool, draft_rows, tree_rows, score_scale):
    request_count, row_count, latent_width = query_rows.shape
    key_width = cache_pool.shape[1]
    rope_width = rope_rows.shape[2]
    local_pages = slots.shape[1]
    page_size = cache_pool.shape[2]
    draft_pad = draft_rows.shape[1]
    row_block = 128
    kernel = functools.partial(
        attention_kernel,
        page_size=page_size,
        latent_width=latent_width,
        score_scale=score_scale,
        row_block=row_block,
    )
    key_rows = local_pages * page_size
    flops = 2 * request_count * row_count * (key_rows + draft_pad) * (key_width + latent_width)
    cost = pl.CostEstimate(
        flops=flops,
        transcendentals=request_count * row_count * (key_rows + draft_pad),
        bytes_accessed=2 * request_count * (row_count + key_rows) * key_width
        + 4 * request_count * row_count * (latent_width + 128 + draft_pad),
    )
    grid_spec = pltpu.PrefetchScalarGridSpec(
        num_scalar_prefetch=2,
        grid=(request_count, local_pages),
        in_specs=[
            pl.BlockSpec((1, row_count, latent_width), lambda r, j, s, n: (r, 0, 0)),
            pl.BlockSpec((1, row_count, rope_width), lambda r, j, s, n: (r, 0, 0)),
            pl.BlockSpec((1, key_width, page_size), lambda r, j, s, n: (s[r, j], 0, 0)),
            pl.BlockSpec((1, draft_pad, key_width), lambda r, j, s, n: (r, 0, 0)),
            pl.BlockSpec((1, row_count, draft_pad), lambda r, j, s, n: (r, 0, 0)),
        ],
        out_specs=[
            pl.BlockSpec((1, row_count, latent_width), lambda r, j, s, n: (r, 0, 0)),
            pl.BlockSpec((1, row_count, 128), lambda r, j, s, n: (r, 0, 0)),
        ],
        scratch_shapes=[pltpu.VMEM((local_pages, key_width, page_size), jnp.bfloat16)],
    )
    return pl.pallas_call(
        kernel,
        grid_spec=grid_spec,
        out_shape=[
            jax.ShapeDtypeStruct((request_count, row_count, latent_width), jnp.float32),
            jax.ShapeDtypeStruct((request_count, row_count, 128), jnp.float32),
        ],
        compiler_params=pltpu.CompilerParams(
            dimension_semantics=("arbitrary", "arbitrary"), vmem_limit_bytes=48 * 1024 * 1024
        ),
        cost_estimate=cost,
    )(slots, limits, query_rows, rope_rows, cache_pool, draft_rows, tree_rows)


def per_device(
    queries,
    draft_latent,
    hidden_in,
    cache_pool,
    page_table,
    cache_len,
    parents,
    accept_leaf,
    absorb_key,
    absorb_value,
    out_proj,
    norm_gain,
    router,
    expert_ids,
    expert_gate_up,
    expert_down,
    shared_gate_up,
    shared_down,
):
    highest = lax.Precision.HIGHEST
    req_count = lax.axis_size("req")
    req_index = lax.axis_index("req")
    ep_count = lax.axis_size("ep")
    request_count, draft_count = parents.shape
    token_count = request_count * draft_count
    head_count = queries.shape[1]
    nope_width = absorb_key.shape[1]
    latent_width = absorb_key.shape[2]
    page_size = cache_pool.shape[1]
    key_width = cache_pool.shape[2]
    page_count = page_table.shape[1]
    score_scale = 1.0 / math.sqrt(queries.shape[2])
    ancestry = ancestors(parents)
    depths = jnp.sum(ancestry, axis=2) - 1.0
    local_pages = page_count // req_count
    page_cols = req_index + req_count * jnp.arange(local_pages, dtype=jnp.int32)
    slot_rows = jnp.take(page_table, page_cols, axis=1)
    pool_slots = cache_pool.shape[0]
    slot_rows = jnp.clip(slot_rows, 0, pool_slots - 1).astype(jnp.int32)
    limits = jnp.clip(
        cache_len[:, None] - page_cols[None, :] * page_size, 0, page_size
    ).astype(jnp.int32)
    draft_share = draft_count // req_count
    draft_cols = req_index * draft_share + jnp.arange(draft_share, dtype=jnp.int32)
    own_latent = draft_latent.reshape(request_count, draft_count, key_width)
    draft_keys = jnp.take(own_latent, draft_cols, axis=1)
    draft_pad = 128
    draft_rows = jnp.pad(draft_keys, ((0, 0), (0, draft_pad - draft_share), (0, 0)))
    tree_ok = (jnp.take(ancestry, draft_cols, axis=2) > 0.5).astype(jnp.float32)
    tree_rows = jnp.broadcast_to(
        tree_ok[:, :, None, :], (request_count, draft_count, head_count, draft_share)
    ).reshape(request_count, draft_count * head_count, draft_share)
    tree_rows = jnp.pad(tree_rows, ((0, 0), (0, 0), (0, draft_pad - draft_share)))
    absorbed = jnp.einsum(
        "thd,hdl->thl", queries[:, :, :nope_width], absorb_key, preferred_element_type=jnp.float32
    ).astype(jnp.bfloat16)
    query_rows = absorbed.reshape(request_count, draft_count * head_count, latent_width)
    rope_rows = queries[:, :, nope_width:].reshape(request_count, draft_count * head_count, -1)
    mixed_rows, stats = paged_attention(
        slot_rows, limits, query_rows, rope_rows, jnp.swapaxes(cache_pool, 1, 2), draft_rows,
        tree_rows, score_scale,
    )
    mixed_latent = mixed_rows.reshape(request_count, draft_count, head_count, latent_width)
    highest_score = stats[:, :, 0].reshape(request_count, draft_count, head_count)
    totals = stats[:, :, 1].reshape(request_count, draft_count, head_count)
    mixed_high = mixed_latent.astype(jnp.bfloat16)
    mixed_low = (mixed_latent - mixed_high.astype(jnp.float32)).astype(jnp.bfloat16)
    partial_head = jnp.einsum(
        "rthl,hlv->rthv", mixed_high, absorb_value, preferred_element_type=jnp.float32
    ) + jnp.einsum("rthl,hlv->rthv", mixed_low, absorb_value, preferred_element_type=jnp.float32)
    head_width = head_count * partial_head.shape[-1]
    low_parts = split_exact(jnp.concatenate([highest_score, totals], axis=-1))
    packed = jnp.concatenate(
        [partial_head.reshape(token_count, head_width).astype(jnp.bfloat16)]
        + [part.reshape(token_count, 2 * head_count) for part in low_parts],
        axis=1,
    )
    gathered = lax.all_gather(packed, "req").astype(jnp.float32)
    part_heads = gathered[:, :, :head_width]
    rejoined = sum(
        gathered[:, :, head_width + 2 * head_count * k : head_width + 2 * head_count * (k + 1)]
        for k in range(3)
    )
    part_max = rejoined[:, :, :head_count]
    part_sum = rejoined[:, :, head_count:]
    top = jnp.max(part_max, axis=0)
    factor = jnp.exp(part_max - top[None])
    merged_sum = jnp.sum(factor * part_sum, axis=0)
    value_width = head_width // head_count
    spread = (
        jnp.arange(head_width, dtype=jnp.int32)[None, :] // value_width
        == jnp.arange(head_count, dtype=jnp.int32)[:, None]
    ).astype(jnp.bfloat16)
    scale_rows = (factor / merged_sum[None]).reshape(req_count * token_count, head_count)
    scale_high = scale_rows.astype(jnp.bfloat16)
    scale_low = (scale_rows - scale_high.astype(jnp.float32)).astype(jnp.bfloat16)
    factor_wide = (
        jnp.dot(scale_high, spread, preferred_element_type=jnp.float32)
        + jnp.dot(scale_low, spread, preferred_element_type=jnp.float32)
    ).reshape(req_count, token_count, head_width)
    head_rows = jnp.sum(factor_wide * part_heads, axis=0).astype(jnp.bfloat16)
    attention = jnp.dot(head_rows, out_proj, preferred_element_type=jnp.float32)
    resid_cols = (hidden_in.astype(jnp.float32) + attention).astype(jnp.bfloat16)
    resid = lax.all_gather(resid_cols, "req", axis=1, tiled=True)
    resid_wide = resid.astype(jnp.float32)
    normed = resid_wide * lax.rsqrt(
        jnp.mean(resid_wide * resid_wide, axis=1, keepdims=True) + 1e-06
    )
    normed = (normed * norm_gain[None, :]).astype(jnp.bfloat16)
    logits = jnp.dot(normed, router, preferred_element_type=jnp.float32)
    lifted = jax.nn.sigmoid(jnp.take_along_axis(logits, expert_ids, axis=1))
    gates = lifted / jnp.sum(lifted, axis=1, keepdims=True)
    shared_gate = jnp.dot(normed, shared_gate_up[0], preferred_element_type=jnp.float32)
    shared_lift = jnp.dot(normed, shared_gate_up[1], preferred_element_type=jnp.float32)
    shared_hidden = (jax.nn.silu(shared_gate) * shared_lift).astype(jnp.bfloat16)
    shared_part = jnp.dot(shared_hidden, shared_down, preferred_element_type=jnp.float32)
    route_width = expert_ids.shape[1]
    local_experts = expert_gate_up.shape[0]
    expert_total = local_experts * ep_count
    capacity = (2 * token_count * route_width + expert_total - 1) // expert_total
    pair_experts = expert_ids.reshape(-1)
    marks = (pair_experts[:, None] == jnp.arange(expert_total, dtype=jnp.int32)[None, :]).astype(
        jnp.int32
    )
    slot_of = jnp.sum(jnp.cumsum(marks, axis=0) * marks, axis=1) - 1
    placement = (pair_experts * capacity + slot_of).reshape(token_count, route_width)
    slot_count = expert_total * capacity
    slot_index = jnp.arange(slot_count, dtype=jnp.int32)
    hits = placement[None, :, :] == slot_index[:, None, None]
    dispatch = jnp.any(hits, axis=2).astype(jnp.bfloat16)
    outgoing = jnp.dot(dispatch, normed, preferred_element_type=jnp.float32).astype(jnp.bfloat16)
    outgoing = outgoing.reshape(ep_count, local_experts, capacity, -1)
    gate_weight = expert_gate_up[:, 0]
    lift_weight = expert_gate_up[:, 1]
    incoming = lax.all_to_all(outgoing, "ep", split_axis=0, concat_axis=0, tiled=True)
    gate_value = jnp.einsum(
        "pecd,edf->pecf", incoming, gate_weight, preferred_element_type=jnp.float32
    )
    lift_value = jnp.einsum(
        "pecd,edf->pecf", incoming, lift_weight, preferred_element_type=jnp.float32
    )
    hidden_rows = (jax.nn.silu(gate_value) * lift_value).astype(jnp.bfloat16)
    feature_share = expert_down.shape[-1] // req_count
    sending = jnp.stack(
        [
            jnp.stack(
                [
                    jnp.dot(
                        hidden_rows[:, expert],
                        expert_down[expert, :, share * feature_share : (share + 1) * feature_share],
                        preferred_element_type=jnp.float32,
                    ).astype(jnp.bfloat16)
                    for expert in range(local_experts)
                ],
                axis=1,
            )
            for share in range(req_count)
        ],
        axis=0,
    ).reshape(req_count * ep_count, local_experts, capacity, feature_share)
    returned = lax.all_to_all(sending, ("req", "ep"), 0, 0, tiled=True).reshape(
        req_count * slot_count, feature_share
    )
    combine = jnp.sum(
        jnp.where(
            placement[:, :, None] == slot_index[None, None, :], gates[:, :, None], 0.0
        ),
        axis=1,
    )
    combine = jnp.tile(combine, (1, req_count))
    combine_high = combine.astype(jnp.bfloat16)
    combine_low = (combine - combine_high.astype(jnp.float32)).astype(jnp.bfloat16)
    both = jnp.dot(
        jnp.concatenate([combine_high, combine_low], axis=0),
        returned,
        preferred_element_type=jnp.float32,
    )
    routed = both[:token_count] + both[token_count:]
    shared_cols = lax.psum_scatter(
        shared_part.astype(jnp.bfloat16), "req", scatter_dimension=1, tiled=True
    )
    layer_out = (
        resid_cols.astype(jnp.float32) + shared_cols.astype(jnp.float32) + routed
    ).astype(jnp.bfloat16)
    starts = cache_len // page_size
    page_now = starts + jnp.mod(req_index - starts, req_count)
    slot_now = jnp.take_along_axis(page_table, page_now[:, None], axis=1)[:, 0]
    old_page = cache_pool[slot_now]
    offsets = (
        page_now[:, None] * page_size
        + jnp.arange(page_size, dtype=jnp.int32)[None, :]
        - cache_len[:, None]
    ).astype(jnp.float32)
    accepted = jnp.take_along_axis(ancestry, accept_leaf[:, None, None], axis=1)[:, 0, :]
    select = accepted[:, None, :] * (depths[:, None, :] == offsets[:, :, None]).astype(jnp.float32)
    written = jnp.einsum(
        "rod,rdk->rok", select.astype(jnp.bfloat16), own_latent, preferred_element_type=jnp.float32
    )
    touched = jnp.sum(select, axis=2) > 0.5
    fresh = jnp.where(touched[..., None], written, old_page.astype(jnp.float32)).astype(
        jnp.bfloat16
    )
    return (layer_out, fresh[:, None])


def solution(mesh):
    in_specs = (
        P("ep", None, None),
        P("ep", None),
        P("ep", "req"),
        P(("req", "ep"), None, None),
        P("ep", None),
        P("ep"),
        P("ep", None),
        P("ep"),
        P(),
        P(),
        P(None, "req"),
        P(),
        P(),
        P("ep", None),
        P("ep", None, None, "req"),
        P("ep", "req", None),
        P(None, None, "req"),
        P("req", None),
    )
    out_specs = (P("ep", "req"), P("ep", "req", None, None))
    return jax.shard_map(
        per_device, mesh=mesh, in_specs=in_specs, out_specs=out_specs, check_vma=False
    )
```

```python
import functools
import math

import jax
import jax.numpy as jnp
from jax import lax
from jax.experimental import pallas as pl
from jax.experimental.pallas import tpu as pltpu
from jax.sharding import PartitionSpec as P

NEGATIVE = -1e30


def ancestors(parents):
    draft_count = parents.shape[-1]
    draft_index = jnp.arange(draft_count, dtype=jnp.int32)
    ancestry = (parents[:, :, None] == draft_index[None, None, :]).astype(jnp.float32)
    ancestry = ancestry + jnp.eye(draft_count, dtype=jnp.float32)[None]
    for doubling in range(max(1, (draft_count - 1).bit_length())):
        ancestry = jnp.minimum(
            jnp.einsum("rij,rjk->rik", ancestry, ancestry, precision=lax.Precision.HIGHEST), 1.0
        )
    return ancestry


def split_exact(values):
    pieces = []
    rest = values
    for _ in range(3):
        piece = lax.reduce_precision(rest, exponent_bits=8, mantissa_bits=7)
        pieces.append(piece.astype(jnp.bfloat16))
        rest = rest - piece
    return pieces


def attention_kernel(
    slots_ref, limits_ref, q_ref, rope_ref, page_ref, draft_ref, tree_ref, mixed_ref, stats_ref,
    keys,
    *, page_size, latent_width, score_scale, row_block
):
    request = pl.program_id(0)
    page = pl.program_id(1)
    page_total = pl.num_programs(1)
    keys[page] = page_ref[0]

    @pl.when(page == page_total - 1)
    def _():
        local_pages = keys.shape[0]
        key_rows = local_pages * page_size
        column = lax.broadcasted_iota(jnp.int32, (1, key_rows), 1)
        limit = jnp.zeros((1, key_rows), jnp.int32)
        for index in range(local_pages):
            limit = jnp.where(column // page_size == index, limits_ref[request, index], limit)
        cache_ok = (column % page_size) < limit
        lane = lax.broadcasted_iota(jnp.int32, (row_block, stats_ref.shape[2]), 1)

        def body(block, carry):
            rows = pl.ds(pl.multiple_of(block * row_block, row_block), row_block)
            query = q_ref[0, rows, :]
            rope = rope_ref[0, rows, :]
            contract = (((1,), (1,)), ((), ()))
            score = jnp.concatenate(
                [
                    jnp.dot(query, keys[index, :latent_width, :], preferred_element_type=jnp.float32)
                    + jnp.dot(rope, keys[index, latent_width:, :], preferred_element_type=jnp.float32)
                    for index in range(local_pages)
                ],
                axis=1,
            ) * score_scale
            score = jnp.where(cache_ok, score, NEGATIVE)
            draft_score = (
                lax.dot_general(
                    query, draft_ref[0, :, :latent_width], contract,
                    preferred_element_type=jnp.float32,
                )
                + lax.dot_general(
                    rope, draft_ref[0, :, latent_width:], contract,
                    preferred_element_type=jnp.float32,
                )
            ) * score_scale
            tree_ok = tree_ref[0, rows, :] > 0.5
            draft_score = jnp.where(tree_ok, draft_score, NEGATIVE)
            top = jnp.maximum(
                jnp.max(score, axis=1, keepdims=True), jnp.max(draft_score, axis=1, keepdims=True)
            )
            weight = jnp.exp(score - top)
            draft_weight = jnp.exp(draft_score - top)
            total = jnp.sum(weight, axis=1, keepdims=True) + jnp.sum(
                draft_weight, axis=1, keepdims=True
            )
            weight_low = weight.astype(jnp.bfloat16)
            mixed = jnp.dot(
                draft_weight.astype(jnp.bfloat16),
                draft_ref[0, :, :latent_width],
                preferred_element_type=jnp.float32,
            )
            for index in range(local_pages):
                mixed = mixed + lax.dot_general(
                    weight_low[:, index * page_size : (index + 1) * page_size],
                    keys[index, :latent_width, :],
                    contract,
                    preferred_element_type=jnp.float32,
                )
            mixed_ref[0, rows, :] = mixed
            stats_ref[0, rows, :] = jnp.where(lane == 0, top, jnp.where(lane == 1, total, 0.0))
            return carry

        lax.fori_loop(0, q_ref.shape[1] // row_block, body, 0)


def paged_attention(slots, limits, query_rows, rope_rows, cache_pool, draft_rows, tree_rows, score_scale):
    request_count, row_count, latent_width = query_rows.shape
    key_width = cache_pool.shape[1]
    rope_width = rope_rows.shape[2]
    local_pages = slots.shape[1]
    page_size = cache_pool.shape[2]
    draft_pad = draft_rows.shape[1]
    row_block = 128
    kernel = functools.partial(
        attention_kernel,
        page_size=page_size,
        latent_width=latent_width,
        score_scale=score_scale,
        row_block=row_block,
    )
    key_rows = local_pages * page_size
    flops = 2 * request_count * row_count * (key_rows + draft_pad) * (key_width + latent_width)
    cost = pl.CostEstimate(
        flops=flops,
        transcendentals=request_count * row_count * (key_rows + draft_pad),
        bytes_accessed=2 * request_count * (row_count + key_rows) * key_width
        + 4 * request_count * row_count * (latent_width + 128 + draft_pad),
    )
    grid_spec = pltpu.PrefetchScalarGridSpec(
        num_scalar_prefetch=2,
        grid=(request_count, local_pages),
        in_specs=[
            pl.BlockSpec((1, row_count, latent_width), lambda r, j, s, n: (r, 0, 0)),
            pl.BlockSpec((1, row_count, rope_width), lambda r, j, s, n: (r, 0, 0)),
            pl.BlockSpec((1, key_width, page_size), lambda r, j, s, n: (s[r, j], 0, 0)),
            pl.BlockSpec((1, draft_pad, key_width), lambda r, j, s, n: (r, 0, 0)),
            pl.BlockSpec((1, row_count, draft_pad), lambda r, j, s, n: (r, 0, 0)),
        ],
        out_specs=[
            pl.BlockSpec((1, row_count, latent_width), lambda r, j, s, n: (r, 0, 0)),
            pl.BlockSpec((1, row_count, 128), lambda r, j, s, n: (r, 0, 0)),
        ],
        scratch_shapes=[pltpu.VMEM((local_pages, key_width, page_size), jnp.bfloat16)],
    )
    return pl.pallas_call(
        kernel,
        grid_spec=grid_spec,
        out_shape=[
            jax.ShapeDtypeStruct((request_count, row_count, latent_width), jnp.float32),
            jax.ShapeDtypeStruct((request_count, row_count, 128), jnp.float32),
        ],
        compiler_params=pltpu.CompilerParams(
            dimension_semantics=("arbitrary", "arbitrary"), vmem_limit_bytes=48 * 1024 * 1024
        ),
        cost_estimate=cost,
    )(slots, limits, query_rows, rope_rows, cache_pool, draft_rows, tree_rows)


def per_device(
    queries,
    draft_latent,
    hidden_in,
    cache_pool,
    page_table,
    cache_len,
    parents,
    accept_leaf,
    absorb_key,
    absorb_value,
    out_proj,
    norm_gain,
    router,
    expert_ids,
    expert_gate_up,
    expert_down,
    shared_gate_up,
    shared_down,
):
    highest = lax.Precision.HIGHEST
    req_count = lax.axis_size("req")
    req_index = lax.axis_index("req")
    ep_count = lax.axis_size("ep")
    request_count, draft_count = parents.shape
    token_count = request_count * draft_count
    head_count = queries.shape[1]
    nope_width = absorb_key.shape[1]
    latent_width = absorb_key.shape[2]
    page_size = cache_pool.shape[1]
    key_width = cache_pool.shape[2]
    page_count = page_table.shape[1]
    score_scale = 1.0 / math.sqrt(queries.shape[2])
    ancestry = ancestors(parents)
    depths = jnp.sum(ancestry, axis=2) - 1.0
    local_pages = page_count // req_count
    page_cols = req_index + req_count * jnp.arange(local_pages, dtype=jnp.int32)
    slot_rows = jnp.take(page_table, page_cols, axis=1)
    pool_slots = cache_pool.shape[0]
    slot_rows = jnp.clip(slot_rows, 0, pool_slots - 1).astype(jnp.int32)
    limits = jnp.clip(
        cache_len[:, None] - page_cols[None, :] * page_size, 0, page_size
    ).astype(jnp.int32)
    draft_share = draft_count // req_count
    draft_cols = req_index * draft_share + jnp.arange(draft_share, dtype=jnp.int32)
    own_latent = draft_latent.reshape(request_count, draft_count, key_width)
    draft_keys = jnp.take(own_latent, draft_cols, axis=1)
    draft_pad = 128
    draft_rows = jnp.pad(draft_keys, ((0, 0), (0, draft_pad - draft_share), (0, 0)))
    tree_ok = (jnp.take(ancestry, draft_cols, axis=2) > 0.5).astype(jnp.float32)
    tree_rows = jnp.broadcast_to(
        tree_ok[:, :, None, :], (request_count, draft_count, head_count, draft_share)
    ).reshape(request_count, draft_count * head_count, draft_share)
    tree_rows = jnp.pad(tree_rows, ((0, 0), (0, 0), (0, draft_pad - draft_share)))
    absorbed = jnp.einsum(
        "thd,hdl->thl", queries[:, :, :nope_width], absorb_key, preferred_element_type=jnp.float32
    ).astype(jnp.bfloat16)
    query_rows = absorbed.reshape(request_count, draft_count * head_count, latent_width)
    rope_rows = queries[:, :, nope_width:].reshape(request_count, draft_count * head_count, -1)
    mixed_rows, stats = paged_attention(
        slot_rows, limits, query_rows, rope_rows, jnp.swapaxes(cache_pool, 1, 2), draft_rows,
        tree_rows, score_scale,
    )
    mixed_latent = mixed_rows.reshape(request_count, draft_count, head_count, latent_width)
    highest_score = stats[:, :, 0].reshape(request_count, draft_count, head_count)
    totals = stats[:, :, 1].reshape(request_count, draft_count, head_count)
    partial_head = jnp.einsum(
        "rthl,hlv->rthv",
        mixed_latent.astype(jnp.bfloat16),
        absorb_value,
        preferred_element_type=jnp.float32,
    )
    head_width = head_count * partial_head.shape[-1]
    low_parts = split_exact(jnp.concatenate([highest_score, totals], axis=-1))
    packed = jnp.concatenate(
        [partial_head.reshape(token_count, head_width).astype(jnp.bfloat16)]
        + [part.reshape(token_count, 2 * head_count) for part in low_parts],
        axis=1,
    )
    gathered = lax.all_gather(packed, "req").astype(jnp.float32)
    part_heads = gathered[:, :, :head_width]
    rejoined = sum(
        gathered[:, :, head_width + 2 * head_count * k : head_width + 2 * head_count * (k + 1)]
        for k in range(3)
    )
    part_max = rejoined[:, :, :head_count]
    part_sum = rejoined[:, :, head_count:]
    top = jnp.max(part_max, axis=0)
    factor = jnp.exp(part_max - top[None])
    merged_sum = jnp.sum(factor * part_sum, axis=0)
    value_width = head_width // head_count
    spread = (
        jnp.arange(head_width, dtype=jnp.int32)[None, :] // value_width
        == jnp.arange(head_count, dtype=jnp.int32)[:, None]
    ).astype(jnp.bfloat16)
    scale_rows = (factor / merged_sum[None]).reshape(req_count * token_count, head_count)
    scale_high = scale_rows.astype(jnp.bfloat16)
    scale_low = (scale_rows - scale_high.astype(jnp.float32)).astype(jnp.bfloat16)
    factor_wide = (
        jnp.dot(scale_high, spread, preferred_element_type=jnp.float32)
        + jnp.dot(scale_low, spread, preferred_element_type=jnp.float32)
    ).reshape(req_count, token_count, head_width)
    head_rows = jnp.sum(factor_wide * part_heads, axis=0).astype(jnp.bfloat16)
    attention = jnp.dot(head_rows, out_proj, preferred_element_type=jnp.float32)
    resid_cols = (hidden_in.astype(jnp.float32) + attention).astype(jnp.bfloat16)
    resid = lax.all_gather(resid_cols, "req", axis=1, tiled=True)
    resid_wide = resid.astype(jnp.float32)
    normed = resid_wide * lax.rsqrt(
        jnp.mean(resid_wide * resid_wide, axis=1, keepdims=True) + 1e-06
    )
    normed = (normed * norm_gain[None, :]).astype(jnp.bfloat16)
    logits = jnp.dot(normed, router, preferred_element_type=jnp.float32)
    lifted = jax.nn.sigmoid(jnp.take_along_axis(logits, expert_ids, axis=1))
    gates = lifted / jnp.sum(lifted, axis=1, keepdims=True)
    shared_gate = jnp.dot(normed, shared_gate_up[0], preferred_element_type=jnp.float32)
    shared_lift = jnp.dot(normed, shared_gate_up[1], preferred_element_type=jnp.float32)
    shared_hidden = (jax.nn.silu(shared_gate) * shared_lift).astype(jnp.bfloat16)
    shared_part = jnp.dot(shared_hidden, shared_down, preferred_element_type=jnp.float32)
    route_width = expert_ids.shape[1]
    local_experts = expert_gate_up.shape[0]
    expert_total = local_experts * ep_count
    capacity = (2 * token_count * route_width + expert_total - 1) // expert_total
    pair_experts = expert_ids.reshape(-1)
    marks = (pair_experts[:, None] == jnp.arange(expert_total, dtype=jnp.int32)[None, :]).astype(
        jnp.int32
    )
    slot_of = jnp.sum(jnp.cumsum(marks, axis=0) * marks, axis=1) - 1
    placement = (pair_experts * capacity + slot_of).reshape(token_count, route_width)
    slot_count = expert_total * capacity
    slot_index = jnp.arange(slot_count, dtype=jnp.int32)
    hits = placement[None, :, :] == slot_index[:, None, None]
    dispatch = jnp.any(hits, axis=2).astype(jnp.bfloat16)
    outgoing = jnp.dot(dispatch, normed, preferred_element_type=jnp.float32).astype(jnp.bfloat16)
    outgoing = outgoing.reshape(ep_count, local_experts, capacity, -1)
    gate_weight = expert_gate_up[:, 0]
    lift_weight = expert_gate_up[:, 1]
    incoming = lax.all_to_all(outgoing, "ep", split_axis=0, concat_axis=0, tiled=True)
    gate_value = jnp.einsum(
        "pecd,edf->pecf", incoming, gate_weight, preferred_element_type=jnp.float32
    )
    lift_value = jnp.einsum(
        "pecd,edf->pecf", incoming, lift_weight, preferred_element_type=jnp.float32
    )
    hidden_rows = (jax.nn.silu(gate_value) * lift_value).astype(jnp.bfloat16)
    feature_share = expert_down.shape[-1] // req_count
    sending = jnp.stack(
        [
            jnp.stack(
                [
                    jnp.dot(
                        hidden_rows[:, expert],
                        expert_down[expert, :, share * feature_share : (share + 1) * feature_share],
                        preferred_element_type=jnp.float32,
                    ).astype(jnp.bfloat16)
                    for expert in range(local_experts)
                ],
                axis=1,
            )
            for share in range(req_count)
        ],
        axis=0,
    ).reshape(req_count * ep_count, local_experts, capacity, feature_share)
    returned = lax.all_to_all(sending, ("req", "ep"), 0, 0, tiled=True).reshape(
        req_count * slot_count, feature_share
    )
    combine = jnp.sum(
        jnp.where(
            placement[:, :, None] == slot_index[None, None, :], gates[:, :, None], 0.0
        ),
        axis=1,
    )
    combine = jnp.tile(combine, (1, req_count))
    combine_high = combine.astype(jnp.bfloat16)
    combine_low = (combine - combine_high.astype(jnp.float32)).astype(jnp.bfloat16)
    both = jnp.dot(
        jnp.concatenate([combine_high, combine_low], axis=0),
        returned,
        preferred_element_type=jnp.float32,
    )
    routed = both[:token_count] + both[token_count:]
    shared_cols = lax.psum_scatter(
        shared_part.astype(jnp.bfloat16), "req", scatter_dimension=1, tiled=True
    )
    layer_out = (
        resid_cols.astype(jnp.float32) + shared_cols.astype(jnp.float32) + routed
    ).astype(jnp.bfloat16)
    starts = cache_len // page_size
    page_now = starts + jnp.mod(req_index - starts, req_count)
    slot_now = jnp.take_along_axis(page_table, page_now[:, None], axis=1)[:, 0]
    old_page = cache_pool[slot_now]
    offsets = (
        page_now[:, None] * page_size
        + jnp.arange(page_size, dtype=jnp.int32)[None, :]
        - cache_len[:, None]
    ).astype(jnp.float32)
    accepted = jnp.take_along_axis(ancestry, accept_leaf[:, None, None], axis=1)[:, 0, :]
    select = accepted[:, None, :] * (depths[:, None, :] == offsets[:, :, None]).astype(jnp.float32)
    written = jnp.einsum(
        "rod,rdk->rok", select.astype(jnp.bfloat16), own_latent, preferred_element_type=jnp.float32
    )
    touched = jnp.sum(select, axis=2) > 0.5
    fresh = jnp.where(touched[..., None], written, old_page.astype(jnp.float32)).astype(
        jnp.bfloat16
    )
    return (layer_out, fresh[:, None])


def solution(mesh):
    in_specs = (
        P("ep", None, None),
        P("ep", None),
        P("ep", "req"),
        P(("req", "ep"), None, None),
        P("ep", None),
        P("ep"),
        P("ep", None),
        P("ep"),
        P(),
        P(),
        P(None, "req"),
        P(),
        P(),
        P("ep", None),
        P("ep", None, None, "req"),
        P("ep", "req", None),
        P(None, None, "req"),
        P("req", None),
    )
    out_specs = (P("ep", "req"), P("ep", "req", None, None))
    return jax.shard_map(
        per_device, mesh=mesh, in_specs=in_specs, out_specs=out_specs, check_vma=False
    )
```

```python
import functools
import math

import jax
import jax.numpy as jnp
from jax import lax
from jax.experimental import pallas as pl
from jax.experimental.pallas import tpu as pltpu
from jax.sharding import PartitionSpec as P

NEGATIVE = -1e30


def ancestors(parents):
    draft_count = parents.shape[-1]
    draft_index = jnp.arange(draft_count, dtype=jnp.int32)
    ancestry = (parents[:, :, None] == draft_index[None, None, :]).astype(jnp.float32)
    ancestry = ancestry + jnp.eye(draft_count, dtype=jnp.float32)[None]
    for doubling in range(max(1, (draft_count - 1).bit_length())):
        ancestry = jnp.minimum(
            jnp.einsum("rij,rjk->rik", ancestry, ancestry, precision=lax.Precision.HIGHEST), 1.0
        )
    return ancestry


def split_exact(values):
    pieces = []
    rest = values
    for _ in range(3):
        piece = lax.reduce_precision(rest, exponent_bits=8, mantissa_bits=7)
        pieces.append(piece.astype(jnp.bfloat16))
        rest = rest - piece
    return pieces


def attention_kernel(
    slots_ref, limits_ref, q_ref, rope_ref, page_ref, draft_ref, tree_ref, mixed_ref, stats_ref,
    keys,
    *, page_size, latent_width, score_scale, row_block
):
    request = pl.program_id(0)
    page = pl.program_id(1)
    page_total = pl.num_programs(1)
    keys[page] = page_ref[0]

    @pl.when(page == page_total - 1)
    def _():
        local_pages = keys.shape[0]
        key_rows = local_pages * page_size
        column = lax.broadcasted_iota(jnp.int32, (1, key_rows), 1)
        limit = jnp.zeros((1, key_rows), jnp.int32)
        for index in range(local_pages):
            limit = jnp.where(column // page_size == index, limits_ref[request, index], limit)
        cache_ok = (column % page_size) < limit
        lane = lax.broadcasted_iota(jnp.int32, (row_block, stats_ref.shape[2]), 1)

        def body(block, carry):
            rows = pl.ds(pl.multiple_of(block * row_block, row_block), row_block)
            query = q_ref[0, rows, :]
            rope = rope_ref[0, rows, :]
            contract = (((1,), (1,)), ((), ()))
            score = jnp.concatenate(
                [
                    jnp.dot(query, keys[index, :latent_width, :], preferred_element_type=jnp.float32)
                    + jnp.dot(rope, keys[index, latent_width:, :], preferred_element_type=jnp.float32)
                    for index in range(local_pages)
                ],
                axis=1,
            ) * score_scale
            score = jnp.where(cache_ok, score, NEGATIVE)
            draft_score = (
                lax.dot_general(
                    query, draft_ref[0, :, :latent_width], contract,
                    preferred_element_type=jnp.float32,
                )
                + lax.dot_general(
                    rope, draft_ref[0, :, latent_width:], contract,
                    preferred_element_type=jnp.float32,
                )
            ) * score_scale
            tree_ok = tree_ref[0, rows, :] > 0.5
            draft_score = jnp.where(tree_ok, draft_score, NEGATIVE)
            top = jnp.maximum(
                jnp.max(score, axis=1, keepdims=True), jnp.max(draft_score, axis=1, keepdims=True)
            )
            weight = jnp.exp(score - top)
            draft_weight = jnp.exp(draft_score - top)
            total = jnp.sum(weight, axis=1, keepdims=True) + jnp.sum(
                draft_weight, axis=1, keepdims=True
            )
            weight_low = weight.astype(jnp.bfloat16)
            mixed = jnp.dot(
                draft_weight.astype(jnp.bfloat16),
                draft_ref[0, :, :latent_width],
                preferred_element_type=jnp.float32,
            )
            for index in range(local_pages):
                mixed = mixed + lax.dot_general(
                    weight_low[:, index * page_size : (index + 1) * page_size],
                    keys[index, :latent_width, :],
                    contract,
                    preferred_element_type=jnp.float32,
                )
            mixed_ref[0, rows, :] = mixed
            stats_ref[0, rows, :] = jnp.where(lane == 0, top, jnp.where(lane == 1, total, 0.0))
            return carry

        lax.fori_loop(0, q_ref.shape[1] // row_block, body, 0)


def paged_attention(slots, limits, query_rows, rope_rows, cache_pool, draft_rows, tree_rows, score_scale):
    request_count, row_count, latent_width = query_rows.shape
    key_width = cache_pool.shape[1]
    rope_width = rope_rows.shape[2]
    local_pages = slots.shape[1]
    page_size = cache_pool.shape[2]
    draft_pad = draft_rows.shape[1]
    row_block = 128
    kernel = functools.partial(
        attention_kernel,
        page_size=page_size,
        latent_width=latent_width,
        score_scale=score_scale,
        row_block=row_block,
    )
    key_rows = local_pages * page_size
    flops = 2 * request_count * row_count * (key_rows + draft_pad) * (key_width + latent_width)
    cost = pl.CostEstimate(
        flops=flops,
        transcendentals=request_count * row_count * (key_rows + draft_pad),
        bytes_accessed=2 * request_count * (row_count + key_rows) * key_width
        + 4 * request_count * row_count * (latent_width + 128 + draft_pad),
    )
    grid_spec = pltpu.PrefetchScalarGridSpec(
        num_scalar_prefetch=2,
        grid=(request_count, local_pages),
        in_specs=[
            pl.BlockSpec((1, row_count, latent_width), lambda r, j, s, n: (r, 0, 0)),
            pl.BlockSpec((1, row_count, rope_width), lambda r, j, s, n: (r, 0, 0)),
            pl.BlockSpec((1, key_width, page_size), lambda r, j, s, n: (s[r, j], 0, 0)),
            pl.BlockSpec((1, draft_pad, key_width), lambda r, j, s, n: (r, 0, 0)),
            pl.BlockSpec((1, row_count, draft_pad), lambda r, j, s, n: (r, 0, 0)),
        ],
        out_specs=[
            pl.BlockSpec((1, row_count, latent_width), lambda r, j, s, n: (r, 0, 0)),
            pl.BlockSpec((1, row_count, 128), lambda r, j, s, n: (r, 0, 0)),
        ],
        scratch_shapes=[pltpu.VMEM((local_pages, key_width, page_size), jnp.bfloat16)],
    )
    return pl.pallas_call(
        kernel,
        grid_spec=grid_spec,
        out_shape=[
            jax.ShapeDtypeStruct((request_count, row_count, latent_width), jnp.float32),
            jax.ShapeDtypeStruct((request_count, row_count, 128), jnp.float32),
        ],
        compiler_params=pltpu.CompilerParams(
            dimension_semantics=("arbitrary", "arbitrary"), vmem_limit_bytes=48 * 1024 * 1024
        ),
        cost_estimate=cost,
    )(slots, limits, query_rows, rope_rows, cache_pool, draft_rows, tree_rows)


def per_device(
    queries,
    draft_latent,
    hidden_in,
    cache_pool,
    page_table,
    cache_len,
    parents,
    accept_leaf,
    absorb_key,
    absorb_value,
    out_proj,
    norm_gain,
    router,
    expert_ids,
    expert_gate_up,
    expert_down,
    shared_gate_up,
    shared_down,
):
    highest = lax.Precision.HIGHEST
    req_count = lax.axis_size("req")
    req_index = lax.axis_index("req")
    ep_count = lax.axis_size("ep")
    request_count, draft_count = parents.shape
    token_count = request_count * draft_count
    head_count = queries.shape[1]
    nope_width = absorb_key.shape[1]
    latent_width = absorb_key.shape[2]
    page_size = cache_pool.shape[1]
    key_width = cache_pool.shape[2]
    page_count = page_table.shape[1]
    score_scale = 1.0 / math.sqrt(queries.shape[2])
    ancestry = ancestors(parents)
    depths = jnp.sum(ancestry, axis=2) - 1.0
    local_pages = page_count // req_count
    page_cols = req_index + req_count * jnp.arange(local_pages, dtype=jnp.int32)
    slot_rows = jnp.take(page_table, page_cols, axis=1)
    pool_slots = cache_pool.shape[0]
    slot_rows = jnp.clip(slot_rows, 0, pool_slots - 1).astype(jnp.int32)
    limits = jnp.clip(
        cache_len[:, None] - page_cols[None, :] * page_size, 0, page_size
    ).astype(jnp.int32)
    draft_share = draft_count // req_count
    draft_cols = req_index * draft_share + jnp.arange(draft_share, dtype=jnp.int32)
    own_latent = draft_latent.reshape(request_count, draft_count, key_width)
    draft_keys = jnp.take(own_latent, draft_cols, axis=1)
    draft_pad = 128
    draft_rows = jnp.pad(draft_keys, ((0, 0), (0, draft_pad - draft_share), (0, 0)))
    tree_ok = (jnp.take(ancestry, draft_cols, axis=2) > 0.5).astype(jnp.float32)
    tree_rows = jnp.broadcast_to(
        tree_ok[:, :, None, :], (request_count, draft_count, head_count, draft_share)
    ).reshape(request_count, draft_count * head_count, draft_share)
    tree_rows = jnp.pad(tree_rows, ((0, 0), (0, 0), (0, draft_pad - draft_share)))
    absorbed = jnp.einsum(
        "thd,hdl->thl", queries[:, :, :nope_width], absorb_key, preferred_element_type=jnp.float32
    ).astype(jnp.bfloat16)
    query_rows = absorbed.reshape(request_count, draft_count * head_count, latent_width)
    rope_rows = queries[:, :, nope_width:].reshape(request_count, draft_count * head_count, -1)
    mixed_rows, stats = paged_attention(
        slot_rows, limits, query_rows, rope_rows, jnp.swapaxes(cache_pool, 1, 2), draft_rows,
        tree_rows, score_scale,
    )
    mixed_latent = mixed_rows.reshape(request_count, draft_count, head_count, latent_width)
    highest_score = stats[:, :, 0].reshape(request_count, draft_count, head_count)
    totals = stats[:, :, 1].reshape(request_count, draft_count, head_count)
    partial_head = jnp.einsum(
        "rthl,hlv->rthv",
        mixed_latent.astype(jnp.bfloat16),
        absorb_value,
        preferred_element_type=jnp.float32,
    )
    head_width = head_count * partial_head.shape[-1]
    low_parts = split_exact(jnp.concatenate([highest_score, totals], axis=-1))
    packed = jnp.concatenate(
        [partial_head.reshape(token_count, head_width).astype(jnp.bfloat16)]
        + [part.reshape(token_count, 2 * head_count) for part in low_parts],
        axis=1,
    )
    gathered = lax.all_gather(packed, "req").astype(jnp.float32)
    part_heads = gathered[:, :, :head_width]
    rejoined = sum(
        gathered[:, :, head_width + 2 * head_count * k : head_width + 2 * head_count * (k + 1)]
        for k in range(3)
    )
    part_max = rejoined[:, :, :head_count]
    part_sum = rejoined[:, :, head_count:]
    top = jnp.max(part_max, axis=0)
    factor = jnp.exp(part_max - top[None])
    merged_sum = jnp.sum(factor * part_sum, axis=0)
    value_width = head_width // head_count
    spread = (
        jnp.arange(head_width, dtype=jnp.int32)[None, :] // value_width
        == jnp.arange(head_count, dtype=jnp.int32)[:, None]
    ).astype(jnp.bfloat16)
    scale_rows = (factor / merged_sum[None]).reshape(req_count * token_count, head_count)
    factor_wide = jnp.dot(
        scale_rows.astype(jnp.bfloat16), spread, preferred_element_type=jnp.float32
    ).reshape(req_count, token_count, head_width)
    head_rows = jnp.sum(factor_wide * part_heads, axis=0).astype(jnp.bfloat16)
    attention = jnp.dot(head_rows, out_proj, preferred_element_type=jnp.float32)
    resid_cols = (hidden_in.astype(jnp.float32) + attention).astype(jnp.bfloat16)
    resid = lax.all_gather(resid_cols, "req", axis=1, tiled=True)
    resid_wide = resid.astype(jnp.float32)
    normed = resid_wide * lax.rsqrt(
        jnp.mean(resid_wide * resid_wide, axis=1, keepdims=True) + 1e-06
    )
    normed = (normed * norm_gain[None, :]).astype(jnp.bfloat16)
    logits = jnp.dot(normed, router, preferred_element_type=jnp.float32)
    lifted = jax.nn.sigmoid(jnp.take_along_axis(logits, expert_ids, axis=1))
    gates = lifted / jnp.sum(lifted, axis=1, keepdims=True)
    shared_gate = jnp.dot(normed, shared_gate_up[0], preferred_element_type=jnp.float32)
    shared_lift = jnp.dot(normed, shared_gate_up[1], preferred_element_type=jnp.float32)
    shared_hidden = (jax.nn.silu(shared_gate) * shared_lift).astype(jnp.bfloat16)
    shared_part = jnp.dot(shared_hidden, shared_down, preferred_element_type=jnp.float32)
    route_width = expert_ids.shape[1]
    local_experts = expert_gate_up.shape[0]
    expert_total = local_experts * ep_count
    capacity = (2 * token_count * route_width + expert_total - 1) // expert_total
    pair_experts = expert_ids.reshape(-1)
    marks = (pair_experts[:, None] == jnp.arange(expert_total, dtype=jnp.int32)[None, :]).astype(
        jnp.int32
    )
    slot_of = jnp.sum(jnp.cumsum(marks, axis=0) * marks, axis=1) - 1
    placement = (pair_experts * capacity + slot_of).reshape(token_count, route_width)
    slot_count = expert_total * capacity
    slot_index = jnp.arange(slot_count, dtype=jnp.int32)
    hits = placement[None, :, :] == slot_index[:, None, None]
    dispatch = jnp.any(hits, axis=2).astype(jnp.bfloat16)
    outgoing = jnp.dot(dispatch, normed, preferred_element_type=jnp.float32).astype(jnp.bfloat16)
    outgoing = outgoing.reshape(ep_count, local_experts, capacity, -1)
    gate_weight = expert_gate_up[:, 0]
    lift_weight = expert_gate_up[:, 1]
    incoming = lax.all_to_all(outgoing, "ep", split_axis=0, concat_axis=0, tiled=True)
    gate_value = jnp.einsum(
        "pecd,edf->pecf", incoming, gate_weight, preferred_element_type=jnp.float32
    )
    lift_value = jnp.einsum(
        "pecd,edf->pecf", incoming, lift_weight, preferred_element_type=jnp.float32
    )
    hidden_rows = (jax.nn.silu(gate_value) * lift_value).astype(jnp.bfloat16)
    feature_share = expert_down.shape[-1] // req_count
    sending = jnp.stack(
        [
            jnp.stack(
                [
                    jnp.dot(
                        hidden_rows[:, expert],
                        expert_down[expert, :, share * feature_share : (share + 1) * feature_share],
                        preferred_element_type=jnp.float32,
                    ).astype(jnp.bfloat16)
                    for expert in range(local_experts)
                ],
                axis=1,
            )
            for share in range(req_count)
        ],
        axis=0,
    ).reshape(req_count * ep_count, local_experts, capacity, feature_share)
    returned = lax.all_to_all(sending, ("req", "ep"), 0, 0, tiled=True).reshape(
        req_count * slot_count, feature_share
    )
    combine = jnp.sum(
        jnp.where(
            placement[:, :, None] == slot_index[None, None, :], gates[:, :, None], 0.0
        ),
        axis=1,
    )
    combine = jnp.tile(combine, (1, req_count))
    combine_high = combine.astype(jnp.bfloat16)
    combine_low = (combine - combine_high.astype(jnp.float32)).astype(jnp.bfloat16)
    both = jnp.dot(
        jnp.concatenate([combine_high, combine_low], axis=0),
        returned,
        preferred_element_type=jnp.float32,
    )
    routed = both[:token_count] + both[token_count:]
    shared_cols = lax.psum_scatter(
        shared_part.astype(jnp.bfloat16), "req", scatter_dimension=1, tiled=True
    )
    layer_out = (
        resid_cols.astype(jnp.float32) + shared_cols.astype(jnp.float32) + routed
    ).astype(jnp.bfloat16)
    starts = cache_len // page_size
    page_now = starts + jnp.mod(req_index - starts, req_count)
    slot_now = jnp.take_along_axis(page_table, page_now[:, None], axis=1)[:, 0]
    old_page = cache_pool[slot_now]
    offsets = (
        page_now[:, None] * page_size
        + jnp.arange(page_size, dtype=jnp.int32)[None, :]
        - cache_len[:, None]
    ).astype(jnp.float32)
    accepted = jnp.take_along_axis(ancestry, accept_leaf[:, None, None], axis=1)[:, 0, :]
    select = accepted[:, None, :] * (depths[:, None, :] == offsets[:, :, None]).astype(jnp.float32)
    written = jnp.einsum(
        "rod,rdk->rok", select.astype(jnp.bfloat16), own_latent, preferred_element_type=jnp.float32
    )
    touched = jnp.sum(select, axis=2) > 0.5
    fresh = jnp.where(touched[..., None], written, old_page.astype(jnp.float32)).astype(
        jnp.bfloat16
    )
    return (layer_out, fresh[:, None])


def solution(mesh):
    in_specs = (
        P("ep", None, None),
        P("ep", None),
        P("ep", "req"),
        P(("req", "ep"), None, None),
        P("ep", None),
        P("ep"),
        P("ep", None),
        P("ep"),
        P(),
        P(),
        P(None, "req"),
        P(),
        P(),
        P("ep", None),
        P("ep", None, None, "req"),
        P("ep", "req", None),
        P(None, None, "req"),
        P("req", None),
    )
    out_specs = (P("ep", "req"), P("ep", "req", None, None))
    return jax.shard_map(
        per_device, mesh=mesh, in_specs=in_specs, out_specs=out_specs, check_vma=False
    )
```

```python
import functools
import math

import jax
import jax.numpy as jnp
from jax import lax
from jax.experimental import pallas as pl
from jax.experimental.pallas import tpu as pltpu
from jax.sharding import PartitionSpec as P

NEGATIVE = -1e30


def ancestors(parents):
    draft_count = parents.shape[-1]
    draft_index = jnp.arange(draft_count, dtype=jnp.int32)
    ancestry = (parents[:, :, None] == draft_index[None, None, :]).astype(jnp.float32)
    ancestry = ancestry + jnp.eye(draft_count, dtype=jnp.float32)[None]
    for doubling in range(max(1, (draft_count - 1).bit_length())):
        ancestry = jnp.minimum(
            jnp.einsum("rij,rjk->rik", ancestry, ancestry, precision=lax.Precision.HIGHEST), 1.0
        )
    return ancestry


def split_exact(values):
    pieces = []
    rest = values
    for _ in range(3):
        piece = lax.reduce_precision(rest, exponent_bits=8, mantissa_bits=7)
        pieces.append(piece.astype(jnp.bfloat16))
        rest = rest - piece
    return pieces


def attention_kernel(
    slots_ref, limits_ref, q_ref, rope_ref, page_ref, draft_ref, tree_ref, mixed_ref, stats_ref,
    keys,
    *, page_size, latent_width, score_scale, row_block
):
    request = pl.program_id(0)
    page = pl.program_id(1)
    page_total = pl.num_programs(1)
    keys[page] = page_ref[0]

    @pl.when(page == page_total - 1)
    def _():
        local_pages = keys.shape[0]
        key_rows = local_pages * page_size
        column = lax.broadcasted_iota(jnp.int32, (1, key_rows), 1)
        limit = jnp.zeros((1, key_rows), jnp.int32)
        for index in range(local_pages):
            limit = jnp.where(column // page_size == index, limits_ref[request, index], limit)
        cache_ok = (column % page_size) < limit
        lane = lax.broadcasted_iota(jnp.int32, (row_block, stats_ref.shape[2]), 1)

        def body(block, carry):
            rows = pl.ds(pl.multiple_of(block * row_block, row_block), row_block)
            query = q_ref[0, rows, :]
            rope = rope_ref[0, rows, :]
            contract = (((1,), (1,)), ((), ()))
            score = jnp.concatenate(
                [
                    jnp.dot(query, keys[index, :latent_width, :], preferred_element_type=jnp.float32)
                    + jnp.dot(rope, keys[index, latent_width:, :], preferred_element_type=jnp.float32)
                    for index in range(local_pages)
                ],
                axis=1,
            ) * score_scale
            score = jnp.where(cache_ok, score, NEGATIVE)
            draft_score = (
                lax.dot_general(
                    query, draft_ref[0, :, :latent_width], contract,
                    preferred_element_type=jnp.float32,
                )
                + lax.dot_general(
                    rope, draft_ref[0, :, latent_width:], contract,
                    preferred_element_type=jnp.float32,
                )
            ) * score_scale
            tree_ok = tree_ref[0, rows, :] > 0.5
            draft_score = jnp.where(tree_ok, draft_score, NEGATIVE)
            top = jnp.maximum(
                jnp.max(score, axis=1, keepdims=True), jnp.max(draft_score, axis=1, keepdims=True)
            )
            weight = jnp.exp(score - top)
            draft_weight = jnp.exp(draft_score - top)
            total = jnp.sum(weight, axis=1, keepdims=True) + jnp.sum(
                draft_weight, axis=1, keepdims=True
            )
            weight_low = weight.astype(jnp.bfloat16)
            mixed = jnp.dot(
                draft_weight.astype(jnp.bfloat16),
                draft_ref[0, :, :latent_width],
                preferred_element_type=jnp.float32,
            )
            for index in range(local_pages):
                mixed = mixed + lax.dot_general(
                    weight_low[:, index * page_size : (index + 1) * page_size],
                    keys[index, :latent_width, :],
                    contract,
                    preferred_element_type=jnp.float32,
                )
            mixed_ref[0, rows, :] = mixed
            stats_ref[0, rows, :] = jnp.where(lane == 0, top, jnp.where(lane == 1, total, 0.0))
            return carry

        lax.fori_loop(0, q_ref.shape[1] // row_block, body, 0)


def paged_attention(slots, limits, query_rows, rope_rows, cache_pool, draft_rows, tree_rows, score_scale):
    request_count, row_count, latent_width = query_rows.shape
    key_width = cache_pool.shape[1]
    rope_width = rope_rows.shape[2]
    local_pages = slots.shape[1]
    page_size = cache_pool.shape[2]
    draft_pad = draft_rows.shape[1]
    row_block = 128
    kernel = functools.partial(
        attention_kernel,
        page_size=page_size,
        latent_width=latent_width,
        score_scale=score_scale,
        row_block=row_block,
    )
    key_rows = local_pages * page_size
    flops = 2 * request_count * row_count * (key_rows + draft_pad) * (key_width + latent_width)
    cost = pl.CostEstimate(
        flops=flops,
        transcendentals=request_count * row_count * (key_rows + draft_pad),
        bytes_accessed=2 * request_count * (row_count + key_rows) * key_width
        + 4 * request_count * row_count * (latent_width + 128 + draft_pad),
    )
    grid_spec = pltpu.PrefetchScalarGridSpec(
        num_scalar_prefetch=2,
        grid=(request_count, local_pages),
        in_specs=[
            pl.BlockSpec((1, row_count, latent_width), lambda r, j, s, n: (r, 0, 0)),
            pl.BlockSpec((1, row_count, rope_width), lambda r, j, s, n: (r, 0, 0)),
            pl.BlockSpec((1, key_width, page_size), lambda r, j, s, n: (s[r, j], 0, 0)),
            pl.BlockSpec((1, draft_pad, key_width), lambda r, j, s, n: (r, 0, 0)),
            pl.BlockSpec((1, row_count, draft_pad), lambda r, j, s, n: (r, 0, 0)),
        ],
        out_specs=[
            pl.BlockSpec((1, row_count, latent_width), lambda r, j, s, n: (r, 0, 0)),
            pl.BlockSpec((1, row_count, 128), lambda r, j, s, n: (r, 0, 0)),
        ],
        scratch_shapes=[pltpu.VMEM((local_pages, key_width, page_size), jnp.bfloat16)],
    )
    return pl.pallas_call(
        kernel,
        grid_spec=grid_spec,
        out_shape=[
            jax.ShapeDtypeStruct((request_count, row_count, latent_width), jnp.float32),
            jax.ShapeDtypeStruct((request_count, row_count, 128), jnp.float32),
        ],
        compiler_params=pltpu.CompilerParams(
            dimension_semantics=("arbitrary", "arbitrary"), vmem_limit_bytes=48 * 1024 * 1024
        ),
        cost_estimate=cost,
    )(slots, limits, query_rows, rope_rows, cache_pool, draft_rows, tree_rows)


def per_device(
    queries,
    draft_latent,
    hidden_in,
    cache_pool,
    page_table,
    cache_len,
    parents,
    accept_leaf,
    absorb_key,
    absorb_value,
    out_proj,
    norm_gain,
    router,
    expert_ids,
    expert_gate_up,
    expert_down,
    shared_gate_up,
    shared_down,
):
    highest = lax.Precision.HIGHEST
    req_count = lax.axis_size("req")
    req_index = lax.axis_index("req")
    ep_count = lax.axis_size("ep")
    request_count, draft_count = parents.shape
    token_count = request_count * draft_count
    head_count = queries.shape[1]
    nope_width = absorb_key.shape[1]
    latent_width = absorb_key.shape[2]
    page_size = cache_pool.shape[1]
    key_width = cache_pool.shape[2]
    page_count = page_table.shape[1]
    score_scale = 1.0 / math.sqrt(queries.shape[2])
    ancestry = ancestors(parents)
    depths = jnp.sum(ancestry, axis=2) - 1.0
    local_pages = page_count // req_count
    page_cols = req_index + req_count * jnp.arange(local_pages, dtype=jnp.int32)
    slot_rows = jnp.take(page_table, page_cols, axis=1)
    pool_slots = cache_pool.shape[0]
    slot_rows = jnp.clip(slot_rows, 0, pool_slots - 1).astype(jnp.int32)
    limits = jnp.clip(
        cache_len[:, None] - page_cols[None, :] * page_size, 0, page_size
    ).astype(jnp.int32)
    draft_share = draft_count // req_count
    draft_cols = req_index * draft_share + jnp.arange(draft_share, dtype=jnp.int32)
    own_latent = draft_latent.reshape(request_count, draft_count, key_width)
    draft_keys = jnp.take(own_latent, draft_cols, axis=1)
    draft_pad = 128
    draft_rows = jnp.pad(draft_keys, ((0, 0), (0, draft_pad - draft_share), (0, 0)))
    tree_ok = (jnp.take(ancestry, draft_cols, axis=2) > 0.5).astype(jnp.float32)
    tree_rows = jnp.broadcast_to(
        tree_ok[:, :, None, :], (request_count, draft_count, head_count, draft_share)
    ).reshape(request_count, draft_count * head_count, draft_share)
    tree_rows = jnp.pad(tree_rows, ((0, 0), (0, 0), (0, draft_pad - draft_share)))
    absorbed = jnp.einsum(
        "thd,hdl->thl", queries[:, :, :nope_width], absorb_key, preferred_element_type=jnp.float32
    ).astype(jnp.bfloat16)
    query_rows = absorbed.reshape(request_count, draft_count * head_count, latent_width)
    rope_rows = queries[:, :, nope_width:].reshape(request_count, draft_count * head_count, -1)
    mixed_rows, stats = paged_attention(
        slot_rows, limits, query_rows, rope_rows, jnp.swapaxes(cache_pool, 1, 2), draft_rows,
        tree_rows, score_scale,
    )
    mixed_latent = mixed_rows.reshape(request_count, draft_count, head_count, latent_width)
    highest_score = stats[:, :, 0].reshape(request_count, draft_count, head_count)
    totals = stats[:, :, 1].reshape(request_count, draft_count, head_count)
    partial_head = jnp.einsum(
        "rthl,hlv->rthv",
        mixed_latent.astype(jnp.bfloat16),
        absorb_value,
        preferred_element_type=jnp.float32,
    )
    head_width = head_count * partial_head.shape[-1]
    low_parts = split_exact(jnp.concatenate([highest_score, totals], axis=-1))
    packed = jnp.concatenate(
        [partial_head.reshape(token_count, head_width).astype(jnp.bfloat16)]
        + [part.reshape(token_count, 2 * head_count) for part in low_parts],
        axis=1,
    )
    gathered = lax.all_gather(packed, "req").astype(jnp.float32)
    part_heads = gathered[:, :, :head_width]
    rejoined = sum(
        gathered[:, :, head_width + 2 * head_count * k : head_width + 2 * head_count * (k + 1)]
        for k in range(3)
    )
    part_max = rejoined[:, :, :head_count]
    part_sum = rejoined[:, :, head_count:]
    top = jnp.max(part_max, axis=0)
    factor = jnp.exp(part_max - top[None])
    merged_sum = jnp.sum(factor * part_sum, axis=0)
    value_width = head_width // head_count
    spread = (
        jnp.arange(head_width, dtype=jnp.int32)[None, :] // value_width
        == jnp.arange(head_count, dtype=jnp.int32)[:, None]
    ).astype(jnp.bfloat16)
    scale_rows = (factor / merged_sum[None]).reshape(req_count * token_count, head_count)
    factor_wide = jnp.dot(
        scale_rows.astype(jnp.bfloat16), spread, preferred_element_type=jnp.float32
    ).reshape(req_count, token_count, head_width)
    head_rows = jnp.sum(factor_wide * part_heads, axis=0).astype(jnp.bfloat16)
    attention = jnp.dot(head_rows, out_proj, preferred_element_type=jnp.float32)
    resid_cols = (hidden_in.astype(jnp.float32) + attention).astype(jnp.bfloat16)
    resid = lax.all_gather(resid_cols, "req", axis=1, tiled=True)
    resid_wide = resid.astype(jnp.float32)
    normed = resid_wide * lax.rsqrt(
        jnp.mean(resid_wide * resid_wide, axis=1, keepdims=True) + 1e-06
    )
    normed = (normed * norm_gain[None, :]).astype(jnp.bfloat16)
    logits = jnp.dot(normed, router, preferred_element_type=jnp.float32)
    lifted = jax.nn.sigmoid(jnp.take_along_axis(logits, expert_ids, axis=1))
    gates = lifted / jnp.sum(lifted, axis=1, keepdims=True)
    shared_gate = jnp.dot(normed, shared_gate_up[0], preferred_element_type=jnp.float32)
    shared_lift = jnp.dot(normed, shared_gate_up[1], preferred_element_type=jnp.float32)
    shared_hidden = (jax.nn.silu(shared_gate) * shared_lift).astype(jnp.bfloat16)
    shared_part = jnp.dot(shared_hidden, shared_down, preferred_element_type=jnp.float32)
    route_width = expert_ids.shape[1]
    local_experts = expert_gate_up.shape[0]
    expert_total = local_experts * ep_count
    capacity = (2 * token_count * route_width + expert_total - 1) // expert_total
    pair_experts = expert_ids.reshape(-1)
    marks = (pair_experts[:, None] == jnp.arange(expert_total, dtype=jnp.int32)[None, :]).astype(
        jnp.int32
    )
    slot_of = jnp.sum(jnp.cumsum(marks, axis=0) * marks, axis=1) - 1
    placement = (pair_experts * capacity + slot_of).reshape(token_count, route_width)
    slot_count = expert_total * capacity
    slot_index = jnp.arange(slot_count, dtype=jnp.int32)
    hits = placement[None, :, :] == slot_index[:, None, None]
    dispatch = jnp.any(hits, axis=2).astype(jnp.bfloat16)
    outgoing = jnp.dot(dispatch, normed, preferred_element_type=jnp.float32).astype(jnp.bfloat16)
    outgoing = outgoing.reshape(ep_count, local_experts, capacity, -1)
    gate_weight = expert_gate_up[:, 0]
    lift_weight = expert_gate_up[:, 1]
    incoming = lax.all_to_all(outgoing, "ep", split_axis=0, concat_axis=0, tiled=True)
    gate_value = jnp.einsum(
        "pecd,edf->pecf", incoming, gate_weight, preferred_element_type=jnp.float32
    )
    lift_value = jnp.einsum(
        "pecd,edf->pecf", incoming, lift_weight, preferred_element_type=jnp.float32
    )
    hidden_rows = (jax.nn.silu(gate_value) * lift_value).astype(jnp.bfloat16)
    feature_share = expert_down.shape[-1] // req_count
    sending = jnp.stack(
        [
            jnp.stack(
                [
                    jnp.dot(
                        hidden_rows[:, expert],
                        expert_down[expert, :, share * feature_share : (share + 1) * feature_share],
                        preferred_element_type=jnp.float32,
                    ).astype(jnp.bfloat16)
                    for expert in range(local_experts)
                ],
                axis=1,
            )
            for share in range(req_count)
        ],
        axis=0,
    ).reshape(req_count * ep_count, local_experts, capacity, feature_share)
    returned = lax.all_to_all(sending, ("req", "ep"), 0, 0, tiled=True).reshape(
        req_count * slot_count, feature_share
    )
    combine = jnp.sum(
        jnp.where(
            placement[:, :, None] == slot_index[None, None, :], gates[:, :, None], 0.0
        ),
        axis=1,
    )
    combine = jnp.tile(combine, (1, req_count))
    routed = jnp.dot(combine.astype(jnp.bfloat16), returned, preferred_element_type=jnp.float32)
    shared_cols = lax.psum_scatter(
        shared_part.astype(jnp.bfloat16), "req", scatter_dimension=1, tiled=True
    )
    layer_out = (
        resid_cols.astype(jnp.float32) + shared_cols.astype(jnp.float32) + routed
    ).astype(jnp.bfloat16)
    starts = cache_len // page_size
    page_now = starts + jnp.mod(req_index - starts, req_count)
    slot_now = jnp.take_along_axis(page_table, page_now[:, None], axis=1)[:, 0]
    old_page = cache_pool[slot_now]
    offsets = (
        page_now[:, None] * page_size
        + jnp.arange(page_size, dtype=jnp.int32)[None, :]
        - cache_len[:, None]
    ).astype(jnp.float32)
    accepted = jnp.take_along_axis(ancestry, accept_leaf[:, None, None], axis=1)[:, 0, :]
    select = accepted[:, None, :] * (depths[:, None, :] == offsets[:, :, None]).astype(jnp.float32)
    written = jnp.einsum(
        "rod,rdk->rok", select.astype(jnp.bfloat16), own_latent, preferred_element_type=jnp.float32
    )
    touched = jnp.sum(select, axis=2) > 0.5
    fresh = jnp.where(touched[..., None], written, old_page.astype(jnp.float32)).astype(
        jnp.bfloat16
    )
    return (layer_out, fresh[:, None])


def solution(mesh):
    in_specs = (
        P("ep", None, None),
        P("ep", None),
        P("ep", "req"),
        P(("req", "ep"), None, None),
        P("ep", None),
        P("ep"),
        P("ep", None),
        P("ep"),
        P(),
        P(),
        P(None, "req"),
        P(),
        P(),
        P("ep", None),
        P("ep", None, None, "req"),
        P("ep", "req", None),
        P(None, None, "req"),
        P("req", None),
    )
    out_specs = (P("ep", "req"), P("ep", "req", None, None))
    return jax.shard_map(
        per_device, mesh=mesh, in_specs=in_specs, out_specs=out_specs, check_vma=False
    )
```

```python
import functools
import math

import jax
import jax.numpy as jnp
from jax import lax
from jax.experimental import pallas as pl
from jax.experimental.pallas import tpu as pltpu
from jax.sharding import PartitionSpec as P

NEGATIVE = -1e30


def ancestors(parents):
    draft_count = parents.shape[-1]
    draft_index = jnp.arange(draft_count, dtype=jnp.int32)
    ancestry = (parents[:, :, None] == draft_index[None, None, :]).astype(jnp.float32)
    ancestry = ancestry + jnp.eye(draft_count, dtype=jnp.float32)[None]
    for doubling in range(max(1, (draft_count - 1).bit_length())):
        ancestry = jnp.minimum(
            jnp.einsum("rij,rjk->rik", ancestry, ancestry, precision=lax.Precision.HIGHEST), 1.0
        )
    return ancestry


def split_exact(values):
    pieces = []
    rest = values
    for _ in range(3):
        piece = lax.reduce_precision(rest, exponent_bits=8, mantissa_bits=7)
        pieces.append(piece.astype(jnp.bfloat16))
        rest = rest - piece
    return pieces


def attention_kernel(
    slots_ref, limits_ref, q_ref, rope_ref, page_ref, draft_ref, tree_ref, mixed_ref, stats_ref,
    keys,
    *, page_size, latent_width, score_scale, row_block
):
    request = pl.program_id(0)
    page = pl.program_id(1)
    page_total = pl.num_programs(1)
    keys[page] = page_ref[0]

    @pl.when(page == page_total - 1)
    def _():
        local_pages = keys.shape[0]
        key_rows = local_pages * page_size
        column = lax.broadcasted_iota(jnp.int32, (1, key_rows), 1)
        limit = jnp.zeros((1, key_rows), jnp.int32)
        for index in range(local_pages):
            limit = jnp.where(column // page_size == index, limits_ref[request, index], limit)
        cache_ok = (column % page_size) < limit
        lane = lax.broadcasted_iota(jnp.int32, (row_block, stats_ref.shape[2]), 1)

        def body(block, carry):
            rows = pl.ds(pl.multiple_of(block * row_block, row_block), row_block)
            query = q_ref[0, rows, :]
            rope = rope_ref[0, rows, :]
            contract = (((1,), (1,)), ((), ()))
            score = jnp.concatenate(
                [
                    jnp.dot(query, keys[index, :latent_width, :], preferred_element_type=jnp.float32)
                    + jnp.dot(rope, keys[index, latent_width:, :], preferred_element_type=jnp.float32)
                    for index in range(local_pages)
                ],
                axis=1,
            ) * score_scale
            score = jnp.where(cache_ok, score, NEGATIVE)
            draft_score = (
                lax.dot_general(
                    query, draft_ref[0, :, :latent_width], contract,
                    preferred_element_type=jnp.float32,
                )
                + lax.dot_general(
                    rope, draft_ref[0, :, latent_width:], contract,
                    preferred_element_type=jnp.float32,
                )
            ) * score_scale
            tree_ok = tree_ref[0, rows, :] > 0.5
            draft_score = jnp.where(tree_ok, draft_score, NEGATIVE)
            top = jnp.maximum(
                jnp.max(score, axis=1, keepdims=True), jnp.max(draft_score, axis=1, keepdims=True)
            )
            weight = jnp.exp(score - top)
            draft_weight = jnp.exp(draft_score - top)
            total = jnp.sum(weight, axis=1, keepdims=True) + jnp.sum(
                draft_weight, axis=1, keepdims=True
            )
            weight_low = weight.astype(jnp.bfloat16)
            mixed = jnp.dot(
                draft_weight.astype(jnp.bfloat16),
                draft_ref[0, :, :latent_width],
                preferred_element_type=jnp.float32,
            )
            for index in range(local_pages):
                mixed = mixed + lax.dot_general(
                    weight_low[:, index * page_size : (index + 1) * page_size],
                    keys[index, :latent_width, :],
                    contract,
                    preferred_element_type=jnp.float32,
                )
            mixed_ref[0, rows, :] = mixed
            stats_ref[0, rows, :] = jnp.where(lane == 0, top, jnp.where(lane == 1, total, 0.0))
            return carry

        lax.fori_loop(0, q_ref.shape[1] // row_block, body, 0)


def paged_attention(slots, limits, query_rows, rope_rows, cache_pool, draft_rows, tree_rows, score_scale):
    request_count, row_count, latent_width = query_rows.shape
    key_width = cache_pool.shape[1]
    rope_width = rope_rows.shape[2]
    local_pages = slots.shape[1]
    page_size = cache_pool.shape[2]
    draft_pad = draft_rows.shape[1]
    row_block = 256
    kernel = functools.partial(
        attention_kernel,
        page_size=page_size,
        latent_width=latent_width,
        score_scale=score_scale,
        row_block=row_block,
    )
    key_rows = local_pages * page_size
    flops = 2 * request_count * row_count * (key_rows + draft_pad) * (key_width + latent_width)
    cost = pl.CostEstimate(
        flops=flops,
        transcendentals=request_count * row_count * (key_rows + draft_pad),
        bytes_accessed=2 * request_count * (row_count + key_rows) * key_width
        + 4 * request_count * row_count * (latent_width + 128 + draft_pad),
    )
    grid_spec = pltpu.PrefetchScalarGridSpec(
        num_scalar_prefetch=2,
        grid=(request_count, local_pages),
        in_specs=[
            pl.BlockSpec((1, row_count, latent_width), lambda r, j, s, n: (r, 0, 0)),
            pl.BlockSpec((1, row_count, rope_width), lambda r, j, s, n: (r, 0, 0)),
            pl.BlockSpec((1, key_width, page_size), lambda r, j, s, n: (s[r, j], 0, 0)),
            pl.BlockSpec((1, draft_pad, key_width), lambda r, j, s, n: (r, 0, 0)),
            pl.BlockSpec((1, row_count, draft_pad), lambda r, j, s, n: (r, 0, 0)),
        ],
        out_specs=[
            pl.BlockSpec((1, row_count, latent_width), lambda r, j, s, n: (r, 0, 0)),
            pl.BlockSpec((1, row_count, 128), lambda r, j, s, n: (r, 0, 0)),
        ],
        scratch_shapes=[pltpu.VMEM((local_pages, key_width, page_size), jnp.bfloat16)],
    )
    return pl.pallas_call(
        kernel,
        grid_spec=grid_spec,
        out_shape=[
            jax.ShapeDtypeStruct((request_count, row_count, latent_width), jnp.float32),
            jax.ShapeDtypeStruct((request_count, row_count, 128), jnp.float32),
        ],
        compiler_params=pltpu.CompilerParams(
            dimension_semantics=("arbitrary", "arbitrary"), vmem_limit_bytes=48 * 1024 * 1024
        ),
        cost_estimate=cost,
    )(slots, limits, query_rows, rope_rows, cache_pool, draft_rows, tree_rows)


def per_device(
    queries,
    draft_latent,
    hidden_in,
    cache_pool,
    page_table,
    cache_len,
    parents,
    accept_leaf,
    absorb_key,
    absorb_value,
    out_proj,
    norm_gain,
    router,
    expert_ids,
    expert_gate_up,
    expert_down,
    shared_gate_up,
    shared_down,
):
    highest = lax.Precision.HIGHEST
    req_count = lax.axis_size("req")
    req_index = lax.axis_index("req")
    ep_count = lax.axis_size("ep")
    request_count, draft_count = parents.shape
    token_count = request_count * draft_count
    head_count = queries.shape[1]
    nope_width = absorb_key.shape[1]
    latent_width = absorb_key.shape[2]
    page_size = cache_pool.shape[1]
    key_width = cache_pool.shape[2]
    page_count = page_table.shape[1]
    score_scale = 1.0 / math.sqrt(queries.shape[2])
    ancestry = ancestors(parents)
    depths = jnp.sum(ancestry, axis=2) - 1.0
    local_pages = page_count // req_count
    page_cols = req_index + req_count * jnp.arange(local_pages, dtype=jnp.int32)
    slot_rows = jnp.take(page_table, page_cols, axis=1)
    pool_slots = cache_pool.shape[0]
    slot_rows = jnp.clip(slot_rows, 0, pool_slots - 1).astype(jnp.int32)
    limits = jnp.clip(
        cache_len[:, None] - page_cols[None, :] * page_size, 0, page_size
    ).astype(jnp.int32)
    draft_share = draft_count // req_count
    draft_cols = req_index * draft_share + jnp.arange(draft_share, dtype=jnp.int32)
    own_latent = draft_latent.reshape(request_count, draft_count, key_width)
    draft_keys = jnp.take(own_latent, draft_cols, axis=1)
    draft_pad = 128
    draft_rows = jnp.pad(draft_keys, ((0, 0), (0, draft_pad - draft_share), (0, 0)))
    tree_ok = (jnp.take(ancestry, draft_cols, axis=2) > 0.5).astype(jnp.float32)
    tree_rows = jnp.broadcast_to(
        tree_ok[:, :, None, :], (request_count, draft_count, head_count, draft_share)
    ).reshape(request_count, draft_count * head_count, draft_share)
    tree_rows = jnp.pad(tree_rows, ((0, 0), (0, 0), (0, draft_pad - draft_share)))
    absorbed = jnp.einsum(
        "thd,hdl->thl", queries[:, :, :nope_width], absorb_key, preferred_element_type=jnp.float32
    ).astype(jnp.bfloat16)
    query_rows = absorbed.reshape(request_count, draft_count * head_count, latent_width)
    rope_rows = queries[:, :, nope_width:].reshape(request_count, draft_count * head_count, -1)
    mixed_rows, stats = paged_attention(
        slot_rows, limits, query_rows, rope_rows, jnp.swapaxes(cache_pool, 1, 2), draft_rows,
        tree_rows, score_scale,
    )
    mixed_latent = mixed_rows.reshape(request_count, draft_count, head_count, latent_width)
    highest_score = stats[:, :, 0].reshape(request_count, draft_count, head_count)
    totals = stats[:, :, 1].reshape(request_count, draft_count, head_count)
    partial_head = jnp.einsum(
        "rthl,hlv->rthv",
        mixed_latent.astype(jnp.bfloat16),
        absorb_value,
        preferred_element_type=jnp.float32,
    )
    head_width = head_count * partial_head.shape[-1]
    low_parts = split_exact(jnp.concatenate([highest_score, totals], axis=-1))
    packed = jnp.concatenate(
        [partial_head.reshape(token_count, head_width).astype(jnp.bfloat16)]
        + [part.reshape(token_count, 2 * head_count) for part in low_parts],
        axis=1,
    )
    gathered = lax.all_gather(packed, "req").astype(jnp.float32)
    part_heads = gathered[:, :, :head_width]
    rejoined = sum(
        gathered[:, :, head_width + 2 * head_count * k : head_width + 2 * head_count * (k + 1)]
        for k in range(3)
    )
    part_max = rejoined[:, :, :head_count]
    part_sum = rejoined[:, :, head_count:]
    top = jnp.max(part_max, axis=0)
    factor = jnp.exp(part_max - top[None])
    merged_sum = jnp.sum(factor * part_sum, axis=0)
    value_width = head_width // head_count
    spread = (
        jnp.arange(head_width, dtype=jnp.int32)[None, :] // value_width
        == jnp.arange(head_count, dtype=jnp.int32)[:, None]
    ).astype(jnp.bfloat16)
    scale_rows = (factor / merged_sum[None]).reshape(req_count * token_count, head_count)
    factor_wide = jnp.dot(
        scale_rows.astype(jnp.bfloat16), spread, preferred_element_type=jnp.float32
    ).reshape(req_count, token_count, head_width)
    head_rows = jnp.sum(factor_wide * part_heads, axis=0).astype(jnp.bfloat16)
    attention = jnp.dot(head_rows, out_proj, preferred_element_type=jnp.float32)
    resid_cols = (hidden_in.astype(jnp.float32) + attention).astype(jnp.bfloat16)
    resid = lax.all_gather(resid_cols, "req", axis=1, tiled=True)
    resid_wide = resid.astype(jnp.float32)
    normed = resid_wide * lax.rsqrt(
        jnp.mean(resid_wide * resid_wide, axis=1, keepdims=True) + 1e-06
    )
    normed = (normed * norm_gain[None, :]).astype(jnp.bfloat16)
    logits = jnp.dot(normed, router, preferred_element_type=jnp.float32)
    lifted = jax.nn.sigmoid(jnp.take_along_axis(logits, expert_ids, axis=1))
    gates = lifted / jnp.sum(lifted, axis=1, keepdims=True)
    shared_gate = jnp.dot(normed, shared_gate_up[0], preferred_element_type=jnp.float32)
    shared_lift = jnp.dot(normed, shared_gate_up[1], preferred_element_type=jnp.float32)
    shared_hidden = (jax.nn.silu(shared_gate) * shared_lift).astype(jnp.bfloat16)
    shared_part = jnp.dot(shared_hidden, shared_down, preferred_element_type=jnp.float32)
    route_width = expert_ids.shape[1]
    local_experts = expert_gate_up.shape[0]
    expert_total = local_experts * ep_count
    capacity = (2 * token_count * route_width + expert_total - 1) // expert_total
    pair_experts = expert_ids.reshape(-1)
    marks = (pair_experts[:, None] == jnp.arange(expert_total, dtype=jnp.int32)[None, :]).astype(
        jnp.int32
    )
    slot_of = jnp.sum(jnp.cumsum(marks, axis=0) * marks, axis=1) - 1
    placement = (pair_experts * capacity + slot_of).reshape(token_count, route_width)
    slot_count = expert_total * capacity
    slot_index = jnp.arange(slot_count, dtype=jnp.int32)
    hits = placement[None, :, :] == slot_index[:, None, None]
    dispatch = jnp.any(hits, axis=2).astype(jnp.bfloat16)
    outgoing = jnp.dot(dispatch, normed, preferred_element_type=jnp.float32).astype(jnp.bfloat16)
    outgoing = outgoing.reshape(ep_count, local_experts, capacity, -1)
    gate_weight = expert_gate_up[:, 0]
    lift_weight = expert_gate_up[:, 1]
    incoming = lax.all_to_all(outgoing, "ep", split_axis=0, concat_axis=0, tiled=True)
    gate_value = jnp.einsum(
        "pecd,edf->pecf", incoming, gate_weight, preferred_element_type=jnp.float32
    )
    lift_value = jnp.einsum(
        "pecd,edf->pecf", incoming, lift_weight, preferred_element_type=jnp.float32
    )
    hidden_rows = (jax.nn.silu(gate_value) * lift_value).astype(jnp.bfloat16)
    feature_share = expert_down.shape[-1] // req_count
    sending = jnp.stack(
        [
            jnp.stack(
                [
                    jnp.dot(
                        hidden_rows[:, expert],
                        expert_down[expert, :, share * feature_share : (share + 1) * feature_share],
                        preferred_element_type=jnp.float32,
                    ).astype(jnp.bfloat16)
                    for expert in range(local_experts)
                ],
                axis=1,
            )
            for share in range(req_count)
        ],
        axis=0,
    ).reshape(req_count * ep_count, local_experts, capacity, feature_share)
    returned = lax.all_to_all(sending, ("req", "ep"), 0, 0, tiled=True).reshape(
        req_count * slot_count, feature_share
    )
    combine = jnp.sum(
        jnp.where(
            placement[:, :, None] == slot_index[None, None, :], gates[:, :, None], 0.0
        ),
        axis=1,
    )
    combine = jnp.tile(combine, (1, req_count))
    combine_high = combine.astype(jnp.bfloat16)
    combine_low = (combine - combine_high.astype(jnp.float32)).astype(jnp.bfloat16)
    both = jnp.dot(
        jnp.concatenate([combine_high, combine_low], axis=0),
        returned,
        preferred_element_type=jnp.float32,
    )
    routed = both[:token_count] + both[token_count:]
    shared_cols = lax.psum_scatter(
        shared_part.astype(jnp.bfloat16), "req", scatter_dimension=1, tiled=True
    )
    layer_out = (
        resid_cols.astype(jnp.float32) + shared_cols.astype(jnp.float32) + routed
    ).astype(jnp.bfloat16)
    starts = cache_len // page_size
    page_now = starts + jnp.mod(req_index - starts, req_count)
    slot_now = jnp.take_along_axis(page_table, page_now[:, None], axis=1)[:, 0]
    old_page = cache_pool[slot_now]
    offsets = (
        page_now[:, None] * page_size
        + jnp.arange(page_size, dtype=jnp.int32)[None, :]
        - cache_len[:, None]
    ).astype(jnp.float32)
    accepted = jnp.take_along_axis(ancestry, accept_leaf[:, None, None], axis=1)[:, 0, :]
    select = accepted[:, None, :] * (depths[:, None, :] == offsets[:, :, None]).astype(jnp.float32)
    written = jnp.einsum(
        "rod,rdk->rok", select.astype(jnp.bfloat16), own_latent, preferred_element_type=jnp.float32
    )
    touched = jnp.sum(select, axis=2) > 0.5
    fresh = jnp.where(touched[..., None], written, old_page.astype(jnp.float32)).astype(
        jnp.bfloat16
    )
    return (layer_out, fresh[:, None])


def solution(mesh):
    in_specs = (
        P("ep", None, None),
        P("ep", None),
        P("ep", "req"),
        P(("req", "ep"), None, None),
        P("ep", None),
        P("ep"),
        P("ep", None),
        P("ep"),
        P(),
        P(),
        P(None, "req"),
        P(),
        P(),
        P("ep", None),
        P("ep", None, None, "req"),
        P("ep", "req", None),
        P(None, None, "req"),
        P("req", None),
    )
    out_specs = (P("ep", "req"), P("ep", "req", None, None))
    return jax.shard_map(
        per_device, mesh=mesh, in_specs=in_specs, out_specs=out_specs, check_vma=False
    )
```

```python
import functools
import math

import jax
import jax.numpy as jnp
from jax import lax
from jax.experimental import pallas as pl
from jax.experimental.pallas import tpu as pltpu
from jax.sharding import PartitionSpec as P

NEGATIVE = -1e30


def ancestors(parents):
    draft_count = parents.shape[-1]
    draft_index = jnp.arange(draft_count, dtype=jnp.int32)
    ancestry = (parents[:, :, None] == draft_index[None, None, :]).astype(jnp.float32)
    ancestry = ancestry + jnp.eye(draft_count, dtype=jnp.float32)[None]
    for doubling in range(max(1, (draft_count - 1).bit_length())):
        ancestry = jnp.minimum(
            jnp.einsum("rij,rjk->rik", ancestry, ancestry, precision=lax.Precision.HIGHEST), 1.0
        )
    return ancestry


def split_exact(values):
    pieces = []
    rest = values
    for _ in range(3):
        piece = lax.reduce_precision(rest, exponent_bits=8, mantissa_bits=7)
        pieces.append(piece.astype(jnp.bfloat16))
        rest = rest - piece
    return pieces


def attention_kernel(
    slots_ref, limits_ref, q_ref, rope_ref, page_ref, draft_ref, tree_ref, mixed_ref, stats_ref,
    keys,
    *, page_size, latent_width, score_scale, row_block
):
    request = pl.program_id(0)
    page = pl.program_id(1)
    page_total = pl.num_programs(1)
    keys[page] = page_ref[0]

    @pl.when(page == page_total - 1)
    def _():
        local_pages = keys.shape[0]
        key_rows = local_pages * page_size
        column = lax.broadcasted_iota(jnp.int32, (1, key_rows), 1)
        limit = jnp.zeros((1, key_rows), jnp.int32)
        for index in range(local_pages):
            limit = jnp.where(column // page_size == index, limits_ref[request, index], limit)
        cache_ok = (column % page_size) < limit
        lane = lax.broadcasted_iota(jnp.int32, (row_block, stats_ref.shape[2]), 1)

        def body(block, carry):
            rows = pl.ds(pl.multiple_of(block * row_block, row_block), row_block)
            query = q_ref[0, rows, :]
            rope = rope_ref[0, rows, :]
            contract = (((1,), (1,)), ((), ()))
            score = jnp.concatenate(
                [
                    jnp.dot(query, keys[index, :latent_width, :], preferred_element_type=jnp.float32)
                    + jnp.dot(rope, keys[index, latent_width:, :], preferred_element_type=jnp.float32)
                    for index in range(local_pages)
                ],
                axis=1,
            ) * score_scale
            score = jnp.where(cache_ok, score, NEGATIVE)
            draft_score = (
                lax.dot_general(
                    query, draft_ref[0, :, :latent_width], contract,
                    preferred_element_type=jnp.float32,
                )
                + lax.dot_general(
                    rope, draft_ref[0, :, latent_width:], contract,
                    preferred_element_type=jnp.float32,
                )
            ) * score_scale
            tree_ok = tree_ref[0, rows, :] > 0.5
            draft_score = jnp.where(tree_ok, draft_score, NEGATIVE)
            top = jnp.maximum(
                jnp.max(score, axis=1, keepdims=True), jnp.max(draft_score, axis=1, keepdims=True)
            )
            weight = jnp.exp(score - top)
            draft_weight = jnp.exp(draft_score - top)
            total = jnp.sum(weight, axis=1, keepdims=True) + jnp.sum(
                draft_weight, axis=1, keepdims=True
            )
            weight_low = weight.astype(jnp.bfloat16)
            mixed = jnp.dot(
                draft_weight.astype(jnp.bfloat16),
                draft_ref[0, :, :latent_width],
                preferred_element_type=jnp.float32,
            )
            for index in range(local_pages):
                mixed = mixed + lax.dot_general(
                    weight_low[:, index * page_size : (index + 1) * page_size],
                    keys[index, :latent_width, :],
                    contract,
                    preferred_element_type=jnp.float32,
                )
            mixed_ref[0, rows, :] = mixed
            stats_ref[0, rows, :] = jnp.where(lane == 0, top, jnp.where(lane == 1, total, 0.0))
            return carry

        lax.fori_loop(0, q_ref.shape[1] // row_block, body, 0)


def paged_attention(slots, limits, query_rows, rope_rows, cache_pool, draft_rows, tree_rows, score_scale):
    request_count, row_count, latent_width = query_rows.shape
    key_width = cache_pool.shape[1]
    rope_width = rope_rows.shape[2]
    local_pages = slots.shape[1]
    page_size = cache_pool.shape[2]
    draft_pad = draft_rows.shape[1]
    row_block = 512
    kernel = functools.partial(
        attention_kernel,
        page_size=page_size,
        latent_width=latent_width,
        score_scale=score_scale,
        row_block=row_block,
    )
    key_rows = local_pages * page_size
    flops = 2 * request_count * row_count * (key_rows + draft_pad) * (key_width + latent_width)
    cost = pl.CostEstimate(
        flops=flops,
        transcendentals=request_count * row_count * (key_rows + draft_pad),
        bytes_accessed=2 * request_count * (row_count + key_rows) * key_width
        + 4 * request_count * row_count * (latent_width + 128 + draft_pad),
    )
    grid_spec = pltpu.PrefetchScalarGridSpec(
        num_scalar_prefetch=2,
        grid=(request_count, local_pages),
        in_specs=[
            pl.BlockSpec((1, row_count, latent_width), lambda r, j, s, n: (r, 0, 0)),
            pl.BlockSpec((1, row_count, rope_width), lambda r, j, s, n: (r, 0, 0)),
            pl.BlockSpec((1, key_width, page_size), lambda r, j, s, n: (s[r, j], 0, 0)),
            pl.BlockSpec((1, draft_pad, key_width), lambda r, j, s, n: (r, 0, 0)),
            pl.BlockSpec((1, row_count, draft_pad), lambda r, j, s, n: (r, 0, 0)),
        ],
        out_specs=[
            pl.BlockSpec((1, row_count, latent_width), lambda r, j, s, n: (r, 0, 0)),
            pl.BlockSpec((1, row_count, 128), lambda r, j, s, n: (r, 0, 0)),
        ],
        scratch_shapes=[pltpu.VMEM((local_pages, key_width, page_size), jnp.bfloat16)],
    )
    return pl.pallas_call(
        kernel,
        grid_spec=grid_spec,
        out_shape=[
            jax.ShapeDtypeStruct((request_count, row_count, latent_width), jnp.float32),
            jax.ShapeDtypeStruct((request_count, row_count, 128), jnp.float32),
        ],
        compiler_params=pltpu.CompilerParams(
            dimension_semantics=("arbitrary", "arbitrary"), vmem_limit_bytes=48 * 1024 * 1024
        ),
        cost_estimate=cost,
    )(slots, limits, query_rows, rope_rows, cache_pool, draft_rows, tree_rows)


def per_device(
    queries,
    draft_latent,
    hidden_in,
    cache_pool,
    page_table,
    cache_len,
    parents,
    accept_leaf,
    absorb_key,
    absorb_value,
    out_proj,
    norm_gain,
    router,
    expert_ids,
    expert_gate_up,
    expert_down,
    shared_gate_up,
    shared_down,
):
    highest = lax.Precision.HIGHEST
    req_count = lax.axis_size("req")
    req_index = lax.axis_index("req")
    ep_count = lax.axis_size("ep")
    request_count, draft_count = parents.shape
    token_count = request_count * draft_count
    head_count = queries.shape[1]
    nope_width = absorb_key.shape[1]
    latent_width = absorb_key.shape[2]
    page_size = cache_pool.shape[1]
    key_width = cache_pool.shape[2]
    page_count = page_table.shape[1]
    score_scale = 1.0 / math.sqrt(queries.shape[2])
    ancestry = ancestors(parents)
    depths = jnp.sum(ancestry, axis=2) - 1.0
    local_pages = page_count // req_count
    page_cols = req_index + req_count * jnp.arange(local_pages, dtype=jnp.int32)
    slot_rows = jnp.take(page_table, page_cols, axis=1)
    pool_slots = cache_pool.shape[0]
    slot_rows = jnp.clip(slot_rows, 0, pool_slots - 1).astype(jnp.int32)
    limits = jnp.clip(
        cache_len[:, None] - page_cols[None, :] * page_size, 0, page_size
    ).astype(jnp.int32)
    draft_share = draft_count // req_count
    draft_cols = req_index * draft_share + jnp.arange(draft_share, dtype=jnp.int32)
    own_latent = draft_latent.reshape(request_count, draft_count, key_width)
    draft_keys = jnp.take(own_latent, draft_cols, axis=1)
    draft_pad = 128
    draft_rows = jnp.pad(draft_keys, ((0, 0), (0, draft_pad - draft_share), (0, 0)))
    tree_ok = (jnp.take(ancestry, draft_cols, axis=2) > 0.5).astype(jnp.float32)
    tree_rows = jnp.broadcast_to(
        tree_ok[:, :, None, :], (request_count, draft_count, head_count, draft_share)
    ).reshape(request_count, draft_count * head_count, draft_share)
    tree_rows = jnp.pad(tree_rows, ((0, 0), (0, 0), (0, draft_pad - draft_share)))
    absorbed = jnp.einsum(
        "thd,hdl->thl", queries[:, :, :nope_width], absorb_key, preferred_element_type=jnp.float32
    ).astype(jnp.bfloat16)
    query_rows = absorbed.reshape(request_count, draft_count * head_count, latent_width)
    rope_rows = queries[:, :, nope_width:].reshape(request_count, draft_count * head_count, -1)
    mixed_rows, stats = paged_attention(
        slot_rows, limits, query_rows, rope_rows, jnp.swapaxes(cache_pool, 1, 2), draft_rows,
        tree_rows, score_scale,
    )
    mixed_latent = mixed_rows.reshape(request_count, draft_count, head_count, latent_width)
    highest_score = stats[:, :, 0].reshape(request_count, draft_count, head_count)
    totals = stats[:, :, 1].reshape(request_count, draft_count, head_count)
    partial_head = jnp.einsum(
        "rthl,hlv->rthv",
        mixed_latent.astype(jnp.bfloat16),
        absorb_value,
        preferred_element_type=jnp.float32,
    )
    head_width = head_count * partial_head.shape[-1]
    low_parts = split_exact(jnp.concatenate([highest_score, totals], axis=-1))
    packed = jnp.concatenate(
        [partial_head.reshape(token_count, head_width).astype(jnp.bfloat16)]
        + [part.reshape(token_count, 2 * head_count) for part in low_parts],
        axis=1,
    )
    gathered = lax.all_gather(packed, "req").astype(jnp.float32)
    part_heads = gathered[:, :, :head_width]
    rejoined = sum(
        gathered[:, :, head_width + 2 * head_count * k : head_width + 2 * head_count * (k + 1)]
        for k in range(3)
    )
    part_max = rejoined[:, :, :head_count]
    part_sum = rejoined[:, :, head_count:]
    top = jnp.max(part_max, axis=0)
    factor = jnp.exp(part_max - top[None])
    merged_sum = jnp.sum(factor * part_sum, axis=0)
    value_width = head_width // head_count
    spread = (
        jnp.arange(head_width, dtype=jnp.int32)[None, :] // value_width
        == jnp.arange(head_count, dtype=jnp.int32)[:, None]
    ).astype(jnp.bfloat16)
    scale_rows = (factor / merged_sum[None]).reshape(req_count * token_count, head_count)
    factor_wide = jnp.dot(
        scale_rows.astype(jnp.bfloat16), spread, preferred_element_type=jnp.float32
    ).reshape(req_count, token_count, head_width)
    head_rows = jnp.sum(factor_wide * part_heads, axis=0).astype(jnp.bfloat16)
    attention = jnp.dot(head_rows, out_proj, preferred_element_type=jnp.float32)
    resid_cols = (hidden_in.astype(jnp.float32) + attention).astype(jnp.bfloat16)
    resid = lax.all_gather(resid_cols, "req", axis=1, tiled=True)
    resid_wide = resid.astype(jnp.float32)
    normed = resid_wide * lax.rsqrt(
        jnp.mean(resid_wide * resid_wide, axis=1, keepdims=True) + 1e-06
    )
    normed = (normed * norm_gain[None, :]).astype(jnp.bfloat16)
    logits = jnp.dot(normed, router, preferred_element_type=jnp.float32)
    lifted = jax.nn.sigmoid(jnp.take_along_axis(logits, expert_ids, axis=1))
    gates = lifted / jnp.sum(lifted, axis=1, keepdims=True)
    shared_gate = jnp.dot(normed, shared_gate_up[0], preferred_element_type=jnp.float32)
    shared_lift = jnp.dot(normed, shared_gate_up[1], preferred_element_type=jnp.float32)
    shared_hidden = (jax.nn.silu(shared_gate) * shared_lift).astype(jnp.bfloat16)
    shared_part = jnp.dot(shared_hidden, shared_down, preferred_element_type=jnp.float32)
    route_width = expert_ids.shape[1]
    local_experts = expert_gate_up.shape[0]
    expert_total = local_experts * ep_count
    capacity = (2 * token_count * route_width + expert_total - 1) // expert_total
    pair_experts = expert_ids.reshape(-1)
    marks = (pair_experts[:, None] == jnp.arange(expert_total, dtype=jnp.int32)[None, :]).astype(
        jnp.int32
    )
    slot_of = jnp.sum(jnp.cumsum(marks, axis=0) * marks, axis=1) - 1
    placement = (pair_experts * capacity + slot_of).reshape(token_count, route_width)
    slot_count = expert_total * capacity
    slot_index = jnp.arange(slot_count, dtype=jnp.int32)
    hits = placement[None, :, :] == slot_index[:, None, None]
    dispatch = jnp.any(hits, axis=2).astype(jnp.bfloat16)
    outgoing = jnp.dot(dispatch, normed, preferred_element_type=jnp.float32).astype(jnp.bfloat16)
    outgoing = outgoing.reshape(ep_count, local_experts, capacity, -1)
    gate_weight = expert_gate_up[:, 0]
    lift_weight = expert_gate_up[:, 1]
    incoming = lax.all_to_all(outgoing, "ep", split_axis=0, concat_axis=0, tiled=True)
    gate_value = jnp.einsum(
        "pecd,edf->pecf", incoming, gate_weight, preferred_element_type=jnp.float32
    )
    lift_value = jnp.einsum(
        "pecd,edf->pecf", incoming, lift_weight, preferred_element_type=jnp.float32
    )
    hidden_rows = (jax.nn.silu(gate_value) * lift_value).astype(jnp.bfloat16)
    feature_share = expert_down.shape[-1] // req_count
    sending = jnp.stack(
        [
            jnp.stack(
                [
                    jnp.dot(
                        hidden_rows[:, expert],
                        expert_down[expert, :, share * feature_share : (share + 1) * feature_share],
                        preferred_element_type=jnp.float32,
                    ).astype(jnp.bfloat16)
                    for expert in range(local_experts)
                ],
                axis=1,
            )
            for share in range(req_count)
        ],
        axis=0,
    ).reshape(req_count * ep_count, local_experts, capacity, feature_share)
    returned = lax.all_to_all(sending, ("req", "ep"), 0, 0, tiled=True).reshape(
        req_count * slot_count, feature_share
    )
    combine = jnp.sum(
        jnp.where(
            placement[:, :, None] == slot_index[None, None, :], gates[:, :, None], 0.0
        ),
        axis=1,
    )
    combine = jnp.tile(combine, (1, req_count))
    combine_high = combine.astype(jnp.bfloat16)
    combine_low = (combine - combine_high.astype(jnp.float32)).astype(jnp.bfloat16)
    both = jnp.dot(
        jnp.concatenate([combine_high, combine_low], axis=0),
        returned,
        preferred_element_type=jnp.float32,
    )
    routed = both[:token_count] + both[token_count:]
    shared_cols = lax.psum_scatter(
        shared_part.astype(jnp.bfloat16), "req", scatter_dimension=1, tiled=True
    )
    layer_out = (
        resid_cols.astype(jnp.float32) + shared_cols.astype(jnp.float32) + routed
    ).astype(jnp.bfloat16)
    starts = cache_len // page_size
    page_now = starts + jnp.mod(req_index - starts, req_count)
    slot_now = jnp.take_along_axis(page_table, page_now[:, None], axis=1)[:, 0]
    old_page = cache_pool[slot_now]
    offsets = (
        page_now[:, None] * page_size
        + jnp.arange(page_size, dtype=jnp.int32)[None, :]
        - cache_len[:, None]
    ).astype(jnp.float32)
    accepted = jnp.take_along_axis(ancestry, accept_leaf[:, None, None], axis=1)[:, 0, :]
    select = accepted[:, None, :] * (depths[:, None, :] == offsets[:, :, None]).astype(jnp.float32)
    written = jnp.einsum(
        "rod,rdk->rok", select.astype(jnp.bfloat16), own_latent, preferred_element_type=jnp.float32
    )
    touched = jnp.sum(select, axis=2) > 0.5
    fresh = jnp.where(touched[..., None], written, old_page.astype(jnp.float32)).astype(
        jnp.bfloat16
    )
    return (layer_out, fresh[:, None])


def solution(mesh):
    in_specs = (
        P("ep", None, None),
        P("ep", None),
        P("ep", "req"),
        P(("req", "ep"), None, None),
        P("ep", None),
        P("ep"),
        P("ep", None),
        P("ep"),
        P(),
        P(),
        P(None, "req"),
        P(),
        P(),
        P("ep", None),
        P("ep", None, None, "req"),
        P("ep", "req", None),
        P(None, None, "req"),
        P("req", None),
    )
    out_specs = (P("ep", "req"), P("ep", "req", None, None))
    return jax.shard_map(
        per_device, mesh=mesh, in_specs=in_specs, out_specs=out_specs, check_vma=False
    )
```
